32 devices in a mesh: dp: 2 (over y), expert: 16 (over z, x, core).
Axes of the slice: x: 2, y: 2, z: 4, core: 2. Of those that a mesh axis runs over, the one named last changes fastest.
Arguments:
- tokens: bfloat16 [4096, 1024], P(('dp', 'expert')), may hold values from -6 to 6
- masked: int32 [4096], P(('dp', 'expert')), may hold values 0 or 1
- importance: float32 [4096], P(('dp', 'expert')), may hold values from 1 to 10
- routes: int32 [4096, 8], P(('dp', 'expert')), may hold values from 0 to 15, all different within a row; in each aligned block of 128 rows (0 to 127, 128 to 255, ...) at most 96 rows name the same one
- gates: float32 [4096, 8], P(('dp', 'expert')), may hold values from 0.05 to 0.3
- cotangent: bfloat16 [4096, 1024], P(('dp', 'expert')), may hold values from -6 to 6
- w_gate: bfloat16 [16, 512, 1024], P('expert'), may hold values from -0.1875 to 0.1875
- w_up: bfloat16 [16, 512, 1024], P('expert'), may hold values from -0.1875 to 0.1875
- w_down: bfloat16 [16, 512, 1024], P('expert'), may hold values from -0.25 to 0.25
Outputs:
- mixed: bfloat16 [4096, 1024], P(('dp', 'expert'))
- weight_grads: float32 [16, 512, 3, 1024], P('expert', 'dp')
The draws below stay inside these ranges and needn't reach their ends.
Inputs may be any that keep to these rules, and one draw needn't show every extreme that they name: `routes`: among the 128 rows of one device (aligned blocks of rows), no expert is named by more than 96 rows, a bound that some block reaches; a row names 8 different experts.
All inputs are finite; a program needn't handle non-finite values. No bound on the sum of `masked` on one device may be relied on, other than what follows from the above.
Results may differ from the reference program's by a relative error of at most 0.0057.
Values may be sent and summed in bfloat16 or wider, within the bound.
No kernel may reach another device: no remote copies, remote signals or barrier semaphores. Data moves between devices by JAX's collectives and lax.ppermute only.
A program may use at most 64 MiB of HBM per device.

```python
import math
import jax
import jax.numpy as jnp
import numpy as np
from jax import lax

D = 1024
FF = 512
TOPK = 8
TOK_DEV = 128
EXPERTS = 16
TOKENS = 4096
CAP = 96


def set_ends(drawn, stream_key, least, high):
    extent = drawn.shape
    spot = [jax.random.randint(jax.random.fold_in(stream_key, axis), (), 0, extent[axis]) for axis in range(len(extent))]
    drawn = drawn.at[tuple(spot)].set(least)
    longest = extent.index(max(extent))
    spot[longest] = (spot[longest] + 1) % extent[longest]
    return drawn.at[tuple(spot)].set(high)


def block_levels(own_key, dims, split, least, high):
    loudness, own = 1.0, jax.random.fold_in(own_key, 6)
    for position, blocks in split:
        heights = jnp.exp(jax.random.uniform(jax.random.fold_in(own, position), (blocks,), jnp.float32, least / len(split), high / len(split)))
        loudness = loudness * jnp.repeat(heights, dims[position] // blocks).reshape([-1 if axis == position else 1 for axis in range(len(dims))])
    return loudness


def routed_block(rng, own, number, rows, count, top, reach, lean):
    order = jax.random.permutation(rng, count)
    crowded, usual = shares(count, rows * top, reach, lean, True), shares(count, rows * top, reach, lean, False)
    places = jnp.arange(count)

    def named(sizes, turn):
        used = int((sizes > 0).sum())
        fixed = max(1, used // 4)
        passed = fixed + (places - fixed + turn * (used - fixed)) % max(1, count - fixed)
        return jnp.zeros((count,), jnp.int32).at[order[jnp.where(places < fixed, places, passed)]].set(jnp.asarray(sizes, jnp.int32))

    sizes = jnp.where(number % 4 == 0, named(crowded, number // 4), named(usual, number - number // 4 - 1))
    mixed = jax.random.permutation(jax.random.fold_in(own, 3), count)
    donor, receiver = mixed[0:count // 2 * 2:2], mixed[1:count // 2 * 2:2]
    room = jnp.minimum(sizes[donor] - 1, reach - sizes[receiver]) // 2
    room = jnp.where((donor == order[0]) | (receiver == order[0]) | (sizes[receiver] == 0), 0, jnp.maximum(room, 0))
    passed = jax.random.randint(jax.random.fold_in(own, 4), (count // 2,), 0, 1 << 20) % (room + 1)
    sizes = sizes.at[donor].add(-passed).at[receiver].add(passed)
    labels = jnp.searchsorted(jnp.cumsum(sizes), jnp.arange(rows * top), side="right").astype(jnp.int32)
    listing = labels.reshape(top, rows).T
    listing = listing[jax.random.permutation(jax.random.fold_in(own, 1), rows)]
    turn = jax.random.randint(jax.random.fold_in(own, 2), (rows, 1), 0, top)
    return jnp.take_along_axis(listing, (jnp.arange(top)[None, :] + turn) % top, axis=1)


def shares(number_of, total, bound, lean, full):
    loads = [(1 << 20) // math.isqrt(grade ** lean) + 1 for grade in range(1, number_of + 1)]
    largest = bound if full else min(bound, max(-(-total // number_of), total * loads[0] // sum(loads)))
    least = 1 if total - largest >= number_of - 1 else 0
    holding, surplus = [largest] + [least] * (number_of - 1), total - largest - least * (number_of - 1)
    while surplus > 0:
        candidates = [i for i in range(1, number_of) if holding[i] < largest] or [i for i in range(1, number_of) if holding[i] < bound]
        mass, remaining = sum([loads[i] for i in candidates]), surplus
        for i in candidates:
            addition = min(bound - holding[i], max(1, remaining * loads[i] // mass), surplus)
            holding[i] = holding[i] + addition
            surplus = surplus - addition
    return np.array(holding)


def normal_values(own_key, shape, width, most, cuts=(), held_as=jnp.bfloat16):
    gain = block_levels(own_key, shape, cuts, -0.22, 0.18) if cuts else 1.0
    array = jax.random.normal(own_key, shape, jnp.float32) * width * gain
    return jnp.minimum(jnp.maximum(array, -most), most).astype(held_as)


def setup_inputs(seed: int = 0) -> dict:
    arg_keys = jax.random.split(jax.random.key(seed), 10)
    tokens = normal_values(arg_keys[0], (TOKENS, D), 1.0, 6.0, ((0, 32),))
    masked = set_ends((jax.random.randint(arg_keys[1], (TOKENS,), 0, 2) < 1).astype(jnp.int32), jax.random.fold_in(arg_keys[1], 1), 0, 1)
    importance = jnp.clip(jnp.exp(math.log(10.0) - 2.3025851 * jax.random.uniform(arg_keys[2], (TOKENS,), jnp.float32) ** block_levels(arg_keys[2], (TOKENS,), ((0, 32),), -0.2, 0.2)), 1.0, 10.0)
    routes_keys = jax.random.split(jax.random.fold_in(arg_keys[3], 1), TOKENS // TOK_DEV)
    routes_turns = jax.random.permutation(jax.random.fold_in(arg_keys[3], 3), TOKENS // TOK_DEV)
    routes = jax.vmap(lambda own, number: routed_block(jax.random.fold_in(arg_keys[3], 2), own, number, TOK_DEV, EXPERTS, TOPK, CAP, 2))(routes_keys, routes_turns).reshape((TOKENS, TOPK))
    gates = jnp.clip(jnp.exp(math.log(0.3) - 1.7917595 * jax.random.uniform(arg_keys[4], (TOKENS, TOPK), jnp.float32) ** block_levels(arg_keys[4], (TOKENS, TOPK), ((0, 32),), -0.2, 0.2)), 0.05, 0.3)
    cotangent = normal_values(arg_keys[5], (TOKENS, D), 1.0, 6.0, ((0, 32),))
    w_gate = normal_values(arg_keys[6], (EXPERTS, FF, D), D ** -0.5, 0.1875, ((0, 16),))
    w_up = normal_values(arg_keys[7], (EXPERTS, FF, D), D ** -0.5, 0.1875, ((0, 16),))
    w_down = normal_values(arg_keys[8], (EXPERTS, FF, D), FF ** -0.5, 0.25, ((0, 16),))
    return {"tokens": tokens, "masked": masked, "importance": importance, "routes": routes, "gates": gates, "cotangent": cotangent, "w_gate": w_gate, "w_up": w_up, "w_down": w_down}


def block_slots(block_routes):
    onehot = (block_routes[:, None] == jnp.arange(EXPERTS, dtype=jnp.int32)[None, :]).astype(jnp.int32)
    before = jnp.cumsum(onehot, axis=0) - onehot
    return jnp.sum(before * onehot, axis=1).astype(jnp.int32)


def reference(tokens, masked, importance, routes, gates, cotangent, w_gate, w_up, w_down):
    nblocks = TOKENS // TOK_DEV
    span = TOK_DEV * TOPK
    flat = routes.reshape(nblocks, span).astype(jnp.int32)
    slots = lax.map(block_slots, flat)
    findex = jnp.arange(nblocks * span, dtype=jnp.int32).reshape(nblocks, span)
    place = jnp.arange(nblocks, dtype=jnp.int32)[:, None] * CAP + slots
    table = jnp.full((EXPERTS, nblocks * CAP), -1, jnp.int32).at[flat, place].set(findex)
    coef = importance * masked.astype(jnp.float32)
    gate_flat = gates.reshape(-1)

    def expert_step(total, inputs):
        rows, wgate, wup, wdown = inputs
        valid = rows >= 0
        safe = jnp.maximum(rows, 0)
        owner = safe // TOPK
        xrows = jnp.where(valid[:, None], tokens[owner], jnp.zeros((), tokens.dtype))
        weight = jnp.where(valid, gate_flat[safe], jnp.zeros((), gate_flat.dtype))
        factor = coef[owner] * weight
        qrows = (factor[:, None] * cotangent[owner].astype(jnp.float32)).astype(jnp.bfloat16)
        gate_pre = jnp.dot(xrows, wgate.T, preferred_element_type=jnp.float32)
        up_pre = jnp.dot(xrows, wup.T, preferred_element_type=jnp.float32)
        sig = jax.nn.sigmoid(gate_pre)
        act = gate_pre * sig
        hidden = (act * up_pre).astype(jnp.bfloat16)
        expert_out = jnp.dot(hidden, wdown, preferred_element_type=jnp.float32).astype(jnp.bfloat16)
        contrib = weight[:, None] * expert_out.astype(jnp.float32)
        total = total.at[owner].add(jnp.where(valid[:, None], contrib, jnp.zeros((), contrib.dtype)))
        back = jnp.dot(qrows, wdown.T, preferred_element_type=jnp.float32)
        d_gate = (back * up_pre * sig * (1.0 + gate_pre * (1.0 - sig))).astype(jnp.bfloat16)
        d_up = (back * act).astype(jnp.bfloat16)
        grad_gate = jnp.dot(d_gate.T, xrows, preferred_element_type=jnp.float32)
        grad_up = jnp.dot(d_up.T, xrows, preferred_element_type=jnp.float32)
        grad_down = jnp.dot(hidden.T, qrows, preferred_element_type=jnp.float32)
        return total, jnp.stack([grad_gate, grad_up, grad_down], axis=1)

    start = jnp.zeros((TOKENS, D), jnp.float32)
    total, weight_grads = lax.scan(expert_step, start, (table, w_gate, w_up, w_down))
    return total.astype(jnp.bfloat16), weight_grads
```

```python
import jax
import jax.numpy as jnp
from jax import lax
from jax.sharding import PartitionSpec as P

GATHER_ROWS = 2048
RETURN = "a2a"


def contract_rows(left, right):
    return lax.dot_general(
        left, right, (((0,), (0,)), ((), ())), preferred_element_type=jnp.float32
    )


def contract_cols(left, right):
    return lax.dot_general(
        left, right, (((1,), (1,)), ((), ())), preferred_element_type=jnp.float32
    )


def expert_math(rows_x, rows_q, wgate, wup, wdown):
    gate_pre = contract_cols(rows_x, wgate)
    up_pre = contract_cols(rows_x, wup)
    sig = jax.nn.sigmoid(gate_pre)
    act = gate_pre * sig
    hidden = (act * up_pre).astype(jnp.bfloat16)
    expert_out = jnp.dot(hidden, wdown, preferred_element_type=jnp.float32).astype(
        jnp.bfloat16
    )
    back = contract_cols(rows_q, wdown)
    d_gate = (back * up_pre * sig * (1.0 + gate_pre * (1.0 - sig))).astype(jnp.bfloat16)
    d_up = (back * act).astype(jnp.bfloat16)
    grad_gate = contract_rows(d_gate, rows_x)
    grad_up = contract_rows(d_up, rows_x)
    grad_down = contract_rows(hidden, rows_q)
    return expert_out, jnp.stack([grad_gate, grad_up, grad_down], axis=1)


def reduce_grads(grads, width):
    share = grads.shape[0] // lax.axis_size("dp")
    summed = lax.psum_scatter(grads, "dp", scatter_dimension=0, tiled=True)
    return summed.reshape(1, share, 3, width)


def source_slots(routes, experts):
    flat = routes.reshape(-1)
    onehot = (flat[:, None] == jnp.arange(experts, dtype=jnp.int32)[None, :]).astype(jnp.int32)
    before = jnp.cumsum(onehot, axis=0) - onehot
    return flat, jnp.sum(before * onehot, axis=1)


def local_a2a(tokens, masked, importance, routes, gates, cotangent, w_gate, w_up, w_down):
    tok_rows = tokens.shape[0]
    width = tokens.shape[1]
    topk = routes.shape[1]
    experts = lax.axis_size("expert")
    capacity = min(tok_rows, 3 * tok_rows * topk // (2 * experts))
    flat, slots = source_slots(routes, experts)
    target = flat * capacity + slots
    owner = jnp.arange(tok_rows * topk, dtype=jnp.int32) // topk
    coef = importance * masked.astype(jnp.float32)
    factor = (coef[:, None] * gates).reshape(-1)
    sent_x = jnp.zeros((experts * capacity, width), jnp.bfloat16).at[target].set(tokens[owner])
    scaled = (factor[:, None] * cotangent[owner].astype(jnp.float32)).astype(jnp.bfloat16)
    sent_q = jnp.zeros((experts * capacity, width), jnp.bfloat16).at[target].set(scaled)
    layout = (experts, capacity, width)
    recv_x = lax.all_to_all(sent_x.reshape(layout), "expert", 0, 0, tiled=True)
    recv_q = lax.all_to_all(sent_q.reshape(layout), "expert", 0, 0, tiled=True)
    expert_out, grads = expert_math(
        recv_x.reshape(-1, width), recv_q.reshape(-1, width), w_gate[0], w_up[0], w_down[0]
    )
    returned = lax.all_to_all(expert_out.reshape(layout), "expert", 0, 0, tiled=True)
    picked = returned.reshape(-1, width)[target].astype(jnp.float32)
    summed = jnp.sum(picked.reshape(tok_rows, topk, width) * gates[:, :, None], axis=1)
    return summed.astype(jnp.bfloat16), reduce_grads(grads, width)


def local_gather(tokens, masked, importance, routes, gates, cotangent, w_gate, w_up, w_down):
    tok_rows = tokens.shape[0]
    width = tokens.shape[1]
    topk = routes.shape[1]
    experts = lax.axis_size("expert")
    capacity = min(tok_rows, 3 * tok_rows * topk // (2 * experts))
    me = lax.axis_index("expert")
    coef = importance * masked.astype(jnp.float32)
    factor = coef[:, None] * gates
    meta = jnp.concatenate([routes.astype(jnp.float32), factor, gates], axis=1)

    all_x = lax.all_gather(tokens, "expert", axis=0, tiled=True)
    all_meta = lax.all_gather(meta, "expert", axis=0, tiled=True)
    all_c = lax.all_gather(cotangent, "expert", axis=0, tiled=True)

    all_routes = all_meta[:, :topk].astype(jnp.int32)
    hit = all_routes == me
    zero = jnp.zeros((), jnp.float32)
    fac = jnp.sum(jnp.where(hit, all_meta[:, topk:2 * topk], zero), axis=1)
    gte = jnp.sum(jnp.where(hit, all_meta[:, 2 * topk:], zero), axis=1)
    routed = jnp.any(hit, axis=1).reshape(experts, tok_rows)
    ahead = (
        lax.broadcasted_iota(jnp.int32, (tok_rows, tok_rows), 0)
        < lax.broadcasted_iota(jnp.int32, (tok_rows, tok_rows), 1)
    ).astype(jnp.bfloat16)
    rank = jnp.dot(
        routed.astype(jnp.bfloat16), ahead, preferred_element_type=jnp.float32
    ).astype(jnp.int32)
    slot_ids = lax.broadcasted_iota(jnp.int32, (experts, capacity, tok_rows), 1)
    pick = (routed[:, None, :] & (rank[:, None, :] == slot_ids)).astype(jnp.bfloat16)

    def select(values):
        rows = jnp.einsum(
            "sjt,std->sjd",
            pick,
            values.reshape(experts, tok_rows, width),
            preferred_element_type=jnp.float32,
        )
        return rows.astype(jnp.bfloat16).reshape(experts * capacity, width)

    rows_x = select(all_x)
    all_q = (fac[:, None] * all_c.astype(jnp.float32)).astype(jnp.bfloat16)
    rows_q = select(all_q)
    expert_out, grads = expert_math(rows_x, rows_q, w_gate[0], w_up[0], w_down[0])

    if RETURN == "scatter":
        dense = jnp.einsum(
            "sjt,sjd->std",
            pick,
            expert_out.reshape(experts, capacity, width),
            preferred_element_type=jnp.float32,
        ).reshape(experts * tok_rows, width)
        contrib = gte[:, None] * dense
        summed = lax.psum_scatter(contrib, "expert", scatter_dimension=0, tiled=True)
    else:
        returned = lax.all_to_all(
            expert_out.reshape(experts, capacity, width), "expert", 0, 0, tiled=True
        )
        flat, slots = source_slots(routes, experts)
        target = flat * capacity + slots
        choose = (
            target[:, None]
            == lax.broadcasted_iota(jnp.int32, (tok_rows * topk, experts * capacity), 1)
        ).astype(jnp.bfloat16)
        picked = jnp.dot(
            choose, returned.reshape(-1, width), preferred_element_type=jnp.float32
        )
        summed = jnp.sum(picked.reshape(tok_rows, topk, width) * gates[:, :, None], axis=1)
    return summed.astype(jnp.bfloat16), reduce_grads(grads, width)


def local(*args):
    tokens = args[0]
    if lax.axis_size("expert") * tokens.shape[0] <= GATHER_ROWS:
        return local_gather(*args)
    return local_a2a(*args)


def solution(mesh):
    in_specs = (
        P(("dp", "expert"), None),
        P(("dp", "expert")),
        P(("dp", "expert")),
        P(("dp", "expert"), None),
        P(("dp", "expert"), None),
        P(("dp", "expert"), None),
        P("expert", None, None),
        P("expert", None, None),
        P("expert", None, None),
    )
    out_specs = (P(("dp", "expert"), None), P("expert", "dp", None, None))
    return jax.shard_map(local, mesh=mesh, in_specs=in_specs, out_specs=out_specs, check_vma=False)
```

```python
import jax
import jax.numpy as jnp
from jax import lax
from jax.sharding import PartitionSpec as P

GATHER_ROWS = 2048
RETURN = "scatter"


def contract_rows(left, right):
    return lax.dot_general(
        left, right, (((0,), (0,)), ((), ())), preferred_element_type=jnp.float32
    )


def contract_cols(left, right):
    return lax.dot_general(
        left, right, (((1,), (1,)), ((), ())), preferred_element_type=jnp.float32
    )


def expert_math(rows_x, rows_q, wgate, wup, wdown):
    gate_pre = contract_cols(rows_x, wgate)
    up_pre = contract_cols(rows_x, wup)
    sig = jax.nn.sigmoid(gate_pre)
    act = gate_pre * sig
    hidden = (act * up_pre).astype(jnp.bfloat16)
    expert_out = jnp.dot(hidden, wdown, preferred_element_type=jnp.float32).astype(
        jnp.bfloat16
    )
    back = contract_cols(rows_q, wdown)
    d_gate = (back * up_pre * sig * (1.0 + gate_pre * (1.0 - sig))).astype(jnp.bfloat16)
    d_up = (back * act).astype(jnp.bfloat16)
    grad_gate = contract_rows(d_gate, rows_x)
    grad_up = contract_rows(d_up, rows_x)
    grad_down = contract_rows(hidden, rows_q)
    return expert_out, jnp.stack([grad_gate, grad_up, grad_down], axis=1)


def reduce_grads(grads, width):
    share = grads.shape[0] // lax.axis_size("dp")
    summed = lax.psum_scatter(grads, "dp", scatter_dimension=0, tiled=True)
    return summed.reshape(1, share, 3, width)


def source_slots(routes, experts):
    flat = routes.reshape(-1)
    onehot = (flat[:, None] == jnp.arange(experts, dtype=jnp.int32)[None, :]).astype(jnp.int32)
    before = jnp.cumsum(onehot, axis=0) - onehot
    return flat, jnp.sum(before * onehot, axis=1)


def local_a2a(tokens, masked, importance, routes, gates, cotangent, w_gate, w_up, w_down):
    tok_rows = tokens.shape[0]
    width = tokens.shape[1]
    topk = routes.shape[1]
    experts = lax.axis_size("expert")
    capacity = min(tok_rows, 3 * tok_rows * topk // (2 * experts))
    flat, slots = source_slots(routes, experts)
    target = flat * capacity + slots
    owner = jnp.arange(tok_rows * topk, dtype=jnp.int32) // topk
    coef = importance * masked.astype(jnp.float32)
    factor = (coef[:, None] * gates).reshape(-1)
    sent_x = jnp.zeros((experts * capacity, width), jnp.bfloat16).at[target].set(tokens[owner])
    scaled = (factor[:, None] * cotangent[owner].astype(jnp.float32)).astype(jnp.bfloat16)
    sent_q = jnp.zeros((experts * capacity, width), jnp.bfloat16).at[target].set(scaled)
    layout = (experts, capacity, width)
    recv_x = lax.all_to_all(sent_x.reshape(layout), "expert", 0, 0, tiled=True)
    recv_q = lax.all_to_all(sent_q.reshape(layout), "expert", 0, 0, tiled=True)
    expert_out, grads = expert_math(
        recv_x.reshape(-1, width), recv_q.reshape(-1, width), w_gate[0], w_up[0], w_down[0]
    )
    returned = lax.all_to_all(expert_out.reshape(layout), "expert", 0, 0, tiled=True)
    picked = returned.reshape(-1, width)[target].astype(jnp.float32)
    summed = jnp.sum(picked.reshape(tok_rows, topk, width) * gates[:, :, None], axis=1)
    return summed.astype(jnp.bfloat16), reduce_grads(grads, width)


def local_gather(tokens, masked, importance, routes, gates, cotangent, w_gate, w_up, w_down):
    tok_rows = tokens.shape[0]
    width = tokens.shape[1]
    topk = routes.shape[1]
    experts = lax.axis_size("expert")
    capacity = min(tok_rows, 3 * tok_rows * topk // (2 * experts))
    me = lax.axis_index("expert")
    coef = importance * masked.astype(jnp.float32)
    factor = coef[:, None] * gates
    meta = jnp.concatenate([routes.astype(jnp.float32), factor, gates], axis=1)

    all_x = lax.all_gather(tokens, "expert", axis=0, tiled=True)
    all_meta = lax.all_gather(meta, "expert", axis=0, tiled=True)
    all_c = lax.all_gather(cotangent, "expert", axis=0, tiled=True)

    all_routes = all_meta[:, :topk].astype(jnp.int32)
    hit = all_routes == me
    zero = jnp.zeros((), jnp.float32)
    fac = jnp.sum(jnp.where(hit, all_meta[:, topk:2 * topk], zero), axis=1)
    gte = jnp.sum(jnp.where(hit, all_meta[:, 2 * topk:], zero), axis=1)
    routed = jnp.any(hit, axis=1).reshape(experts, tok_rows)
    ahead = (
        lax.broadcasted_iota(jnp.int32, (tok_rows, tok_rows), 0)
        < lax.broadcasted_iota(jnp.int32, (tok_rows, tok_rows), 1)
    ).astype(jnp.bfloat16)
    rank = jnp.dot(
        routed.astype(jnp.bfloat16), ahead, preferred_element_type=jnp.float32
    ).astype(jnp.int32)
    slot_ids = lax.broadcasted_iota(jnp.int32, (experts, capacity, tok_rows), 1)
    pick = (routed[:, None, :] & (rank[:, None, :] == slot_ids)).astype(jnp.bfloat16)

    def select(values):
        rows = jnp.einsum(
            "sjt,std->sjd",
            pick,
            values.reshape(experts, tok_rows, width),
            preferred_element_type=jnp.float32,
        )
        return rows.astype(jnp.bfloat16).reshape(experts * capacity, width)

    rows_x = select(all_x)
    all_q = (fac[:, None] * all_c.astype(jnp.float32)).astype(jnp.bfloat16)
    rows_q = select(all_q)
    expert_out, grads = expert_math(rows_x, rows_q, w_gate[0], w_up[0], w_down[0])

    if RETURN == "scatter":
        dense = jnp.einsum(
            "sjt,sjd->std",
            pick,
            expert_out.reshape(experts, capacity, width),
            preferred_element_type=jnp.float32,
        ).reshape(experts * tok_rows, width)
        contrib = gte[:, None] * dense
        summed = lax.psum_scatter(contrib, "expert", scatter_dimension=0, tiled=True)
    else:
        returned = lax.all_to_all(
            expert_out.reshape(experts, capacity, width), "expert", 0, 0, tiled=True
        )
        flat, slots = source_slots(routes, experts)
        target = flat * capacity + slots
        choose = (
            target[:, None]
            == lax.broadcasted_iota(jnp.int32, (tok_rows * topk, experts * capacity), 1)
        ).astype(jnp.bfloat16)
        picked = jnp.dot(
            choose, returned.reshape(-1, width), preferred_element_type=jnp.float32
        )
        summed = jnp.sum(picked.reshape(tok_rows, topk, width) * gates[:, :, None], axis=1)
    return summed.astype(jnp.bfloat16), reduce_grads(grads, width)


def local(*args):
    tokens = args[0]
    if lax.axis_size("expert") * tokens.shape[0] <= GATHER_ROWS:
        return local_gather(*args)
    return local_a2a(*args)


def solution(mesh):
    in_specs = (
        P(("dp", "expert"), None),
        P(("dp", "expert")),
        P(("dp", "expert")),
        P(("dp", "expert"), None),
        P(("dp", "expert"), None),
        P(("dp", "expert"), None),
        P("expert", None, None),
        P("expert", None, None),
        P("expert", None, None),
    )
    out_specs = (P(("dp", "expert"), None), P("expert", "dp", None, None))
    return jax.shard_map(local, mesh=mesh, in_specs=in_specs, out_specs=out_specs, check_vma=False)
```

```python
import jax
import jax.numpy as jnp
from jax import lax
from jax.sharding import PartitionSpec as P

GATHER_ROWS = 2048


def contract_rows(left, right):
    return lax.dot_general(
        left, right, (((0,), (0,)), ((), ())), preferred_element_type=jnp.float32
    )


def contract_cols(left, right):
    return lax.dot_general(
        left, right, (((1,), (1,)), ((), ())), preferred_element_type=jnp.float32
    )


def expert_math(rows_x, rows_q, wgate, wup, wdown):
    gate_pre = contract_cols(rows_x, wgate)
    up_pre = contract_cols(rows_x, wup)
    sig = jax.nn.sigmoid(gate_pre)
    act = gate_pre * sig
    hidden = (act * up_pre).astype(jnp.bfloat16)
    expert_out = jnp.dot(hidden, wdown, preferred_element_type=jnp.float32).astype(
        jnp.bfloat16
    )
    back = contract_cols(rows_q, wdown)
    d_gate = (back * up_pre * sig * (1.0 + gate_pre * (1.0 - sig))).astype(jnp.bfloat16)
    d_up = (back * act).astype(jnp.bfloat16)
    grad_gate = contract_rows(d_gate, rows_x)
    grad_up = contract_rows(d_up, rows_x)
    grad_down = contract_rows(hidden, rows_q)
    return expert_out, jnp.stack([grad_gate, grad_up, grad_down], axis=1)


def reduce_grads(grads, width):
    share = grads.shape[0] // lax.axis_size("dp")
    summed = lax.psum_scatter(grads, "dp", scatter_dimension=0, tiled=True)
    return summed.reshape(1, share, 3, width)


def source_slots(routes, experts):
    flat = routes.reshape(-1)
    onehot = (flat[:, None] == jnp.arange(experts, dtype=jnp.int32)[None, :]).astype(jnp.int32)
    before = jnp.cumsum(onehot, axis=0) - onehot
    return flat, jnp.sum(before * onehot, axis=1)


def local_a2a(tokens, masked, importance, routes, gates, cotangent, w_gate, w_up, w_down):
    tok_rows = tokens.shape[0]
    width = tokens.shape[1]
    topk = routes.shape[1]
    experts = lax.axis_size("expert")
    capacity = min(tok_rows, 3 * tok_rows * topk // (2 * experts))
    flat, slots = source_slots(routes, experts)
    target = flat * capacity + slots
    owner = jnp.arange(tok_rows * topk, dtype=jnp.int32) // topk
    coef = importance * masked.astype(jnp.float32)
    factor = (coef[:, None] * gates).reshape(-1)
    sent_x = jnp.zeros((experts * capacity, width), jnp.bfloat16).at[target].set(tokens[owner])
    scaled = (factor[:, None] * cotangent[owner].astype(jnp.float32)).astype(jnp.bfloat16)
    sent_q = jnp.zeros((experts * capacity, width), jnp.bfloat16).at[target].set(scaled)
    layout = (experts, capacity, width)
    recv_x = lax.all_to_all(sent_x.reshape(layout), "expert", 0, 0, tiled=True)
    recv_q = lax.all_to_all(sent_q.reshape(layout), "expert", 0, 0, tiled=True)
    expert_out, grads = expert_math(
        recv_x.reshape(-1, width), recv_q.reshape(-1, width), w_gate[0], w_up[0], w_down[0]
    )
    returned = lax.all_to_all(expert_out.reshape(layout), "expert", 0, 0, tiled=True)
    picked = returned.reshape(-1, width)[target].astype(jnp.float32)
    summed = jnp.sum(picked.reshape(tok_rows, topk, width) * gates[:, :, None], axis=1)
    return summed.astype(jnp.bfloat16), reduce_grads(grads, width)


def exact_pieces(values):
    high = lax.reduce_precision(values, exponent_bits=8, mantissa_bits=7)
    rest = values - high
    middle = lax.reduce_precision(rest, exponent_bits=8, mantissa_bits=7)
    low = rest - middle
    return [part.astype(jnp.bfloat16) for part in (high, middle, low)]


def joined(pieces):
    total = pieces[0].astype(jnp.float32) + pieces[1].astype(jnp.float32)
    return total + pieces[2].astype(jnp.float32)


def gather_replica(values):
    mine = lax.all_gather(values, "ez", axis=0, tiled=True)
    other = lax.ppermute(mine, "core", [(0, 1), (1, 0)])
    return jnp.concatenate([mine, other], axis=0)


def reduce_grads_dp(grad_half, width):
    ndp = lax.axis_size("dp")
    if ndp != 2:
        grads = jnp.concatenate([grad_half(h) for h in range(ndp)], axis=0)
        return reduce_grads(grads, width)
    d = lax.axis_index("dp")
    sent = lax.ppermute(grad_half(1 - d), "dp", [(0, 1), (1, 0)])
    summed = grad_half(d) + sent
    return summed.reshape(1, summed.shape[0], 3, width)


def local_gather(tokens, masked, importance, routes, gates, cotangent, w_gate, w_up, w_down):
    tok_rows = tokens.shape[0]
    width = tokens.shape[1]
    topk = routes.shape[1]
    ncore = lax.axis_size("core")
    nchip = lax.axis_size("ez")
    experts = nchip * ncore
    capacity = min(tok_rows, 3 * tok_rows * topk // (2 * experts))
    core = lax.axis_index("core")
    me = lax.axis_index("ez") * ncore + core
    coef = importance * masked.astype(jnp.float32)
    factor = coef[:, None] * gates
    meta = [routes.astype(jnp.bfloat16)] + exact_pieces(factor) + exact_pieces(gates)
    pad = (-topk * len(meta)) % 128
    meta.append(jnp.zeros((tok_rows, pad), jnp.bfloat16))
    packed = jnp.concatenate([tokens] + meta, axis=1)

    all_p = gather_replica(packed)
    all_c = gather_replica(cotangent)
    all_x = all_p[:, :width]
    cols = [all_p[:, width + topk * i: width + topk * (i + 1)] for i in range(7)]
    hit = cols[0].astype(jnp.int32) == me
    zero = jnp.zeros((), jnp.float32)
    fac = jnp.sum(jnp.where(hit, joined(cols[1:4]), zero), axis=1)
    routed = jnp.any(hit, axis=1).reshape(experts, tok_rows)
    ahead = (
        lax.broadcasted_iota(jnp.int32, (tok_rows, tok_rows), 0)
        < lax.broadcasted_iota(jnp.int32, (tok_rows, tok_rows), 1)
    ).astype(jnp.bfloat16)
    rank = jnp.dot(
        routed.astype(jnp.bfloat16), ahead, preferred_element_type=jnp.float32
    ).astype(jnp.int32)
    slot_ids = lax.broadcasted_iota(jnp.int32, (experts, capacity, tok_rows), 1)
    pick = (routed[:, None, :] & (rank[:, None, :] == slot_ids)).astype(jnp.bfloat16)

    def select(values):
        rows = jnp.einsum(
            "sjt,std->sjd",
            pick,
            values.reshape(experts, tok_rows, width),
            preferred_element_type=jnp.float32,
        )
        return rows.astype(jnp.bfloat16).reshape(experts * capacity, width)

    rows_x = select(all_x)
    all_q = (fac[:, None] * all_c.astype(jnp.float32)).astype(jnp.bfloat16)
    rows_q = select(all_q)
    wgate, wup, wdown = w_gate[0], w_up[0], w_down[0]
    gate_pre = contract_cols(rows_x, wgate)
    up_pre = contract_cols(rows_x, wup)
    sig = jax.nn.sigmoid(gate_pre)
    act = gate_pre * sig
    hidden = (act * up_pre).astype(jnp.bfloat16)
    expert_out = jnp.dot(hidden, wdown, preferred_element_type=jnp.float32).astype(
        jnp.bfloat16
    )

    by_group = expert_out.reshape(ncore, nchip, capacity, width)
    ordered = jnp.stack(
        [lax.dynamic_index_in_dim(by_group, k ^ core, 0, keepdims=False) for k in range(ncore)],
        axis=1,
    ).reshape(experts, capacity, width)
    returned = lax.all_to_all(ordered, ("ez", "core"), 0, 0, tiled=True)

    back = contract_cols(rows_q, wdown)
    d_gate = (back * up_pre * sig * (1.0 + gate_pre * (1.0 - sig))).astype(jnp.bfloat16)
    d_up = (back * act).astype(jnp.bfloat16)
    share = d_gate.shape[1] // lax.axis_size("dp")

    def grad_half(h):
        def part(v):
            return lax.dynamic_slice_in_dim(v, h * share, share, axis=1)

        return jnp.stack(
            [
                contract_rows(part(d_gate), rows_x),
                contract_rows(part(d_up), rows_x),
                contract_rows(part(hidden), rows_q),
            ],
            axis=1,
        )

    weight_grads = reduce_grads_dp(grad_half, width)

    flat, slots = source_slots(routes, experts)
    target = flat * capacity + slots
    choose = (
        target[:, None]
        == lax.broadcasted_iota(jnp.int32, (tok_rows * topk, experts * capacity), 1)
    ).astype(jnp.bfloat16)
    picked = jnp.dot(choose, returned.reshape(-1, width), preferred_element_type=jnp.float32)
    summed = jnp.sum(picked.reshape(tok_rows, topk, width) * gates[:, :, None], axis=1)
    return summed.astype(jnp.bfloat16), weight_grads


def specs(rows, experts):
    return (
        (P(rows, None), P(rows), P(rows), P(rows, None), P(rows, None), P(rows, None))
        + (P(experts, None, None),) * 3,
        (P(rows, None), P(experts, "dp", None, None)),
    )


def solution(mesh):
    ndp, nexp = mesh.shape["dp"], mesh.shape["expert"]
    split = jax.sharding.Mesh(mesh.devices.reshape(ndp, nexp // 2, 2), ("dp", "ez", "core"))
    ins, outs = specs(("dp", "ez", "core"), ("ez", "core"))
    gathered = jax.shard_map(local_gather, mesh=split, in_specs=ins, out_specs=outs, check_vma=False)
    ins, outs = specs(("dp", "expert"), "expert")
    routed = jax.shard_map(local_a2a, mesh=mesh, in_specs=ins, out_specs=outs, check_vma=False)

    def run(*args):
        if args[0].shape[0] // ndp <= GATHER_ROWS:
            return gathered(*args)
        return routed(*args)

    return run
```

```python
import jax
import jax.numpy as jnp
from jax import lax
from jax.sharding import PartitionSpec as P

GATHER_ROWS = 2048


def contract_rows(left, right):
    return lax.dot_general(
        left, right, (((0,), (0,)), ((), ())), preferred_element_type=jnp.float32
    )


def contract_cols(left, right):
    return lax.dot_general(
        left, right, (((1,), (1,)), ((), ())), preferred_element_type=jnp.float32
    )


def expert_math(rows_x, rows_q, wgate, wup, wdown):
    gate_pre = contract_cols(rows_x, wgate)
    up_pre = contract_cols(rows_x, wup)
    sig = jax.nn.sigmoid(gate_pre)
    act = gate_pre * sig
    hidden = (act * up_pre).astype(jnp.bfloat16)
    expert_out = jnp.dot(hidden, wdown, preferred_element_type=jnp.float32).astype(
        jnp.bfloat16
    )
    back = contract_cols(rows_q, wdown)
    d_gate = (back * up_pre * sig * (1.0 + gate_pre * (1.0 - sig))).astype(jnp.bfloat16)
    d_up = (back * act).astype(jnp.bfloat16)
    grad_gate = contract_rows(d_gate, rows_x)
    grad_up = contract_rows(d_up, rows_x)
    grad_down = contract_rows(hidden, rows_q)
    return expert_out, jnp.stack([grad_gate, grad_up, grad_down], axis=1)


def reduce_grads(grads, width):
    share = grads.shape[0] // lax.axis_size("dp")
    summed = lax.psum_scatter(grads, "dp", scatter_dimension=0, tiled=True)
    return summed.reshape(1, share, 3, width)


def source_slots(routes, experts):
    flat = routes.reshape(-1)
    onehot = (flat[:, None] == jnp.arange(experts, dtype=jnp.int32)[None, :]).astype(jnp.int32)
    before = jnp.cumsum(onehot, axis=0) - onehot
    return flat, jnp.sum(before * onehot, axis=1)


def local_a2a(tokens, masked, importance, routes, gates, cotangent, w_gate, w_up, w_down):
    tok_rows = tokens.shape[0]
    width = tokens.shape[1]
    topk = routes.shape[1]
    experts = lax.axis_size("expert")
    capacity = min(tok_rows, 3 * tok_rows * topk // (2 * experts))
    flat, slots = source_slots(routes, experts)
    target = flat * capacity + slots
    owner = jnp.arange(tok_rows * topk, dtype=jnp.int32) // topk
    coef = importance * masked.astype(jnp.float32)
    factor = (coef[:, None] * gates).reshape(-1)
    sent_x = jnp.zeros((experts * capacity, width), jnp.bfloat16).at[target].set(tokens[owner])
    scaled = (factor[:, None] * cotangent[owner].astype(jnp.float32)).astype(jnp.bfloat16)
    sent_q = jnp.zeros((experts * capacity, width), jnp.bfloat16).at[target].set(scaled)
    layout = (experts, capacity, width)
    recv_x = lax.all_to_all(sent_x.reshape(layout), "expert", 0, 0, tiled=True)
    recv_q = lax.all_to_all(sent_q.reshape(layout), "expert", 0, 0, tiled=True)
    expert_out, grads = expert_math(
        recv_x.reshape(-1, width), recv_q.reshape(-1, width), w_gate[0], w_up[0], w_down[0]
    )
    returned = lax.all_to_all(expert_out.reshape(layout), "expert", 0, 0, tiled=True)
    picked = returned.reshape(-1, width)[target].astype(jnp.float32)
    summed = jnp.sum(picked.reshape(tok_rows, topk, width) * gates[:, :, None], axis=1)
    return summed.astype(jnp.bfloat16), reduce_grads(grads, width)


def exact_pieces(values):
    high = lax.reduce_precision(values, exponent_bits=8, mantissa_bits=7)
    rest = values - high
    middle = lax.reduce_precision(rest, exponent_bits=8, mantissa_bits=7)
    low = rest - middle
    return [part.astype(jnp.bfloat16) for part in (high, middle, low)]


def joined(pieces):
    total = pieces[0].astype(jnp.float32) + pieces[1].astype(jnp.float32)
    return total + pieces[2].astype(jnp.float32)


def gather_replica(values):
    mine = lax.all_gather(values, "ez", axis=0, tiled=True)
    other = lax.ppermute(mine, "core", [(0, 1), (1, 0)])
    return jnp.concatenate([mine, other], axis=0)


def reduce_grads_dp(grad_half, width):
    ndp = lax.axis_size("dp")
    if ndp != 2:
        grads = jnp.concatenate([grad_half(h) for h in range(ndp)], axis=0)
        return reduce_grads(grads, width)
    d = lax.axis_index("dp")
    sent = lax.ppermute(grad_half(1 - d), "dp", [(0, 1), (1, 0)])
    summed = grad_half(d) + sent
    return summed.reshape(1, summed.shape[0], 3, width)


def local_gather(tokens, masked, importance, routes, gates, cotangent, w_gate, w_up, w_down):
    tok_rows = tokens.shape[0]
    width = tokens.shape[1]
    topk = routes.shape[1]
    ncore = lax.axis_size("core")
    nchip = lax.axis_size("ez")
    experts = nchip * ncore
    capacity = min(tok_rows, 3 * tok_rows * topk // (2 * experts))
    core = lax.axis_index("core")
    me = lax.axis_index("ez") * ncore + core
    coef = importance * masked.astype(jnp.float32)
    factor = coef[:, None] * gates
    meta = [routes.astype(jnp.bfloat16)] + exact_pieces(factor) + exact_pieces(gates)
    pad = (-topk * len(meta)) % 128
    meta.append(jnp.zeros((tok_rows, pad), jnp.bfloat16))
    packed = jnp.concatenate([tokens, cotangent] + meta, axis=1)

    all_p = gather_replica(packed)
    all_x = all_p[:, :width]
    all_c = all_p[:, width:2 * width]
    cols = [all_p[:, 2 * width + topk * i: 2 * width + topk * (i + 1)] for i in range(7)]
    hit = cols[0].astype(jnp.int32) == me
    zero = jnp.zeros((), jnp.float32)
    fac = jnp.sum(jnp.where(hit, joined(cols[1:4]), zero), axis=1)
    routed = jnp.any(hit, axis=1).reshape(experts, tok_rows)
    ahead = (
        lax.broadcasted_iota(jnp.int32, (tok_rows, tok_rows), 0)
        < lax.broadcasted_iota(jnp.int32, (tok_rows, tok_rows), 1)
    ).astype(jnp.bfloat16)
    rank = jnp.dot(
        routed.astype(jnp.bfloat16), ahead, preferred_element_type=jnp.float32
    ).astype(jnp.int32)
    slot_ids = lax.broadcasted_iota(jnp.int32, (experts, capacity, tok_rows), 1)
    pick = (routed[:, None, :] & (rank[:, None, :] == slot_ids)).astype(jnp.bfloat16)

    def select(values):
        rows = jnp.einsum(
            "sjt,std->sjd",
            pick,
            values.reshape(experts, tok_rows, width),
            preferred_element_type=jnp.float32,
        )
        return rows.astype(jnp.bfloat16).reshape(experts * capacity, width)

    rows_x = select(all_x)
    all_q = (fac[:, None] * all_c.astype(jnp.float32)).astype(jnp.bfloat16)
    rows_q = select(all_q)
    wgate, wup, wdown = w_gate[0], w_up[0], w_down[0]
    gate_pre = contract_cols(rows_x, wgate)
    up_pre = contract_cols(rows_x, wup)
    sig = jax.nn.sigmoid(gate_pre)
    act = gate_pre * sig
    hidden = (act * up_pre).astype(jnp.bfloat16)
    expert_out = jnp.dot(hidden, wdown, preferred_element_type=jnp.float32).astype(
        jnp.bfloat16
    )

    by_group = expert_out.reshape(ncore, nchip, capacity, width)
    ordered = jnp.stack(
        [lax.dynamic_index_in_dim(by_group, k ^ core, 0, keepdims=False) for k in range(ncore)],
        axis=1,
    ).reshape(experts, capacity, width)
    returned = lax.all_to_all(ordered, ("ez", "core"), 0, 0, tiled=True)

    back = contract_cols(rows_q, wdown)
    d_gate = (back * up_pre * sig * (1.0 + gate_pre * (1.0 - sig))).astype(jnp.bfloat16)
    d_up = (back * act).astype(jnp.bfloat16)
    share = d_gate.shape[1] // lax.axis_size("dp")

    def grad_half(h):
        def part(v):
            return lax.dynamic_slice_in_dim(v, h * share, share, axis=1)

        return jnp.stack(
            [
                contract_rows(part(d_gate), rows_x),
                contract_rows(part(d_up), rows_x),
                contract_rows(part(hidden), rows_q),
            ],
            axis=1,
        )

    weight_grads = reduce_grads_dp(grad_half, width)

    flat, slots = source_slots(routes, experts)
    target = flat * capacity + slots
    choose = (
        target[:, None]
        == lax.broadcasted_iota(jnp.int32, (tok_rows * topk, experts * capacity), 1)
    ).astype(jnp.bfloat16)
    picked = jnp.dot(choose, returned.reshape(-1, width), preferred_element_type=jnp.float32)
    summed = jnp.sum(picked.reshape(tok_rows, topk, width) * gates[:, :, None], axis=1)
    return summed.astype(jnp.bfloat16), weight_grads


def specs(rows, experts):
    return (
        (P(rows, None), P(rows), P(rows), P(rows, None), P(rows, None), P(rows, None))
        + (P(experts, None, None),) * 3,
        (P(rows, None), P(experts, "dp", None, None)),
    )


def solution(mesh):
    ndp, nexp = mesh.shape["dp"], mesh.shape["expert"]
    split = jax.sharding.Mesh(mesh.devices.reshape(ndp, nexp // 2, 2), ("dp", "ez", "core"))
    ins, outs = specs(("dp", "ez", "core"), ("ez", "core"))
    gathered = jax.shard_map(local_gather, mesh=split, in_specs=ins, out_specs=outs, check_vma=False)
    ins, outs = specs(("dp", "expert"), "expert")
    routed = jax.shard_map(local_a2a, mesh=mesh, in_specs=ins, out_specs=outs, check_vma=False)

    def run(*args):
        if args[0].shape[0] // ndp <= GATHER_ROWS:
            return gathered(*args)
        return routed(*args)

    return run
```

```python
import jax
import jax.numpy as jnp
from jax import lax
from jax.sharding import PartitionSpec as P

GATHER_ROWS = 2048


def contract_rows(left, right):
    return lax.dot_general(
        left, right, (((0,), (0,)), ((), ())), preferred_element_type=jnp.float32
    )


def contract_cols(left, right):
    return lax.dot_general(
        left, right, (((1,), (1,)), ((), ())), preferred_element_type=jnp.float32
    )


def expert_math(rows_x, rows_q, wgate, wup, wdown):
    gate_pre = contract_cols(rows_x, wgate)
    up_pre = contract_cols(rows_x, wup)
    sig = jax.nn.sigmoid(gate_pre)
    act = gate_pre * sig
    hidden = (act * up_pre).astype(jnp.bfloat16)
    expert_out = jnp.dot(hidden, wdown, preferred_element_type=jnp.float32).astype(
        jnp.bfloat16
    )
    back = contract_cols(rows_q, wdown)
    d_gate = (back * up_pre * sig * (1.0 + gate_pre * (1.0 - sig))).astype(jnp.bfloat16)
    d_up = (back * act).astype(jnp.bfloat16)
    grad_gate = contract_rows(d_gate, rows_x)
    grad_up = contract_rows(d_up, rows_x)
    grad_down = contract_rows(hidden, rows_q)
    return expert_out, jnp.stack([grad_gate, grad_up, grad_down], axis=1)


def reduce_grads(grads, width):
    share = grads.shape[0] // lax.axis_size("dp")
    summed = lax.psum_scatter(grads, "dp", scatter_dimension=0, tiled=True)
    return summed.reshape(1, share, 3, width)


def source_slots(routes, experts):
    flat = routes.reshape(-1)
    onehot = (flat[:, None] == jnp.arange(experts, dtype=jnp.int32)[None, :]).astype(jnp.int32)
    before = jnp.cumsum(onehot, axis=0) - onehot
    return flat, jnp.sum(before * onehot, axis=1)


def local_a2a(tokens, masked, importance, routes, gates, cotangent, w_gate, w_up, w_down):
    tok_rows = tokens.shape[0]
    width = tokens.shape[1]
    topk = routes.shape[1]
    experts = lax.axis_size("expert")
    capacity = min(tok_rows, 3 * tok_rows * topk // (2 * experts))
    flat, slots = source_slots(routes, experts)
    target = flat * capacity + slots
    owner = jnp.arange(tok_rows * topk, dtype=jnp.int32) // topk
    coef = importance * masked.astype(jnp.float32)
    factor = (coef[:, None] * gates).reshape(-1)
    sent_x = jnp.zeros((experts * capacity, width), jnp.bfloat16).at[target].set(tokens[owner])
    scaled = (factor[:, None] * cotangent[owner].astype(jnp.float32)).astype(jnp.bfloat16)
    sent_q = jnp.zeros((experts * capacity, width), jnp.bfloat16).at[target].set(scaled)
    layout = (experts, capacity, width)
    recv_x = lax.all_to_all(sent_x.reshape(layout), "expert", 0, 0, tiled=True)
    recv_q = lax.all_to_all(sent_q.reshape(layout), "expert", 0, 0, tiled=True)
    expert_out, grads = expert_math(
        recv_x.reshape(-1, width), recv_q.reshape(-1, width), w_gate[0], w_up[0], w_down[0]
    )
    returned = lax.all_to_all(expert_out.reshape(layout), "expert", 0, 0, tiled=True)
    picked = returned.reshape(-1, width)[target].astype(jnp.float32)
    summed = jnp.sum(picked.reshape(tok_rows, topk, width) * gates[:, :, None], axis=1)
    return summed.astype(jnp.bfloat16), reduce_grads(grads, width)


def exact_pieces(values):
    high = lax.reduce_precision(values, exponent_bits=8, mantissa_bits=7)
    rest = values - high
    middle = lax.reduce_precision(rest, exponent_bits=8, mantissa_bits=7)
    low = rest - middle
    return [part.astype(jnp.bfloat16) for part in (high, middle, low)]


def joined(pieces):
    total = pieces[0].astype(jnp.float32) + pieces[1].astype(jnp.float32)
    return total + pieces[2].astype(jnp.float32)


def gather_replica(values):
    mine = lax.all_gather(values, "ez", axis=0, tiled=True)
    return [mine, lax.ppermute(mine, "core", [(0, 1), (1, 0)])]


def slots_by_rank(routes, experts):
    tok_rows = routes.shape[0]
    onehot = routes[:, :, None] == lax.broadcasted_iota(jnp.int32, (1, 1, experts), 2)
    hits = jnp.any(onehot, axis=1).astype(jnp.bfloat16)
    before = (
        lax.broadcasted_iota(jnp.int32, (tok_rows, tok_rows), 0)
        > lax.broadcasted_iota(jnp.int32, (tok_rows, tok_rows), 1)
    ).astype(jnp.bfloat16)
    rank = jnp.dot(before, hits, preferred_element_type=jnp.float32).astype(jnp.int32)
    return jnp.sum(jnp.where(onehot, rank[:, None, :], 0), axis=2)


def reduce_grads_dp(grad_half, width):
    ndp = lax.axis_size("dp")
    if ndp != 2:
        grads = jnp.concatenate([grad_half(h) for h in range(ndp)], axis=0)
        return reduce_grads(grads, width)
    d = lax.axis_index("dp")
    sent = lax.ppermute(grad_half(1 - d), "dp", [(0, 1), (1, 0)])
    summed = grad_half(d) + sent
    return summed.reshape(1, summed.shape[0], 3, width)


def local_gather(tokens, masked, importance, routes, gates, cotangent, w_gate, w_up, w_down):
    tok_rows = tokens.shape[0]
    width = tokens.shape[1]
    topk = routes.shape[1]
    ncore = lax.axis_size("core")
    nchip = lax.axis_size("ez")
    experts = nchip * ncore
    capacity = min(tok_rows, 3 * tok_rows * topk // (2 * experts))
    core = lax.axis_index("core")
    me = lax.axis_index("ez") * ncore + core
    coef = importance * masked.astype(jnp.float32)
    factor = coef[:, None] * gates
    meta = [routes.astype(jnp.bfloat16)] + exact_pieces(factor) + exact_pieces(gates)
    pad = (-topk * len(meta)) % 128
    meta.append(jnp.zeros((tok_rows, pad), jnp.bfloat16))
    packed = jnp.concatenate([tokens, cotangent] + meta, axis=1)

    halves = gather_replica(packed)
    all_p = jnp.concatenate([h[:, 2 * width:] for h in halves], axis=0)
    cols = [all_p[:, topk * i: topk * (i + 1)] for i in range(7)]
    hit = cols[0].astype(jnp.int32) == me
    zero = jnp.zeros((), jnp.float32)
    fac = jnp.sum(jnp.where(hit, joined(cols[1:4]), zero), axis=1)
    routed = jnp.any(hit, axis=1).reshape(experts, tok_rows)
    ahead = (
        lax.broadcasted_iota(jnp.int32, (tok_rows, tok_rows), 0)
        < lax.broadcasted_iota(jnp.int32, (tok_rows, tok_rows), 1)
    ).astype(jnp.bfloat16)
    rank = jnp.dot(
        routed.astype(jnp.bfloat16), ahead, preferred_element_type=jnp.float32
    ).astype(jnp.int32)
    slot_ids = lax.broadcasted_iota(jnp.int32, (experts, capacity, tok_rows), 1)
    pick = (routed[:, None, :] & (rank[:, None, :] == slot_ids)).astype(jnp.bfloat16)

    def select(part, scale=None):
        picked = []
        for h, half in enumerate(halves):
            values = half[:, part * width:(part + 1) * width]
            if scale is not None:
                rows = slice(h * nchip * tok_rows, (h + 1) * nchip * tok_rows)
                values = (scale[rows, None] * values.astype(jnp.float32)).astype(jnp.bfloat16)
            picked.append(
                jnp.einsum(
                    "sjt,std->sjd",
                    pick[h * nchip:(h + 1) * nchip],
                    values.reshape(nchip, tok_rows, width),
                    preferred_element_type=jnp.float32,
                ).astype(jnp.bfloat16)
            )
        return jnp.concatenate(picked, axis=0).reshape(experts * capacity, width)

    rows_x = select(0)
    rows_q = select(1, fac)
    wgate, wup, wdown = w_gate[0], w_up[0], w_down[0]
    gate_pre = contract_cols(rows_x, wgate)
    up_pre = contract_cols(rows_x, wup)
    sig = jax.nn.sigmoid(gate_pre)
    act = gate_pre * sig
    hidden = (act * up_pre).astype(jnp.bfloat16)
    expert_out = jnp.dot(hidden, wdown, preferred_element_type=jnp.float32).astype(
        jnp.bfloat16
    )

    by_group = expert_out.reshape(ncore, nchip, capacity, width)
    ordered = jnp.stack(
        [lax.dynamic_index_in_dim(by_group, k ^ core, 0, keepdims=False) for k in range(ncore)],
        axis=1,
    ).reshape(experts, capacity, width)
    returned = lax.all_to_all(ordered, ("ez", "core"), 0, 0, tiled=True)

    back = contract_cols(rows_q, wdown)
    d_gate = (back * up_pre * sig * (1.0 + gate_pre * (1.0 - sig))).astype(jnp.bfloat16)
    d_up = (back * act).astype(jnp.bfloat16)
    share = d_gate.shape[1] // lax.axis_size("dp")

    def grad_half(h):
        def part(v):
            return lax.dynamic_slice_in_dim(v, h * share, share, axis=1)

        return jnp.stack(
            [
                contract_rows(part(d_gate), rows_x),
                contract_rows(part(d_up), rows_x),
                contract_rows(part(hidden), rows_q),
            ],
            axis=1,
        )

    weight_grads = reduce_grads_dp(grad_half, width)

    target = (routes * capacity + slots_by_rank(routes, experts)).reshape(-1)
    choose = (
        target[:, None]
        == lax.broadcasted_iota(jnp.int32, (tok_rows * topk, experts * capacity), 1)
    ).astype(jnp.bfloat16)
    picked = jnp.dot(choose, returned.reshape(-1, width), preferred_element_type=jnp.float32)
    summed = jnp.sum(picked.reshape(tok_rows, topk, width) * gates[:, :, None], axis=1)
    return summed.astype(jnp.bfloat16), weight_grads


def specs(rows, experts):
    return (
        (P(rows, None), P(rows), P(rows), P(rows, None), P(rows, None), P(rows, None))
        + (P(experts, None, None),) * 3,
        (P(rows, None), P(experts, "dp", None, None)),
    )


def solution(mesh):
    ndp, nexp = mesh.shape["dp"], mesh.shape["expert"]
    split = jax.sharding.Mesh(mesh.devices.reshape(ndp, nexp // 2, 2), ("dp", "ez", "core"))
    ins, outs = specs(("dp", "ez", "core"), ("ez", "core"))
    gathered = jax.shard_map(local_gather, mesh=split, in_specs=ins, out_specs=outs, check_vma=False)
    ins, outs = specs(("dp", "expert"), "expert")
    routed = jax.shard_map(local_a2a, mesh=mesh, in_specs=ins, out_specs=outs, check_vma=False)

    def run(*args):
        if args[0].shape[0] // ndp <= GATHER_ROWS:
            return gathered(*args)
        return routed(*args)

    return run
```

```python
import jax
import jax.numpy as jnp
from jax import lax
from jax.sharding import PartitionSpec as P

GATHER_ROWS = 2048


def contract_rows(left, right):
    return lax.dot_general(
        left, right, (((0,), (0,)), ((), ())), preferred_element_type=jnp.float32
    )


def contract_cols(left, right):
    return lax.dot_general(
        left, right, (((1,), (1,)), ((), ())), preferred_element_type=jnp.float32
    )


def expert_math(rows_x, rows_q, wgate, wup, wdown):
    gate_pre = contract_cols(rows_x, wgate)
    up_pre = contract_cols(rows_x, wup)
    sig = jax.nn.sigmoid(gate_pre)
    act = gate_pre * sig
    hidden = (act * up_pre).astype(jnp.bfloat16)
    expert_out = jnp.dot(hidden, wdown, preferred_element_type=jnp.float32).astype(
        jnp.bfloat16
    )
    back = contract_cols(rows_q, wdown)
    d_gate = (back * up_pre * sig * (1.0 + gate_pre * (1.0 - sig))).astype(jnp.bfloat16)
    d_up = (back * act).astype(jnp.bfloat16)
    grad_gate = contract_rows(d_gate, rows_x)
    grad_up = contract_rows(d_up, rows_x)
    grad_down = contract_rows(hidden, rows_q)
    return expert_out, jnp.stack([grad_gate, grad_up, grad_down], axis=1)


def reduce_grads(grads, width):
    share = grads.shape[0] // lax.axis_size("dp")
    summed = lax.psum_scatter(grads, "dp", scatter_dimension=0, tiled=True)
    return summed.reshape(1, share, 3, width)


def source_slots(routes, experts):
    flat = routes.reshape(-1)
    onehot = (flat[:, None] == jnp.arange(experts, dtype=jnp.int32)[None, :]).astype(jnp.int32)
    before = jnp.cumsum(onehot, axis=0) - onehot
    return flat, jnp.sum(before * onehot, axis=1)


def local_a2a(tokens, masked, importance, routes, gates, cotangent, w_gate, w_up, w_down):
    tok_rows = tokens.shape[0]
    width = tokens.shape[1]
    topk = routes.shape[1]
    experts = lax.axis_size("expert")
    capacity = min(tok_rows, 3 * tok_rows * topk // (2 * experts))
    flat, slots = source_slots(routes, experts)
    target = flat * capacity + slots
    owner = jnp.arange(tok_rows * topk, dtype=jnp.int32) // topk
    coef = importance * masked.astype(jnp.float32)
    factor = (coef[:, None] * gates).reshape(-1)
    sent_x = jnp.zeros((experts * capacity, width), jnp.bfloat16).at[target].set(tokens[owner])
    scaled = (factor[:, None] * cotangent[owner].astype(jnp.float32)).astype(jnp.bfloat16)
    sent_q = jnp.zeros((experts * capacity, width), jnp.bfloat16).at[target].set(scaled)
    layout = (experts, capacity, width)
    recv_x = lax.all_to_all(sent_x.reshape(layout), "expert", 0, 0, tiled=True)
    recv_q = lax.all_to_all(sent_q.reshape(layout), "expert", 0, 0, tiled=True)
    expert_out, grads = expert_math(
        recv_x.reshape(-1, width), recv_q.reshape(-1, width), w_gate[0], w_up[0], w_down[0]
    )
    returned = lax.all_to_all(expert_out.reshape(layout), "expert", 0, 0, tiled=True)
    picked = returned.reshape(-1, width)[target].astype(jnp.float32)
    summed = jnp.sum(picked.reshape(tok_rows, topk, width) * gates[:, :, None], axis=1)
    return summed.astype(jnp.bfloat16), reduce_grads(grads, width)


def exact_pieces(values):
    high = lax.reduce_precision(values, exponent_bits=8, mantissa_bits=7)
    rest = values - high
    middle = lax.reduce_precision(rest, exponent_bits=8, mantissa_bits=7)
    low = rest - middle
    return [part.astype(jnp.bfloat16) for part in (high, middle, low)]


def joined(pieces):
    total = pieces[0].astype(jnp.float32) + pieces[1].astype(jnp.float32)
    return total + pieces[2].astype(jnp.float32)


def gather_replica(values):
    mine = lax.all_gather(values, "ez", axis=0, tiled=True)
    return [mine, lax.ppermute(mine, "core", [(0, 1), (1, 0)])]


def slots_by_rank(routes, experts):
    tok_rows = routes.shape[0]
    onehot = routes[:, :, None] == lax.broadcasted_iota(jnp.int32, (1, 1, experts), 2)
    hits = jnp.any(onehot, axis=1).astype(jnp.bfloat16)
    before = (
        lax.broadcasted_iota(jnp.int32, (tok_rows, tok_rows), 0)
        > lax.broadcasted_iota(jnp.int32, (tok_rows, tok_rows), 1)
    ).astype(jnp.bfloat16)
    rank = jnp.dot(before, hits, preferred_element_type=jnp.float32).astype(jnp.int32)
    return jnp.sum(jnp.where(onehot, rank[:, None, :], 0), axis=2)


def reduce_grads_dp(grad_half, width):
    ndp = lax.axis_size("dp")
    if ndp != 2:
        grads = jnp.concatenate([grad_half(h) for h in range(ndp)], axis=0)
        return reduce_grads(grads, width)
    d = lax.axis_index("dp")
    sent = lax.ppermute(grad_half(1 - d), "dp", [(0, 1), (1, 0)])
    summed = grad_half(d) + sent
    return summed.reshape(1, summed.shape[0], 3, width)


def local_gather(tokens, masked, importance, routes, gates, cotangent, w_gate, w_up, w_down):
    tok_rows = tokens.shape[0]
    width = tokens.shape[1]
    topk = routes.shape[1]
    ncore = lax.axis_size("core")
    nchip = lax.axis_size("ez")
    experts = nchip * ncore
    capacity = min(tok_rows, 3 * tok_rows * topk // (2 * experts))
    core = lax.axis_index("core")
    me = lax.axis_index("ez") * ncore + core
    coef = importance * masked.astype(jnp.float32)
    factor = coef[:, None] * gates
    meta = [routes.astype(jnp.bfloat16)] + exact_pieces(factor) + exact_pieces(gates)
    pad = (-topk * len(meta)) % 128
    meta.append(jnp.zeros((tok_rows, pad), jnp.bfloat16))
    packed = jnp.concatenate([tokens, cotangent] + meta, axis=1)

    halves = gather_replica(packed)
    all_p = jnp.concatenate([h[:, 2 * width:] for h in halves], axis=0)
    cols = [all_p[:, topk * i: topk * (i + 1)] for i in range(7)]
    hit = cols[0].astype(jnp.int32) == me
    zero = jnp.zeros((), jnp.float32)
    fac = jnp.sum(jnp.where(hit, joined(cols[1:4]), zero), axis=1)
    routed = jnp.any(hit, axis=1).reshape(experts, tok_rows)
    ahead = (
        lax.broadcasted_iota(jnp.int32, (tok_rows, tok_rows), 0)
        < lax.broadcasted_iota(jnp.int32, (tok_rows, tok_rows), 1)
    ).astype(jnp.bfloat16)
    rank = jnp.dot(
        routed.astype(jnp.bfloat16), ahead, preferred_element_type=jnp.float32
    ).astype(jnp.int32)
    slot_ids = lax.broadcasted_iota(jnp.int32, (experts, capacity, tok_rows), 1)
    pick = (routed[:, None, :] & (rank[:, None, :] == slot_ids)).astype(jnp.bfloat16)

    def select(part, scale=None):
        picked = []
        for h, half in enumerate(halves):
            values = half[:, part * width:(part + 1) * width]
            if scale is not None:
                rows = slice(h * nchip * tok_rows, (h + 1) * nchip * tok_rows)
                values = (scale[rows, None] * values.astype(jnp.float32)).astype(jnp.bfloat16)
            picked.append(
                jnp.einsum(
                    "sjt,std->sjd",
                    pick[h * nchip:(h + 1) * nchip],
                    values.reshape(nchip, tok_rows, width),
                    preferred_element_type=jnp.float32,
                ).astype(jnp.bfloat16)
            )
        return jnp.concatenate(picked, axis=0).reshape(experts * capacity, width)

    rows_x = select(0)
    rows_q = select(1, fac)
    wgate, wup, wdown = w_gate[0], w_up[0], w_down[0]
    gate_pre = contract_cols(rows_x, wgate)
    up_pre = contract_cols(rows_x, wup)
    sig = jax.nn.sigmoid(gate_pre)
    act = gate_pre * sig
    hidden = (act * up_pre).astype(jnp.bfloat16)
    expert_out = jnp.dot(hidden, wdown, preferred_element_type=jnp.float32).astype(
        jnp.bfloat16
    )

    dense = jnp.einsum(
        "sjt,sjd->std",
        pick,
        expert_out.reshape(experts, capacity, width),
        preferred_element_type=jnp.float32,
    ).astype(jnp.bfloat16)
    own_rows = nchip * tok_rows
    from_partner = lax.ppermute(dense[nchip:], "core", [(0, 1), (1, 0)])
    gate_cols = joined(cols[4:7])[:own_rows]
    routes_own = cols[0][:own_rows].astype(jnp.int32)
    gte = jnp.sum(jnp.where(hit[:own_rows], gate_cols, zero), axis=1)
    gte_partner = jnp.sum(jnp.where(routes_own == (me ^ 1), gate_cols, zero), axis=1)
    combined = (
        gte[:, None] * dense[:nchip].reshape(own_rows, width).astype(jnp.float32)
        + gte_partner[:, None] * from_partner.reshape(own_rows, width).astype(jnp.float32)
    ).astype(jnp.bfloat16)
    returned = lax.all_to_all(
        combined.reshape(nchip, tok_rows, width), "ez", 0, 0, tiled=True
    )

    back = contract_cols(rows_q, wdown)
    d_gate = (back * up_pre * sig * (1.0 + gate_pre * (1.0 - sig))).astype(jnp.bfloat16)
    d_up = (back * act).astype(jnp.bfloat16)
    share = d_gate.shape[1] // lax.axis_size("dp")

    def grad_half(h):
        def part(v):
            return lax.dynamic_slice_in_dim(v, h * share, share, axis=1)

        return jnp.stack(
            [
                contract_rows(part(d_gate), rows_x),
                contract_rows(part(d_up), rows_x),
                contract_rows(part(hidden), rows_q),
            ],
            axis=1,
        )

    weight_grads = reduce_grads_dp(grad_half, width)

    summed = jnp.sum(returned.astype(jnp.float32), axis=0)
    return summed.astype(jnp.bfloat16), weight_grads


def specs(rows, experts):
    return (
        (P(rows, None), P(rows), P(rows), P(rows, None), P(rows, None), P(rows, None))
        + (P(experts, None, None),) * 3,
        (P(rows, None), P(experts, "dp", None, None)),
    )


def solution(mesh):
    ndp, nexp = mesh.shape["dp"], mesh.shape["expert"]
    split = jax.sharding.Mesh(mesh.devices.reshape(ndp, nexp // 2, 2), ("dp", "ez", "core"))
    ins, outs = specs(("dp", "ez", "core"), ("ez", "core"))
    gathered = jax.shard_map(local_gather, mesh=split, in_specs=ins, out_specs=outs, check_vma=False)
    ins, outs = specs(("dp", "expert"), "expert")
    routed = jax.shard_map(local_a2a, mesh=mesh, in_specs=ins, out_specs=outs, check_vma=False)

    def run(*args):
        if args[0].shape[0] // ndp <= GATHER_ROWS:
            return gathered(*args)
        return routed(*args)

    return run
```

```python
import jax
import jax.numpy as jnp
from jax import lax
from jax.sharding import PartitionSpec as P

GATHER_ROWS = 2048


def contract_rows(left, right):
    return lax.dot_general(
        left, right, (((0,), (0,)), ((), ())), preferred_element_type=jnp.float32
    )


def contract_cols(left, right):
    return lax.dot_general(
        left, right, (((1,), (1,)), ((), ())), preferred_element_type=jnp.float32
    )


def expert_math(rows_x, rows_q, wgate, wup, wdown):
    gate_pre = contract_cols(rows_x, wgate)
    up_pre = contract_cols(rows_x, wup)
    sig = jax.nn.sigmoid(gate_pre)
    act = gate_pre * sig
    hidden = (act * up_pre).astype(jnp.bfloat16)
    expert_out = jnp.dot(hidden, wdown, preferred_element_type=jnp.float32).astype(
        jnp.bfloat16
    )
    back = contract_cols(rows_q, wdown)
    d_gate = (back * up_pre * sig * (1.0 + gate_pre * (1.0 - sig))).astype(jnp.bfloat16)
    d_up = (back * act).astype(jnp.bfloat16)
    grad_gate = contract_rows(d_gate, rows_x)
    grad_up = contract_rows(d_up, rows_x)
    grad_down = contract_rows(hidden, rows_q)
    return expert_out, jnp.stack([grad_gate, grad_up, grad_down], axis=1)


def reduce_grads(grads, width):
    share = grads.shape[0] // lax.axis_size("dp")
    summed = lax.psum_scatter(grads, "dp", scatter_dimension=0, tiled=True)
    return summed.reshape(1, share, 3, width)


def source_slots(routes, experts):
    flat = routes.reshape(-1)
    onehot = (flat[:, None] == jnp.arange(experts, dtype=jnp.int32)[None, :]).astype(jnp.int32)
    before = jnp.cumsum(onehot, axis=0) - onehot
    return flat, jnp.sum(before * onehot, axis=1)


def local_a2a(tokens, masked, importance, routes, gates, cotangent, w_gate, w_up, w_down):
    tok_rows = tokens.shape[0]
    width = tokens.shape[1]
    topk = routes.shape[1]
    experts = lax.axis_size("expert")
    capacity = min(tok_rows, 3 * tok_rows * topk // (2 * experts))
    flat, slots = source_slots(routes, experts)
    target = flat * capacity + slots
    owner = jnp.arange(tok_rows * topk, dtype=jnp.int32) // topk
    coef = importance * masked.astype(jnp.float32)
    factor = (coef[:, None] * gates).reshape(-1)
    sent_x = jnp.zeros((experts * capacity, width), jnp.bfloat16).at[target].set(tokens[owner])
    scaled = (factor[:, None] * cotangent[owner].astype(jnp.float32)).astype(jnp.bfloat16)
    sent_q = jnp.zeros((experts * capacity, width), jnp.bfloat16).at[target].set(scaled)
    layout = (experts, capacity, width)
    recv_x = lax.all_to_all(sent_x.reshape(layout), "expert", 0, 0, tiled=True)
    recv_q = lax.all_to_all(sent_q.reshape(layout), "expert", 0, 0, tiled=True)
    expert_out, grads = expert_math(
        recv_x.reshape(-1, width), recv_q.reshape(-1, width), w_gate[0], w_up[0], w_down[0]
    )
    returned = lax.all_to_all(expert_out.reshape(layout), "expert", 0, 0, tiled=True)
    picked = returned.reshape(-1, width)[target].astype(jnp.float32)
    summed = jnp.sum(picked.reshape(tok_rows, topk, width) * gates[:, :, None], axis=1)
    return summed.astype(jnp.bfloat16), reduce_grads(grads, width)


def exact_pieces(values):
    high = lax.reduce_precision(values, exponent_bits=8, mantissa_bits=7)
    rest = values - high
    middle = lax.reduce_precision(rest, exponent_bits=8, mantissa_bits=7)
    low = rest - middle
    return [part.astype(jnp.bfloat16) for part in (high, middle, low)]


def joined(pieces):
    total = pieces[0].astype(jnp.float32) + pieces[1].astype(jnp.float32)
    return total + pieces[2].astype(jnp.float32)


def gather_replica(values):
    mine = lax.all_gather(values, "ez", axis=0, tiled=True)
    return [mine, lax.ppermute(mine, "core", [(0, 1), (1, 0)])]


def slots_by_rank(routes, experts):
    tok_rows = routes.shape[0]
    onehot = routes[:, :, None] == lax.broadcasted_iota(jnp.int32, (1, 1, experts), 2)
    hits = jnp.any(onehot, axis=1).astype(jnp.bfloat16)
    before = (
        lax.broadcasted_iota(jnp.int32, (tok_rows, tok_rows), 0)
        > lax.broadcasted_iota(jnp.int32, (tok_rows, tok_rows), 1)
    ).astype(jnp.bfloat16)
    rank = jnp.dot(before, hits, preferred_element_type=jnp.float32).astype(jnp.int32)
    return jnp.sum(jnp.where(onehot, rank[:, None, :], 0), axis=2)


def reduce_grads_dp(grad_half, width):
    ndp = lax.axis_size("dp")
    if ndp != 2:
        grads = jnp.concatenate([grad_half(h) for h in range(ndp)], axis=0)
        return reduce_grads(grads, width)
    d = lax.axis_index("dp")
    sent = lax.ppermute(grad_half(1 - d).astype(jnp.bfloat16), "dp", [(0, 1), (1, 0)])
    summed = grad_half(d) + sent.astype(jnp.float32)
    return summed.reshape(1, summed.shape[0], 3, width)


def local_gather(tokens, masked, importance, routes, gates, cotangent, w_gate, w_up, w_down):
    tok_rows = tokens.shape[0]
    width = tokens.shape[1]
    topk = routes.shape[1]
    ncore = lax.axis_size("core")
    nchip = lax.axis_size("ez")
    experts = nchip * ncore
    capacity = min(tok_rows, 3 * tok_rows * topk // (2 * experts))
    core = lax.axis_index("core")
    me = lax.axis_index("ez") * ncore + core
    coef = importance * masked.astype(jnp.float32)
    factor = coef[:, None] * gates
    meta = [routes.astype(jnp.bfloat16)] + exact_pieces(factor) + exact_pieces(gates)
    pad = (-topk * len(meta)) % 128
    meta.append(jnp.zeros((tok_rows, pad), jnp.bfloat16))
    packed = jnp.concatenate([tokens, cotangent] + meta, axis=1)

    halves = gather_replica(packed)
    all_p = jnp.concatenate([h[:, 2 * width:] for h in halves], axis=0)
    cols = [all_p[:, topk * i: topk * (i + 1)] for i in range(7)]
    hit = cols[0].astype(jnp.int32) == me
    zero = jnp.zeros((), jnp.float32)
    fac = jnp.sum(jnp.where(hit, joined(cols[1:4]), zero), axis=1)
    routed = jnp.any(hit, axis=1).reshape(experts, tok_rows)
    ahead = (
        lax.broadcasted_iota(jnp.int32, (tok_rows, tok_rows), 0)
        < lax.broadcasted_iota(jnp.int32, (tok_rows, tok_rows), 1)
    ).astype(jnp.bfloat16)
    rank = jnp.dot(
        routed.astype(jnp.bfloat16), ahead, preferred_element_type=jnp.float32
    ).astype(jnp.int32)
    slot_ids = lax.broadcasted_iota(jnp.int32, (experts, capacity, tok_rows), 1)
    pick = (routed[:, None, :] & (rank[:, None, :] == slot_ids)).astype(jnp.bfloat16)

    def select(part, scale=None):
        picked = []
        for h, half in enumerate(halves):
            values = half[:, part * width:(part + 1) * width]
            if scale is not None:
                rows = slice(h * nchip * tok_rows, (h + 1) * nchip * tok_rows)
                values = (scale[rows, None] * values.astype(jnp.float32)).astype(jnp.bfloat16)
            picked.append(
                jnp.einsum(
                    "sjt,std->sjd",
                    pick[h * nchip:(h + 1) * nchip],
                    values.reshape(nchip, tok_rows, width),
                    preferred_element_type=jnp.float32,
                ).astype(jnp.bfloat16)
            )
        return jnp.concatenate(picked, axis=0).reshape(experts * capacity, width)

    rows_x = select(0)
    rows_q = select(1, fac)
    wgate, wup, wdown = w_gate[0], w_up[0], w_down[0]
    gate_pre = contract_cols(rows_x, wgate)
    up_pre = contract_cols(rows_x, wup)
    sig = jax.nn.sigmoid(gate_pre)
    act = gate_pre * sig
    hidden = (act * up_pre).astype(jnp.bfloat16)
    expert_out = jnp.dot(hidden, wdown, preferred_element_type=jnp.float32).astype(
        jnp.bfloat16
    )

    by_group = expert_out.reshape(ncore, nchip, capacity, width)
    ordered = jnp.stack(
        [lax.dynamic_index_in_dim(by_group, k ^ core, 0, keepdims=False) for k in range(ncore)],
        axis=1,
    ).reshape(experts, capacity, width)
    returned = lax.all_to_all(ordered, ("ez", "core"), 0, 0, tiled=True)

    back = contract_cols(rows_q, wdown)
    d_gate = (back * up_pre * sig * (1.0 + gate_pre * (1.0 - sig))).astype(jnp.bfloat16)
    d_up = (back * act).astype(jnp.bfloat16)
    share = d_gate.shape[1] // lax.axis_size("dp")

    def grad_half(h):
        def part(v):
            return lax.dynamic_slice_in_dim(v, h * share, share, axis=1)

        return jnp.stack(
            [
                contract_rows(part(d_gate), rows_x),
                contract_rows(part(d_up), rows_x),
                contract_rows(part(hidden), rows_q),
            ],
            axis=1,
        )

    weight_grads = reduce_grads_dp(grad_half, width)

    target = (routes * capacity + slots_by_rank(routes, experts)).reshape(-1)
    choose = (
        target[:, None]
        == lax.broadcasted_iota(jnp.int32, (tok_rows * topk, experts * capacity), 1)
    ).astype(jnp.bfloat16)
    picked = jnp.dot(choose, returned.reshape(-1, width), preferred_element_type=jnp.float32)
    summed = jnp.sum(picked.reshape(tok_rows, topk, width) * gates[:, :, None], axis=1)
    return summed.astype(jnp.bfloat16), weight_grads


def specs(rows, experts):
    return (
        (P(rows, None), P(rows), P(rows), P(rows, None), P(rows, None), P(rows, None))
        + (P(experts, None, None),) * 3,
        (P(rows, None), P(experts, "dp", None, None)),
    )


def solution(mesh):
    ndp, nexp = mesh.shape["dp"], mesh.shape["expert"]
    split = jax.sharding.Mesh(mesh.devices.reshape(ndp, nexp // 2, 2), ("dp", "ez", "core"))
    ins, outs = specs(("dp", "ez", "core"), ("ez", "core"))
    gathered = jax.shard_map(local_gather, mesh=split, in_specs=ins, out_specs=outs, check_vma=False)
    ins, outs = specs(("dp", "expert"), "expert")
    routed = jax.shard_map(local_a2a, mesh=mesh, in_specs=ins, out_specs=outs, check_vma=False)

    def run(*args):
        if args[0].shape[0] // ndp <= GATHER_ROWS:
            return gathered(*args)
        return routed(*args)

    return run
```

```python
import jax
import jax.numpy as jnp
from jax import lax
from jax.sharding import PartitionSpec as P

GATHER_ROWS = 2048


def contract_rows(left, right):
    return lax.dot_general(
        left, right, (((0,), (0,)), ((), ())), preferred_element_type=jnp.float32
    )


def contract_cols(left, right):
    return lax.dot_general(
        left, right, (((1,), (1,)), ((), ())), preferred_element_type=jnp.float32
    )


def expert_math(rows_x, rows_q, wgate, wup, wdown):
    gate_pre = contract_cols(rows_x, wgate)
    up_pre = contract_cols(rows_x, wup)
    sig = jax.nn.sigmoid(gate_pre)
    act = gate_pre * sig
    hidden = (act * up_pre).astype(jnp.bfloat16)
    expert_out = jnp.dot(hidden, wdown, preferred_element_type=jnp.float32).astype(
        jnp.bfloat16
    )
    back = contract_cols(rows_q, wdown)
    d_gate = (back * up_pre * sig * (1.0 + gate_pre * (1.0 - sig))).astype(jnp.bfloat16)
    d_up = (back * act).astype(jnp.bfloat16)
    grad_gate = contract_rows(d_gate, rows_x)
    grad_up = contract_rows(d_up, rows_x)
    grad_down = contract_rows(hidden, rows_q)
    return expert_out, jnp.stack([grad_gate, grad_up, grad_down], axis=1)


def reduce_grads(grads, width):
    share = grads.shape[0] // lax.axis_size("dp")
    summed = lax.psum_scatter(grads, "dp", scatter_dimension=0, tiled=True)
    return summed.reshape(1, share, 3, width)


def source_slots(routes, experts):
    flat = routes.reshape(-1)
    onehot = (flat[:, None] == jnp.arange(experts, dtype=jnp.int32)[None, :]).astype(jnp.int32)
    before = jnp.cumsum(onehot, axis=0) - onehot
    return flat, jnp.sum(before * onehot, axis=1)


def local_a2a(tokens, masked, importance, routes, gates, cotangent, w_gate, w_up, w_down):
    tok_rows = tokens.shape[0]
    width = tokens.shape[1]
    topk = routes.shape[1]
    experts = lax.axis_size("expert")
    capacity = min(tok_rows, 3 * tok_rows * topk // (2 * experts))
    flat, slots = source_slots(routes, experts)
    target = flat * capacity + slots
    owner = jnp.arange(tok_rows * topk, dtype=jnp.int32) // topk
    coef = importance * masked.astype(jnp.float32)
    factor = (coef[:, None] * gates).reshape(-1)
    sent_x = jnp.zeros((experts * capacity, width), jnp.bfloat16).at[target].set(tokens[owner])
    scaled = (factor[:, None] * cotangent[owner].astype(jnp.float32)).astype(jnp.bfloat16)
    sent_q = jnp.zeros((experts * capacity, width), jnp.bfloat16).at[target].set(scaled)
    layout = (experts, capacity, width)
    recv_x = lax.all_to_all(sent_x.reshape(layout), "expert", 0, 0, tiled=True)
    recv_q = lax.all_to_all(sent_q.reshape(layout), "expert", 0, 0, tiled=True)
    expert_out, grads = expert_math(
        recv_x.reshape(-1, width), recv_q.reshape(-1, width), w_gate[0], w_up[0], w_down[0]
    )
    returned = lax.all_to_all(expert_out.reshape(layout), "expert", 0, 0, tiled=True)
    picked = returned.reshape(-1, width)[target].astype(jnp.float32)
    summed = jnp.sum(picked.reshape(tok_rows, topk, width) * gates[:, :, None], axis=1)
    return summed.astype(jnp.bfloat16), reduce_grads(grads, width)


def exact_pieces(values):
    high = lax.reduce_precision(values, exponent_bits=8, mantissa_bits=7)
    rest = values - high
    middle = lax.reduce_precision(rest, exponent_bits=8, mantissa_bits=7)
    low = rest - middle
    return [part.astype(jnp.bfloat16) for part in (high, middle, low)]


def joined(pieces):
    total = pieces[0].astype(jnp.float32) + pieces[1].astype(jnp.float32)
    return total + pieces[2].astype(jnp.float32)


def gather_replica(values):
    mine = lax.all_gather(values, "ez", axis=0, tiled=True)
    return [mine, lax.ppermute(mine, "core", [(0, 1), (1, 0)])]


def ring_gather(block):
    n = lax.axis_size("ez")
    order = [2 * i for i in range(n // 2)] + [2 * i + 1 for i in reversed(range(n // 2))]
    if n % 2:
        order = list(range(n))
    place = [0] * n
    for p, c in enumerate(order):
        place[c] = p
    me = lax.axis_index("ez")
    at = jnp.asarray(place, jnp.int32)[me]
    ring = jnp.asarray(order, jnp.int32)
    out = jnp.zeros((n,) + block.shape, block.dtype)
    out = lax.dynamic_update_index_in_dim(out, block, me, 0)
    ahead = [(order[i], order[(i + 1) % n]) for i in range(n)]
    behind = [(order[i], order[(i - 1) % n]) for i in range(n)]
    up, down = block, block
    for step in range(1, n // 2 + 1):
        up = lax.ppermute(up, "ez", ahead)
        out = lax.dynamic_update_index_in_dim(out, up, ring[(at - step) % n], 0)
        if step <= (n - 1) // 2:
            down = lax.ppermute(down, "ez", behind)
            out = lax.dynamic_update_index_in_dim(out, down, ring[(at + step) % n], 0)
    mine = out.reshape((n * block.shape[0],) + block.shape[1:])
    return [mine, lax.ppermute(mine, "core", [(0, 1), (1, 0)])]


def slots_by_rank(routes, experts):
    tok_rows = routes.shape[0]
    onehot = routes[:, :, None] == lax.broadcasted_iota(jnp.int32, (1, 1, experts), 2)
    hits = jnp.any(onehot, axis=1).astype(jnp.bfloat16)
    before = (
        lax.broadcasted_iota(jnp.int32, (tok_rows, tok_rows), 0)
        > lax.broadcasted_iota(jnp.int32, (tok_rows, tok_rows), 1)
    ).astype(jnp.bfloat16)
    rank = jnp.dot(before, hits, preferred_element_type=jnp.float32).astype(jnp.int32)
    return jnp.sum(jnp.where(onehot, rank[:, None, :], 0), axis=2)


def reduce_grads_dp(grad_half, width):
    ndp = lax.axis_size("dp")
    if ndp != 2:
        grads = jnp.concatenate([grad_half(h) for h in range(ndp)], axis=0)
        return reduce_grads(grads, width)
    d = lax.axis_index("dp")
    sent = lax.ppermute(grad_half(1 - d).astype(jnp.bfloat16), "dp", [(0, 1), (1, 0)])
    summed = grad_half(d) + sent.astype(jnp.float32)
    return summed.reshape(1, summed.shape[0], 3, width)


def local_gather(tokens, masked, importance, routes, gates, cotangent, w_gate, w_up, w_down):
    tok_rows = tokens.shape[0]
    width = tokens.shape[1]
    topk = routes.shape[1]
    ncore = lax.axis_size("core")
    nchip = lax.axis_size("ez")
    experts = nchip * ncore
    capacity = min(tok_rows, 3 * tok_rows * topk // (2 * experts))
    core = lax.axis_index("core")
    me = lax.axis_index("ez") * ncore + core
    coef = importance * masked.astype(jnp.float32)
    factor = coef[:, None] * gates
    meta = [routes.astype(jnp.bfloat16)] + exact_pieces(factor) + exact_pieces(gates)
    pad = (-topk * len(meta)) % 128
    meta.append(jnp.zeros((tok_rows, pad), jnp.bfloat16))
    packed = jnp.concatenate([tokens] + meta, axis=1)

    halves = gather_replica(packed)
    cot_halves = ring_gather(cotangent)
    all_p = jnp.concatenate([h[:, width:] for h in halves], axis=0)
    cols = [all_p[:, topk * i: topk * (i + 1)] for i in range(7)]
    hit = cols[0].astype(jnp.int32) == me
    zero = jnp.zeros((), jnp.float32)
    fac = jnp.sum(jnp.where(hit, joined(cols[1:4]), zero), axis=1)
    routed = jnp.any(hit, axis=1).reshape(experts, tok_rows)
    ahead = (
        lax.broadcasted_iota(jnp.int32, (tok_rows, tok_rows), 0)
        < lax.broadcasted_iota(jnp.int32, (tok_rows, tok_rows), 1)
    ).astype(jnp.bfloat16)
    rank = jnp.dot(
        routed.astype(jnp.bfloat16), ahead, preferred_element_type=jnp.float32
    ).astype(jnp.int32)
    slot_ids = lax.broadcasted_iota(jnp.int32, (experts, capacity, tok_rows), 1)
    pick = (routed[:, None, :] & (rank[:, None, :] == slot_ids)).astype(jnp.bfloat16)

    def select(part, scale=None):
        picked = []
        for h, half in enumerate(halves if part == 0 else cot_halves):
            values = half[:, :width]
            if scale is not None:
                rows = slice(h * nchip * tok_rows, (h + 1) * nchip * tok_rows)
                values = (scale[rows, None] * values.astype(jnp.float32)).astype(jnp.bfloat16)
            picked.append(
                jnp.einsum(
                    "sjt,std->sjd",
                    pick[h * nchip:(h + 1) * nchip],
                    values.reshape(nchip, tok_rows, width),
                    preferred_element_type=jnp.float32,
                ).astype(jnp.bfloat16)
            )
        return jnp.concatenate(picked, axis=0).reshape(experts * capacity, width)

    rows_x = select(0)
    rows_q = select(1, fac)
    wgate, wup, wdown = w_gate[0], w_up[0], w_down[0]
    gate_pre = contract_cols(rows_x, wgate)
    up_pre = contract_cols(rows_x, wup)
    sig = jax.nn.sigmoid(gate_pre)
    act = gate_pre * sig
    hidden = (act * up_pre).astype(jnp.bfloat16)
    expert_out = jnp.dot(hidden, wdown, preferred_element_type=jnp.float32).astype(
        jnp.bfloat16
    )

    by_group = expert_out.reshape(ncore, nchip, capacity, width)
    ordered = jnp.stack(
        [lax.dynamic_index_in_dim(by_group, k ^ core, 0, keepdims=False) for k in range(ncore)],
        axis=1,
    ).reshape(experts, capacity, width)
    returned = lax.all_to_all(ordered, ("ez", "core"), 0, 0, tiled=True)

    back = contract_cols(rows_q, wdown)
    d_gate = (back * up_pre * sig * (1.0 + gate_pre * (1.0 - sig))).astype(jnp.bfloat16)
    d_up = (back * act).astype(jnp.bfloat16)
    share = d_gate.shape[1] // lax.axis_size("dp")

    def grad_half(h):
        def part(v):
            return lax.dynamic_slice_in_dim(v, h * share, share, axis=1)

        return jnp.stack(
            [
                contract_rows(part(d_gate), rows_x),
                contract_rows(part(d_up), rows_x),
                contract_rows(part(hidden), rows_q),
            ],
            axis=1,
        )

    weight_grads = reduce_grads_dp(grad_half, width)

    target = (routes * capacity + slots_by_rank(routes, experts)).reshape(-1)
    choose = (
        target[:, None]
        == lax.broadcasted_iota(jnp.int32, (tok_rows * topk, experts * capacity), 1)
    ).astype(jnp.bfloat16)
    picked = jnp.dot(choose, returned.reshape(-1, width), preferred_element_type=jnp.float32)
    summed = jnp.sum(picked.reshape(tok_rows, topk, width) * gates[:, :, None], axis=1)
    return summed.astype(jnp.bfloat16), weight_grads


def specs(rows, experts):
    return (
        (P(rows, None), P(rows), P(rows), P(rows, None), P(rows, None), P(rows, None))
        + (P(experts, None, None),) * 3,
        (P(rows, None), P(experts, "dp", None, None)),
    )


def solution(mesh):
    ndp, nexp = mesh.shape["dp"], mesh.shape["expert"]
    split = jax.sharding.Mesh(mesh.devices.reshape(ndp, nexp // 2, 2), ("dp", "ez", "core"))
    ins, outs = specs(("dp", "ez", "core"), ("ez", "core"))
    gathered = jax.shard_map(local_gather, mesh=split, in_specs=ins, out_specs=outs, check_vma=False)
    ins, outs = specs(("dp", "expert"), "expert")
    routed = jax.shard_map(local_a2a, mesh=mesh, in_specs=ins, out_specs=outs, check_vma=False)

    def run(*args):
        if args[0].shape[0] // ndp <= GATHER_ROWS:
            return gathered(*args)
        return routed(*args)

    return run
```

```python
import jax
import jax.numpy as jnp
from jax import lax
from jax.sharding import PartitionSpec as P

GATHER_ROWS = 2048


def contract_rows(left, right):
    return lax.dot_general(
        left, right, (((0,), (0,)), ((), ())), preferred_element_type=jnp.float32
    )


def contract_cols(left, right):
    return lax.dot_general(
        left, right, (((1,), (1,)), ((), ())), preferred_element_type=jnp.float32
    )


def expert_math(rows_x, rows_q, wgate, wup, wdown):
    gate_pre = contract_cols(rows_x, wgate)
    up_pre = contract_cols(rows_x, wup)
    sig = jax.nn.sigmoid(gate_pre)
    act = gate_pre * sig
    hidden = (act * up_pre).astype(jnp.bfloat16)
    expert_out = jnp.dot(hidden, wdown, preferred_element_type=jnp.float32).astype(
        jnp.bfloat16
    )
    back = contract_cols(rows_q, wdown)
    d_gate = (back * up_pre * sig * (1.0 + gate_pre * (1.0 - sig))).astype(jnp.bfloat16)
    d_up = (back * act).astype(jnp.bfloat16)
    grad_gate = contract_rows(d_gate, rows_x)
    grad_up = contract_rows(d_up, rows_x)
    grad_down = contract_rows(hidden, rows_q)
    return expert_out, jnp.stack([grad_gate, grad_up, grad_down], axis=1)


def reduce_grads(grads, width):
    share = grads.shape[0] // lax.axis_size("dp")
    summed = lax.psum_scatter(grads, "dp", scatter_dimension=0, tiled=True)
    return summed.reshape(1, share, 3, width)


def source_slots(routes, experts):
    flat = routes.reshape(-1)
    onehot = (flat[:, None] == jnp.arange(experts, dtype=jnp.int32)[None, :]).astype(jnp.int32)
    before = jnp.cumsum(onehot, axis=0) - onehot
    return flat, jnp.sum(before * onehot, axis=1)


def local_a2a(tokens, masked, importance, routes, gates, cotangent, w_gate, w_up, w_down):
    tok_rows = tokens.shape[0]
    width = tokens.shape[1]
    topk = routes.shape[1]
    experts = lax.axis_size("expert")
    capacity = min(tok_rows, 3 * tok_rows * topk // (2 * experts))
    flat, slots = source_slots(routes, experts)
    target = flat * capacity + slots
    owner = jnp.arange(tok_rows * topk, dtype=jnp.int32) // topk
    coef = importance * masked.astype(jnp.float32)
    factor = (coef[:, None] * gates).reshape(-1)
    sent_x = jnp.zeros((experts * capacity, width), jnp.bfloat16).at[target].set(tokens[owner])
    scaled = (factor[:, None] * cotangent[owner].astype(jnp.float32)).astype(jnp.bfloat16)
    sent_q = jnp.zeros((experts * capacity, width), jnp.bfloat16).at[target].set(scaled)
    layout = (experts, capacity, width)
    recv_x = lax.all_to_all(sent_x.reshape(layout), "expert", 0, 0, tiled=True)
    recv_q = lax.all_to_all(sent_q.reshape(layout), "expert", 0, 0, tiled=True)
    expert_out, grads = expert_math(
        recv_x.reshape(-1, width), recv_q.reshape(-1, width), w_gate[0], w_up[0], w_down[0]
    )
    returned = lax.all_to_all(expert_out.reshape(layout), "expert", 0, 0, tiled=True)
    picked = returned.reshape(-1, width)[target].astype(jnp.float32)
    summed = jnp.sum(picked.reshape(tok_rows, topk, width) * gates[:, :, None], axis=1)
    return summed.astype(jnp.bfloat16), reduce_grads(grads, width)


def exact_pieces(values):
    high = lax.reduce_precision(values, exponent_bits=8, mantissa_bits=7)
    rest = values - high
    middle = lax.reduce_precision(rest, exponent_bits=8, mantissa_bits=7)
    low = rest - middle
    return [part.astype(jnp.bfloat16) for part in (high, middle, low)]


def joined(pieces):
    total = pieces[0].astype(jnp.float32) + pieces[1].astype(jnp.float32)
    return total + pieces[2].astype(jnp.float32)


def gather_replica(values):
    mine = lax.all_gather(values, "ez", axis=0, tiled=True)
    return [mine, lax.ppermute(mine, "core", [(0, 1), (1, 0)])]


def ring_gather(block):
    n = lax.axis_size("ez")
    order = [2 * i for i in range(n // 2)] + [2 * i + 1 for i in reversed(range(n // 2))]
    if n % 2:
        order = list(range(n))
    place = [0] * n
    for p, c in enumerate(order):
        place[c] = p
    me = lax.axis_index("ez")
    at = jnp.asarray(place, jnp.int32)[me]
    ring = jnp.asarray(order, jnp.int32)
    out = jnp.zeros((n,) + block.shape, block.dtype)
    out = lax.dynamic_update_index_in_dim(out, block, me, 0)
    ahead = [(order[i], order[(i + 1) % n]) for i in range(n)]
    behind = [(order[i], order[(i - 1) % n]) for i in range(n)]
    up, down = block, block
    for step in range(1, n // 2 + 1):
        up = lax.ppermute(up, "ez", ahead)
        out = lax.dynamic_update_index_in_dim(out, up, ring[(at - step) % n], 0)
        if step <= (n - 1) // 2:
            down = lax.ppermute(down, "ez", behind)
            out = lax.dynamic_update_index_in_dim(out, down, ring[(at + step) % n], 0)
    mine = out.reshape((n * block.shape[0],) + block.shape[1:])
    return [mine, lax.ppermute(mine, "core", [(0, 1), (1, 0)])]


def slots_by_rank(routes, experts):
    tok_rows = routes.shape[0]
    onehot = routes[:, :, None] == lax.broadcasted_iota(jnp.int32, (1, 1, experts), 2)
    hits = jnp.any(onehot, axis=1).astype(jnp.bfloat16)
    before = (
        lax.broadcasted_iota(jnp.int32, (tok_rows, tok_rows), 0)
        > lax.broadcasted_iota(jnp.int32, (tok_rows, tok_rows), 1)
    ).astype(jnp.bfloat16)
    rank = jnp.dot(before, hits, preferred_element_type=jnp.float32).astype(jnp.int32)
    return jnp.sum(jnp.where(onehot, rank[:, None, :], 0), axis=2)


def reduce_grads_dp(grad_half, width):
    ndp = lax.axis_size("dp")
    if ndp != 2:
        grads = jnp.concatenate([grad_half(h) for h in range(ndp)], axis=0)
        return reduce_grads(grads, width)
    d = lax.axis_index("dp")
    sent = lax.ppermute(grad_half(1 - d).astype(jnp.bfloat16), "dp", [(0, 1), (1, 0)])
    summed = grad_half(d) + sent.astype(jnp.float32)
    return summed.reshape(1, summed.shape[0], 3, width)


def local_gather(tokens, masked, importance, routes, gates, cotangent, w_gate, w_up, w_down):
    tok_rows = tokens.shape[0]
    width = tokens.shape[1]
    topk = routes.shape[1]
    ncore = lax.axis_size("core")
    nchip = lax.axis_size("ez")
    experts = nchip * ncore
    capacity = min(tok_rows, 3 * tok_rows * topk // (2 * experts))
    core = lax.axis_index("core")
    me = lax.axis_index("ez") * ncore + core
    coef = importance * masked.astype(jnp.float32)
    factor = coef[:, None] * gates
    meta = [routes.astype(jnp.bfloat16)] + exact_pieces(factor) + exact_pieces(gates)
    pad = (-topk * len(meta)) % 128
    meta.append(jnp.zeros((tok_rows, pad), jnp.bfloat16))
    packed = jnp.concatenate([tokens] + meta, axis=1)

    halves = gather_replica(packed)
    cot_halves = ring_gather(cotangent)
    all_p = jnp.concatenate([h[:, width:] for h in halves], axis=0)
    cols = [all_p[:, topk * i: topk * (i + 1)] for i in range(7)]
    hit = cols[0].astype(jnp.int32) == me
    zero = jnp.zeros((), jnp.float32)
    fac = jnp.sum(jnp.where(hit, joined(cols[1:4]), zero), axis=1)
    routed = jnp.any(hit, axis=1).reshape(experts, tok_rows)
    ahead = (
        lax.broadcasted_iota(jnp.int32, (tok_rows, tok_rows), 0)
        < lax.broadcasted_iota(jnp.int32, (tok_rows, tok_rows), 1)
    ).astype(jnp.bfloat16)
    rank = jnp.dot(
        routed.astype(jnp.bfloat16), ahead, preferred_element_type=jnp.float32
    ).astype(jnp.int32)
    slot_ids = lax.broadcasted_iota(jnp.int32, (experts, capacity, tok_rows), 1)
    pick = (routed[:, None, :] & (rank[:, None, :] == slot_ids)).astype(jnp.bfloat16)

    def select(part, scale=None):
        picked = []
        for h, half in enumerate(halves if part == 0 else cot_halves):
            values = half[:, :width]
            if scale is not None:
                rows = slice(h * nchip * tok_rows, (h + 1) * nchip * tok_rows)
                values = (scale[rows, None] * values.astype(jnp.float32)).astype(jnp.bfloat16)
            picked.append(
                jnp.einsum(
                    "sjt,std->sjd",
                    pick[h * nchip:(h + 1) * nchip],
                    values.reshape(nchip, tok_rows, width),
                    preferred_element_type=jnp.float32,
                ).astype(jnp.bfloat16)
            )
        return jnp.concatenate(picked, axis=0).reshape(experts * capacity, width)

    rows_x = select(0)
    rows_q = select(1, fac)
    wgate, wup, wdown = w_gate[0], w_up[0], w_down[0]
    gate_pre = contract_cols(rows_x, wgate)
    up_pre = contract_cols(rows_x, wup)
    sig = jax.nn.sigmoid(gate_pre)
    act = gate_pre * sig
    hidden = (act * up_pre).astype(jnp.bfloat16)
    expert_out = jnp.dot(hidden, wdown, preferred_element_type=jnp.float32).astype(
        jnp.bfloat16
    )

    by_group = expert_out.reshape(ncore, nchip, capacity, width)
    ordered = jnp.stack(
        [lax.dynamic_index_in_dim(by_group, k ^ core, 0, keepdims=False) for k in range(ncore)],
        axis=1,
    ).reshape(experts, capacity, width)
    returned = lax.all_to_all(ordered, ("ez", "core"), 0, 0, tiled=True)

    back = contract_cols(rows_q, wdown)
    d_gate = (back * up_pre * sig * (1.0 + gate_pre * (1.0 - sig))).astype(jnp.bfloat16)
    d_up = (back * act).astype(jnp.bfloat16)
    share = d_gate.shape[1] // lax.axis_size("dp")

    def grad_half(h):
        def part(v):
            return lax.dynamic_slice_in_dim(v, h * share, share, axis=1)

        return jnp.stack(
            [
                contract_rows(part(d_gate), rows_x),
                contract_rows(part(d_up), rows_x),
                contract_rows(part(hidden), rows_q),
            ],
            axis=1,
        )

    weight_grads = reduce_grads_dp(grad_half, width)

    target = routes * capacity + slots_by_rank(routes, experts)
    match = target[:, :, None] == lax.broadcasted_iota(
        jnp.int32, (1, 1, experts * capacity), 2
    )
    flat_back = returned.reshape(-1, width)
    parts = []
    for piece in exact_pieces(gates):
        weights = jnp.sum(
            jnp.where(match, piece.astype(jnp.float32)[:, :, None], zero), axis=1
        ).astype(jnp.bfloat16)
        parts.append(jnp.dot(weights, flat_back, preferred_element_type=jnp.float32))
    summed = (parts[0] + parts[1]) + parts[2]
    return summed.astype(jnp.bfloat16), weight_grads


def specs(rows, experts):
    return (
        (P(rows, None), P(rows), P(rows), P(rows, None), P(rows, None), P(rows, None))
        + (P(experts, None, None),) * 3,
        (P(rows, None), P(experts, "dp", None, None)),
    )


def solution(mesh):
    ndp, nexp = mesh.shape["dp"], mesh.shape["expert"]
    split = jax.sharding.Mesh(mesh.devices.reshape(ndp, nexp // 2, 2), ("dp", "ez", "core"))
    ins, outs = specs(("dp", "ez", "core"), ("ez", "core"))
    gathered = jax.shard_map(local_gather, mesh=split, in_specs=ins, out_specs=outs, check_vma=False)
    ins, outs = specs(("dp", "expert"), "expert")
    routed = jax.shard_map(local_a2a, mesh=mesh, in_specs=ins, out_specs=outs, check_vma=False)

    def run(*args):
        if args[0].shape[0] // ndp <= GATHER_ROWS:
            return gathered(*args)
        return routed(*args)

    return run
```

```python
import jax
import jax.numpy as jnp
from jax import lax
from jax.sharding import PartitionSpec as P

GATHER_ROWS = 2048


def contract_rows(left, right):
    return lax.dot_general(
        left, right, (((0,), (0,)), ((), ())), preferred_element_type=jnp.float32
    )


def contract_cols(left, right):
    return lax.dot_general(
        left, right, (((1,), (1,)), ((), ())), preferred_element_type=jnp.float32
    )


def expert_math(rows_x, rows_q, wgate, wup, wdown):
    gate_pre = contract_cols(rows_x, wgate)
    up_pre = contract_cols(rows_x, wup)
    sig = jax.nn.sigmoid(gate_pre)
    act = gate_pre * sig
    hidden = (act * up_pre).astype(jnp.bfloat16)
    expert_out = jnp.dot(hidden, wdown, preferred_element_type=jnp.float32).astype(
        jnp.bfloat16
    )
    back = contract_cols(rows_q, wdown)
    d_gate = (back * up_pre * sig * (1.0 + gate_pre * (1.0 - sig))).astype(jnp.bfloat16)
    d_up = (back * act).astype(jnp.bfloat16)
    grad_gate = contract_rows(d_gate, rows_x)
    grad_up = contract_rows(d_up, rows_x)
    grad_down = contract_rows(hidden, rows_q)
    return expert_out, jnp.stack([grad_gate, grad_up, grad_down], axis=1)


def reduce_grads(grads, width):
    share = grads.shape[0] // lax.axis_size("dp")
    summed = lax.psum_scatter(grads, "dp", scatter_dimension=0, tiled=True)
    return summed.reshape(1, share, 3, width)


def source_slots(routes, experts):
    flat = routes.reshape(-1)
    onehot = (flat[:, None] == jnp.arange(experts, dtype=jnp.int32)[None, :]).astype(jnp.int32)
    before = jnp.cumsum(onehot, axis=0) - onehot
    return flat, jnp.sum(before * onehot, axis=1)


def local_a2a(tokens, masked, importance, routes, gates, cotangent, w_gate, w_up, w_down):
    tok_rows = tokens.shape[0]
    width = tokens.shape[1]
    topk = routes.shape[1]
    experts = lax.axis_size("expert")
    capacity = min(tok_rows, 3 * tok_rows * topk // (2 * experts))
    flat, slots = source_slots(routes, experts)
    target = flat * capacity + slots
    owner = jnp.arange(tok_rows * topk, dtype=jnp.int32) // topk
    coef = importance * masked.astype(jnp.float32)
    factor = (coef[:, None] * gates).reshape(-1)
    sent_x = jnp.zeros((experts * capacity, width), jnp.bfloat16).at[target].set(tokens[owner])
    scaled = (factor[:, None] * cotangent[owner].astype(jnp.float32)).astype(jnp.bfloat16)
    sent_q = jnp.zeros((experts * capacity, width), jnp.bfloat16).at[target].set(scaled)
    layout = (experts, capacity, width)
    recv_x = lax.all_to_all(sent_x.reshape(layout), "expert", 0, 0, tiled=True)
    recv_q = lax.all_to_all(sent_q.reshape(layout), "expert", 0, 0, tiled=True)
    expert_out, grads = expert_math(
        recv_x.reshape(-1, width), recv_q.reshape(-1, width), w_gate[0], w_up[0], w_down[0]
    )
    returned = lax.all_to_all(expert_out.reshape(layout), "expert", 0, 0, tiled=True)
    picked = returned.reshape(-1, width)[target].astype(jnp.float32)
    summed = jnp.sum(picked.reshape(tok_rows, topk, width) * gates[:, :, None], axis=1)
    return summed.astype(jnp.bfloat16), reduce_grads(grads, width)


def exact_pieces(values):
    high = lax.reduce_precision(values, exponent_bits=8, mantissa_bits=7)
    rest = values - high
    middle = lax.reduce_precision(rest, exponent_bits=8, mantissa_bits=7)
    low = rest - middle
    return [part.astype(jnp.bfloat16) for part in (high, middle, low)]


def joined(pieces):
    total = pieces[0].astype(jnp.float32) + pieces[1].astype(jnp.float32)
    return total + pieces[2].astype(jnp.float32)


def gather_replica(values):
    mine = lax.all_gather(values, "ez", axis=0, tiled=True)
    return [mine, lax.ppermute(mine, "core", [(0, 1), (1, 0)])]


def ring_gather(block):
    n = lax.axis_size("ez")
    order = [2 * i for i in range(n // 2)] + [2 * i + 1 for i in reversed(range(n // 2))]
    if n % 2:
        order = list(range(n))
    place = [0] * n
    for p, c in enumerate(order):
        place[c] = p
    me = lax.axis_index("ez")
    at = jnp.asarray(place, jnp.int32)[me]
    ring = jnp.asarray(order, jnp.int32)
    out = jnp.zeros((n,) + block.shape, block.dtype)
    out = lax.dynamic_update_index_in_dim(out, block, me, 0)
    ahead = [(order[i], order[(i + 1) % n]) for i in range(n)]
    behind = [(order[i], order[(i - 1) % n]) for i in range(n)]
    up, down = block, block
    for step in range(1, n // 2 + 1):
        up = lax.ppermute(up, "ez", ahead)
        out = lax.dynamic_update_index_in_dim(out, up, ring[(at - step) % n], 0)
        if step <= (n - 1) // 2:
            down = lax.ppermute(down, "ez", behind)
            out = lax.dynamic_update_index_in_dim(out, down, ring[(at + step) % n], 0)
    mine = out.reshape((n * block.shape[0],) + block.shape[1:])
    return [mine, lax.ppermute(mine, "core", [(0, 1), (1, 0)])]


def slots_by_rank(routes, experts):
    tok_rows = routes.shape[0]
    onehot = routes[:, :, None] == lax.broadcasted_iota(jnp.int32, (1, 1, experts), 2)
    hits = jnp.any(onehot, axis=1).astype(jnp.bfloat16)
    before = (
        lax.broadcasted_iota(jnp.int32, (tok_rows, tok_rows), 0)
        > lax.broadcasted_iota(jnp.int32, (tok_rows, tok_rows), 1)
    ).astype(jnp.bfloat16)
    rank = jnp.dot(before, hits, preferred_element_type=jnp.float32).astype(jnp.int32)
    return jnp.sum(jnp.where(onehot, rank[:, None, :], 0), axis=2)


def reduce_grads_dp(grad_half, width):
    ndp = lax.axis_size("dp")
    if ndp != 2:
        grads = jnp.concatenate([grad_half(h) for h in range(ndp)], axis=0)
        return reduce_grads(grads, width)
    d = lax.axis_index("dp")
    sent = lax.ppermute(grad_half(1 - d).astype(jnp.bfloat16), "dp", [(0, 1), (1, 0)])
    summed = grad_half(d) + sent.astype(jnp.float32)
    return summed.reshape(1, summed.shape[0], 3, width)


def local_gather(tokens, masked, importance, routes, gates, cotangent, w_gate, w_up, w_down):
    tok_rows = tokens.shape[0]
    width = tokens.shape[1]
    topk = routes.shape[1]
    ncore = lax.axis_size("core")
    nchip = lax.axis_size("ez")
    experts = nchip * ncore
    capacity = min(tok_rows, 3 * tok_rows * topk // (2 * experts))
    core = lax.axis_index("core")
    me = lax.axis_index("ez") * ncore + core
    coef = importance * masked.astype(jnp.float32)
    factor = coef[:, None] * gates
    meta = [routes.astype(jnp.bfloat16)] + exact_pieces(factor) + exact_pieces(gates)
    pad = (-topk * len(meta)) % 128
    meta.append(jnp.zeros((tok_rows, pad), jnp.bfloat16))
    packed = jnp.concatenate([tokens] + meta, axis=1)

    gathered = lax.all_gather(packed, ("ez", "core"), axis=0, tiled=True)
    cot_halves = ring_gather(cotangent)
    on_core0 = core == 0
    cot_by_core = [
        jnp.where(on_core0, cot_halves[0], cot_halves[1]),
        jnp.where(on_core0, cot_halves[1], cot_halves[0]),
    ]
    all_p = gathered[:, width:]
    cols = [all_p[:, topk * i: topk * (i + 1)] for i in range(7)]
    hit = cols[0].astype(jnp.int32) == me
    zero = jnp.zeros((), jnp.float32)
    fac = jnp.sum(jnp.where(hit, joined(cols[1:4]), zero), axis=1)
    routed = jnp.any(hit, axis=1).reshape(experts, tok_rows)
    ahead = (
        lax.broadcasted_iota(jnp.int32, (tok_rows, tok_rows), 0)
        < lax.broadcasted_iota(jnp.int32, (tok_rows, tok_rows), 1)
    ).astype(jnp.bfloat16)
    rank = jnp.dot(
        routed.astype(jnp.bfloat16), ahead, preferred_element_type=jnp.float32
    ).astype(jnp.int32)
    slot_ids = lax.broadcasted_iota(jnp.int32, (experts, capacity, tok_rows), 1)
    pick = (routed[:, None, :] & (rank[:, None, :] == slot_ids)).astype(jnp.bfloat16)

    rows_x = jnp.einsum(
        "sjt,std->sjd",
        pick,
        gathered[:, :width].reshape(experts, tok_rows, width),
        preferred_element_type=jnp.float32,
    ).astype(jnp.bfloat16).reshape(experts * capacity, width)
    pick_by_core = pick.reshape(nchip, ncore, capacity, tok_rows)
    fac_by_core = fac.reshape(nchip, ncore, tok_rows)
    rows_q = []
    for k in range(ncore):
        scaled = fac_by_core[:, k, :, None] * cot_by_core[k].reshape(
            nchip, tok_rows, width
        ).astype(jnp.float32)
        rows_q.append(
            jnp.einsum(
                "sjt,std->sjd",
                pick_by_core[:, k],
                scaled.astype(jnp.bfloat16),
                preferred_element_type=jnp.float32,
            ).astype(jnp.bfloat16)
        )
    rows_q = jnp.stack(rows_q, axis=1).reshape(experts * capacity, width)
    wgate, wup, wdown = w_gate[0], w_up[0], w_down[0]
    gate_pre = contract_cols(rows_x, wgate)
    up_pre = contract_cols(rows_x, wup)
    sig = jax.nn.sigmoid(gate_pre)
    act = gate_pre * sig
    hidden = (act * up_pre).astype(jnp.bfloat16)
    expert_out = jnp.dot(hidden, wdown, preferred_element_type=jnp.float32).astype(
        jnp.bfloat16
    )

    ordered = expert_out.reshape(experts, capacity, width)
    returned = lax.all_to_all(ordered, ("ez", "core"), 0, 0, tiled=True)

    back = contract_cols(rows_q, wdown)
    d_gate = (back * up_pre * sig * (1.0 + gate_pre * (1.0 - sig))).astype(jnp.bfloat16)
    d_up = (back * act).astype(jnp.bfloat16)
    share = d_gate.shape[1] // lax.axis_size("dp")

    def grad_half(h):
        def part(v):
            return lax.dynamic_slice_in_dim(v, h * share, share, axis=1)

        return jnp.stack(
            [
                contract_rows(part(d_gate), rows_x),
                contract_rows(part(d_up), rows_x),
                contract_rows(part(hidden), rows_q),
            ],
            axis=1,
        )

    weight_grads = reduce_grads_dp(grad_half, width)

    target = (routes * capacity + slots_by_rank(routes, experts)).reshape(-1)
    choose = (
        target[:, None]
        == lax.broadcasted_iota(jnp.int32, (tok_rows * topk, experts * capacity), 1)
    ).astype(jnp.bfloat16)
    picked = jnp.dot(choose, returned.reshape(-1, width), preferred_element_type=jnp.float32)
    summed = jnp.sum(picked.reshape(tok_rows, topk, width) * gates[:, :, None], axis=1)
    return summed.astype(jnp.bfloat16), weight_grads


def specs(rows, experts):
    return (
        (P(rows, None), P(rows), P(rows), P(rows, None), P(rows, None), P(rows, None))
        + (P(experts, None, None),) * 3,
        (P(rows, None), P(experts, "dp", None, None)),
    )


def solution(mesh):
    ndp, nexp = mesh.shape["dp"], mesh.shape["expert"]
    split = jax.sharding.Mesh(mesh.devices.reshape(ndp, nexp // 2, 2), ("dp", "ez", "core"))
    ins, outs = specs(("dp", "ez", "core"), ("ez", "core"))
    gathered = jax.shard_map(local_gather, mesh=split, in_specs=ins, out_specs=outs, check_vma=False)
    ins, outs = specs(("dp", "expert"), "expert")
    routed = jax.shard_map(local_a2a, mesh=mesh, in_specs=ins, out_specs=outs, check_vma=False)

    def run(*args):
        if args[0].shape[0] // ndp <= GATHER_ROWS:
            return gathered(*args)
        return routed(*args)

    return run
```

```python
import jax
import jax.numpy as jnp
from jax import lax
from jax.sharding import PartitionSpec as P

GATHER_ROWS = 2048


def contract_rows(left, right):
    return lax.dot_general(
        left, right, (((0,), (0,)), ((), ())), preferred_element_type=jnp.float32
    )


def contract_cols(left, right):
    return lax.dot_general(
        left, right, (((1,), (1,)), ((), ())), preferred_element_type=jnp.float32
    )


def expert_math(rows_x, rows_q, wgate, wup, wdown):
    gate_pre = contract_cols(rows_x, wgate)
    up_pre = contract_cols(rows_x, wup)
    sig = jax.nn.sigmoid(gate_pre)
    act = gate_pre * sig
    hidden = (act * up_pre).astype(jnp.bfloat16)
    expert_out = jnp.dot(hidden, wdown, preferred_element_type=jnp.float32).astype(
        jnp.bfloat16
    )
    back = contract_cols(rows_q, wdown)
    d_gate = (back * up_pre * sig * (1.0 + gate_pre * (1.0 - sig))).astype(jnp.bfloat16)
    d_up = (back * act).astype(jnp.bfloat16)
    grad_gate = contract_rows(d_gate, rows_x)
    grad_up = contract_rows(d_up, rows_x)
    grad_down = contract_rows(hidden, rows_q)
    return expert_out, jnp.stack([grad_gate, grad_up, grad_down], axis=1)


def reduce_grads(grads, width):
    share = grads.shape[0] // lax.axis_size("dp")
    summed = lax.psum_scatter(grads, "dp", scatter_dimension=0, tiled=True)
    return summed.reshape(1, share, 3, width)


def source_slots(routes, experts):
    flat = routes.reshape(-1)
    onehot = (flat[:, None] == jnp.arange(experts, dtype=jnp.int32)[None, :]).astype(jnp.int32)
    before = jnp.cumsum(onehot, axis=0) - onehot
    return flat, jnp.sum(before * onehot, axis=1)


def local_a2a(tokens, masked, importance, routes, gates, cotangent, w_gate, w_up, w_down):
    tok_rows = tokens.shape[0]
    width = tokens.shape[1]
    topk = routes.shape[1]
    experts = lax.axis_size("expert")
    capacity = min(tok_rows, 3 * tok_rows * topk // (2 * experts))
    flat, slots = source_slots(routes, experts)
    target = flat * capacity + slots
    owner = jnp.arange(tok_rows * topk, dtype=jnp.int32) // topk
    coef = importance * masked.astype(jnp.float32)
    factor = (coef[:, None] * gates).reshape(-1)
    sent_x = jnp.zeros((experts * capacity, width), jnp.bfloat16).at[target].set(tokens[owner])
    scaled = (factor[:, None] * cotangent[owner].astype(jnp.float32)).astype(jnp.bfloat16)
    sent_q = jnp.zeros((experts * capacity, width), jnp.bfloat16).at[target].set(scaled)
    layout = (experts, capacity, width)
    recv_x = lax.all_to_all(sent_x.reshape(layout), "expert", 0, 0, tiled=True)
    recv_q = lax.all_to_all(sent_q.reshape(layout), "expert", 0, 0, tiled=True)
    expert_out, grads = expert_math(
        recv_x.reshape(-1, width), recv_q.reshape(-1, width), w_gate[0], w_up[0], w_down[0]
    )
    returned = lax.all_to_all(expert_out.reshape(layout), "expert", 0, 0, tiled=True)
    picked = returned.reshape(-1, width)[target].astype(jnp.float32)
    summed = jnp.sum(picked.reshape(tok_rows, topk, width) * gates[:, :, None], axis=1)
    return summed.astype(jnp.bfloat16), reduce_grads(grads, width)


def exact_pieces(values):
    high = lax.reduce_precision(values, exponent_bits=8, mantissa_bits=7)
    rest = values - high
    middle = lax.reduce_precision(rest, exponent_bits=8, mantissa_bits=7)
    low = rest - middle
    return [part.astype(jnp.bfloat16) for part in (high, middle, low)]


def joined(pieces):
    total = pieces[0].astype(jnp.float32) + pieces[1].astype(jnp.float32)
    return total + pieces[2].astype(jnp.float32)


def gather_replica(values):
    mine = lax.all_gather(values, "ez", axis=0, tiled=True)
    return [mine, lax.ppermute(mine, "core", [(0, 1), (1, 0)])]


def ring_gather(block):
    n = lax.axis_size("ez")
    order = [2 * i for i in range(n // 2)] + [2 * i + 1 for i in reversed(range(n // 2))]
    if n % 2:
        order = list(range(n))
    place = [0] * n
    for p, c in enumerate(order):
        place[c] = p
    me = lax.axis_index("ez")
    at = jnp.asarray(place, jnp.int32)[me]
    ring = jnp.asarray(order, jnp.int32)
    out = jnp.zeros((n,) + block.shape, block.dtype)
    out = lax.dynamic_update_index_in_dim(out, block, me, 0)
    ahead = [(order[i], order[(i + 1) % n]) for i in range(n)]
    behind = [(order[i], order[(i - 1) % n]) for i in range(n)]
    up, down = block, block
    for step in range(1, n // 2 + 1):
        up = lax.ppermute(up, "ez", ahead)
        out = lax.dynamic_update_index_in_dim(out, up, ring[(at - step) % n], 0)
        if step <= (n - 1) // 2:
            down = lax.ppermute(down, "ez", behind)
            out = lax.dynamic_update_index_in_dim(out, down, ring[(at + step) % n], 0)
    mine = out.reshape((n * block.shape[0],) + block.shape[1:])
    return [mine, lax.ppermute(mine, "core", [(0, 1), (1, 0)])]


def slots_by_rank(routes, experts):
    tok_rows = routes.shape[0]
    onehot = routes[:, :, None] == lax.broadcasted_iota(jnp.int32, (1, 1, experts), 2)
    hits = jnp.any(onehot, axis=1).astype(jnp.bfloat16)
    before = (
        lax.broadcasted_iota(jnp.int32, (tok_rows, tok_rows), 0)
        > lax.broadcasted_iota(jnp.int32, (tok_rows, tok_rows), 1)
    ).astype(jnp.bfloat16)
    rank = jnp.dot(before, hits, preferred_element_type=jnp.float32).astype(jnp.int32)
    return jnp.sum(jnp.where(onehot, rank[:, None, :], 0), axis=2)


def reduce_grads_dp(grad_half, width):
    ndp = lax.axis_size("dp")
    if ndp != 2:
        grads = jnp.concatenate([grad_half(h) for h in range(ndp)], axis=0)
        return reduce_grads(grads, width)
    d = lax.axis_index("dp")
    sent = lax.ppermute(grad_half(1 - d).astype(jnp.bfloat16), "dp", [(0, 1), (1, 0)])
    summed = grad_half(d) + sent.astype(jnp.float32)
    return summed.reshape(1, summed.shape[0], 3, width)


def local_gather(tokens, masked, importance, routes, gates, cotangent, w_gate, w_up, w_down):
    tok_rows = tokens.shape[0]
    width = tokens.shape[1]
    topk = routes.shape[1]
    ncore = lax.axis_size("core")
    nchip = lax.axis_size("ez")
    experts = nchip * ncore
    capacity = min(tok_rows, 3 * tok_rows * topk // (2 * experts))
    core = lax.axis_index("core")
    me = lax.axis_index("ez") * ncore + core
    coef = importance * masked.astype(jnp.float32)
    factor = coef[:, None] * gates
    meta = [routes.astype(jnp.bfloat16)] + exact_pieces(factor) + exact_pieces(gates)
    pad = (-topk * len(meta)) % 128
    meta.append(jnp.zeros((tok_rows, pad), jnp.bfloat16))
    packed = jnp.concatenate([tokens] + meta, axis=1)

    gathered = lax.all_gather(packed, ("ez", "core"), axis=0, tiled=True)
    cot_halves = ring_gather(cotangent)
    on_core0 = core == 0
    cot_by_core = [
        jnp.where(on_core0, cot_halves[0], cot_halves[1]),
        jnp.where(on_core0, cot_halves[1], cot_halves[0]),
    ]
    all_p = gathered[:, width:]
    cols = [all_p[:, topk * i: topk * (i + 1)] for i in range(7)]
    hit = cols[0].astype(jnp.int32) == me
    zero = jnp.zeros((), jnp.float32)
    fac = jnp.sum(jnp.where(hit, joined(cols[1:4]), zero), axis=1)
    routed = jnp.any(hit, axis=1).reshape(experts, tok_rows)
    ahead = (
        lax.broadcasted_iota(jnp.int32, (tok_rows, tok_rows), 0)
        < lax.broadcasted_iota(jnp.int32, (tok_rows, tok_rows), 1)
    ).astype(jnp.bfloat16)
    rank = jnp.dot(
        routed.astype(jnp.bfloat16), ahead, preferred_element_type=jnp.float32
    ).astype(jnp.int32)
    slot_ids = lax.broadcasted_iota(jnp.int32, (experts, capacity, tok_rows), 1)
    pick = (routed[:, None, :] & (rank[:, None, :] == slot_ids)).astype(jnp.bfloat16)

    rows_x = jnp.einsum(
        "sjt,std->sjd",
        pick,
        gathered[:, :width].reshape(experts, tok_rows, width),
        preferred_element_type=jnp.float32,
    ).astype(jnp.bfloat16).reshape(experts * capacity, width)
    pick_by_core = pick.reshape(nchip, ncore, capacity, tok_rows)
    fac_by_core = fac.reshape(nchip, ncore, tok_rows)
    rows_q = []
    for k in range(ncore):
        scaled = fac_by_core[:, k, :, None] * cot_by_core[k].reshape(
            nchip, tok_rows, width
        ).astype(jnp.float32)
        rows_q.append(
            jnp.einsum(
                "sjt,std->sjd",
                pick_by_core[:, k],
                scaled.astype(jnp.bfloat16),
                preferred_element_type=jnp.float32,
            ).astype(jnp.bfloat16)
        )
    rows_q = jnp.stack(rows_q, axis=1).reshape(experts * capacity, width)
    wgate, wup, wdown = w_gate[0], w_up[0], w_down[0]
    gate_pre = contract_cols(rows_x, wgate)
    up_pre = contract_cols(rows_x, wup)
    sig = jax.nn.sigmoid(gate_pre)
    act = gate_pre * sig
    hidden = (act * up_pre).astype(jnp.bfloat16)
    expert_out = jnp.dot(hidden, wdown, preferred_element_type=jnp.float32).astype(
        jnp.bfloat16
    )

    pick_k = pick.reshape(nchip, ncore, capacity, tok_rows)
    out_k = expert_out.reshape(nchip, ncore, capacity, width)
    dense = [
        jnp.einsum(
            "sjt,sjd->std", pick_k[:, k], out_k[:, k], preferred_element_type=jnp.float32
        ).astype(jnp.bfloat16)
        for k in range(ncore)
    ]
    mine = jnp.where(on_core0, dense[0], dense[1])
    from_partner = lax.ppermute(
        jnp.where(on_core0, dense[1], dense[0]), "core", [(0, 1), (1, 0)]
    )
    gate_all = joined(cols[4:7]).reshape(nchip, ncore, tok_rows, topk)
    routes_all = cols[0].astype(jnp.int32).reshape(nchip, ncore, tok_rows, topk)
    gate_own = jnp.where(on_core0, gate_all[:, 0], gate_all[:, 1])
    routes_own = jnp.where(on_core0, routes_all[:, 0], routes_all[:, 1])
    gte = jnp.sum(jnp.where(routes_own == me, gate_own, zero), axis=2)
    gte_partner = jnp.sum(jnp.where(routes_own == (me ^ 1), gate_own, zero), axis=2)
    combined = (
        gte[:, :, None] * mine.astype(jnp.float32)
        + gte_partner[:, :, None] * from_partner.astype(jnp.float32)
    ).astype(jnp.bfloat16)
    returned = lax.all_to_all(combined, "ez", 0, 0, tiled=True)

    back = contract_cols(rows_q, wdown)
    d_gate = (back * up_pre * sig * (1.0 + gate_pre * (1.0 - sig))).astype(jnp.bfloat16)
    d_up = (back * act).astype(jnp.bfloat16)
    share = d_gate.shape[1] // lax.axis_size("dp")

    def grad_half(h):
        def part(v):
            return lax.dynamic_slice_in_dim(v, h * share, share, axis=1)

        return jnp.stack(
            [
                contract_rows(part(d_gate), rows_x),
                contract_rows(part(d_up), rows_x),
                contract_rows(part(hidden), rows_q),
            ],
            axis=1,
        )

    weight_grads = reduce_grads_dp(grad_half, width)

    summed = jnp.sum(returned.astype(jnp.float32), axis=0)
    return summed.astype(jnp.bfloat16), weight_grads


def specs(rows, experts):
    return (
        (P(rows, None), P(rows), P(rows), P(rows, None), P(rows, None), P(rows, None))
        + (P(experts, None, None),) * 3,
        (P(rows, None), P(experts, "dp", None, None)),
    )


def solution(mesh):
    ndp, nexp = mesh.shape["dp"], mesh.shape["expert"]
    split = jax.sharding.Mesh(mesh.devices.reshape(ndp, nexp // 2, 2), ("dp", "ez", "core"))
    ins, outs = specs(("dp", "ez", "core"), ("ez", "core"))
    gathered = jax.shard_map(local_gather, mesh=split, in_specs=ins, out_specs=outs, check_vma=False)
    ins, outs = specs(("dp", "expert"), "expert")
    routed = jax.shard_map(local_a2a, mesh=mesh, in_specs=ins, out_specs=outs, check_vma=False)

    def run(*args):
        if args[0].shape[0] // ndp <= GATHER_ROWS:
            return gathered(*args)
        return routed(*args)

    return run
```

```python
import jax
import jax.numpy as jnp
from jax import lax
from jax.sharding import PartitionSpec as P

GATHER_ROWS = 2048


def contract_rows(left, right):
    return lax.dot_general(
        left, right, (((0,), (0,)), ((), ())), preferred_element_type=jnp.float32
    )


def contract_cols(left, right):
    return lax.dot_general(
        left, right, (((1,), (1,)), ((), ())), preferred_element_type=jnp.float32
    )


def expert_math(rows_x, rows_q, wgate, wup, wdown):
    gate_pre = contract_cols(rows_x, wgate)
    up_pre = contract_cols(rows_x, wup)
    sig = jax.nn.sigmoid(gate_pre)
    act = gate_pre * sig
    hidden = (act * up_pre).astype(jnp.bfloat16)
    expert_out = jnp.dot(hidden, wdown, preferred_element_type=jnp.float32).astype(
        jnp.bfloat16
    )
    back = contract_cols(rows_q, wdown)
    d_gate = (back * up_pre * sig * (1.0 + gate_pre * (1.0 - sig))).astype(jnp.bfloat16)
    d_up = (back * act).astype(jnp.bfloat16)
    grad_gate = contract_rows(d_gate, rows_x)
    grad_up = contract_rows(d_up, rows_x)
    grad_down = contract_rows(hidden, rows_q)
    return expert_out, jnp.stack([grad_gate, grad_up, grad_down], axis=1)


def reduce_grads(grads, width):
    share = grads.shape[0] // lax.axis_size("dp")
    summed = lax.psum_scatter(grads, "dp", scatter_dimension=0, tiled=True)
    return summed.reshape(1, share, 3, width)


def source_slots(routes, experts):
    flat = routes.reshape(-1)
    onehot = (flat[:, None] == jnp.arange(experts, dtype=jnp.int32)[None, :]).astype(jnp.int32)
    before = jnp.cumsum(onehot, axis=0) - onehot
    return flat, jnp.sum(before * onehot, axis=1)


def local_a2a(tokens, masked, importance, routes, gates, cotangent, w_gate, w_up, w_down):
    tok_rows = tokens.shape[0]
    width = tokens.shape[1]
    topk = routes.shape[1]
    experts = lax.axis_size("expert")
    capacity = min(tok_rows, 3 * tok_rows * topk // (2 * experts))
    flat, slots = source_slots(routes, experts)
    target = flat * capacity + slots
    owner = jnp.arange(tok_rows * topk, dtype=jnp.int32) // topk
    coef = importance * masked.astype(jnp.float32)
    factor = (coef[:, None] * gates).reshape(-1)
    sent_x = jnp.zeros((experts * capacity, width), jnp.bfloat16).at[target].set(tokens[owner])
    scaled = (factor[:, None] * cotangent[owner].astype(jnp.float32)).astype(jnp.bfloat16)
    sent_q = jnp.zeros((experts * capacity, width), jnp.bfloat16).at[target].set(scaled)
    layout = (experts, capacity, width)
    recv_x = lax.all_to_all(sent_x.reshape(layout), "expert", 0, 0, tiled=True)
    recv_q = lax.all_to_all(sent_q.reshape(layout), "expert", 0, 0, tiled=True)
    expert_out, grads = expert_math(
        recv_x.reshape(-1, width), recv_q.reshape(-1, width), w_gate[0], w_up[0], w_down[0]
    )
    returned = lax.all_to_all(expert_out.reshape(layout), "expert", 0, 0, tiled=True)
    picked = returned.reshape(-1, width)[target].astype(jnp.float32)
    summed = jnp.sum(picked.reshape(tok_rows, topk, width) * gates[:, :, None], axis=1)
    return summed.astype(jnp.bfloat16), reduce_grads(grads, width)


def exact_pieces(values):
    high = lax.reduce_precision(values, exponent_bits=8, mantissa_bits=7)
    rest = values - high
    middle = lax.reduce_precision(rest, exponent_bits=8, mantissa_bits=7)
    low = rest - middle
    return [part.astype(jnp.bfloat16) for part in (high, middle, low)]


def joined(pieces):
    total = pieces[0].astype(jnp.float32) + pieces[1].astype(jnp.float32)
    return total + pieces[2].astype(jnp.float32)


def gather_replica(values):
    mine = lax.all_gather(values, "ez", axis=0, tiled=True)
    return [mine, lax.ppermute(mine, "core", [(0, 1), (1, 0)])]


def ring_gather(block):
    n = lax.axis_size("ez")
    order = [2 * i for i in range(n // 2)] + [2 * i + 1 for i in reversed(range(n // 2))]
    if n % 2:
        order = list(range(n))
    place = [0] * n
    for p, c in enumerate(order):
        place[c] = p
    me = lax.axis_index("ez")
    at = jnp.asarray(place, jnp.int32)[me]
    ring = jnp.asarray(order, jnp.int32)
    out = jnp.zeros((n,) + block.shape, block.dtype)
    out = lax.dynamic_update_index_in_dim(out, block, me, 0)
    ahead = [(order[i], order[(i + 1) % n]) for i in range(n)]
    behind = [(order[i], order[(i - 1) % n]) for i in range(n)]
    up, down = block, block
    for step in range(1, n // 2 + 1):
        up = lax.ppermute(up, "ez", ahead)
        out = lax.dynamic_update_index_in_dim(out, up, ring[(at - step) % n], 0)
        if step <= (n - 1) // 2:
            down = lax.ppermute(down, "ez", behind)
            out = lax.dynamic_update_index_in_dim(out, down, ring[(at + step) % n], 0)
    mine = out.reshape((n * block.shape[0],) + block.shape[1:])
    return [mine, lax.ppermute(mine, "core", [(0, 1), (1, 0)])]


def slots_by_rank(routes, experts):
    tok_rows = routes.shape[0]
    onehot = routes[:, :, None] == lax.broadcasted_iota(jnp.int32, (1, 1, experts), 2)
    hits = jnp.any(onehot, axis=1).astype(jnp.bfloat16)
    before = (
        lax.broadcasted_iota(jnp.int32, (tok_rows, tok_rows), 0)
        > lax.broadcasted_iota(jnp.int32, (tok_rows, tok_rows), 1)
    ).astype(jnp.bfloat16)
    rank = jnp.dot(before, hits, preferred_element_type=jnp.float32).astype(jnp.int32)
    return jnp.sum(jnp.where(onehot, rank[:, None, :], 0), axis=2)


def reduce_grads_dp(grad_half, width):
    ndp = lax.axis_size("dp")
    if ndp != 2:
        grads = jnp.concatenate([grad_half(h) for h in range(ndp)], axis=0)
        return reduce_grads(grads, width)
    d = lax.axis_index("dp")
    sent = lax.ppermute(grad_half(1 - d).astype(jnp.bfloat16), "dp", [(0, 1), (1, 0)])
    summed = grad_half(d) + sent.astype(jnp.float32)
    return summed.reshape(1, summed.shape[0], 3, width)


def local_gather(tokens, masked, importance, routes, gates, cotangent, w_gate, w_up, w_down):
    tok_rows = tokens.shape[0]
    width = tokens.shape[1]
    topk = routes.shape[1]
    ncore = lax.axis_size("core")
    nchip = lax.axis_size("ez")
    experts = nchip * ncore
    capacity = min(tok_rows, 3 * tok_rows * topk // (2 * experts))
    core = lax.axis_index("core")
    me = lax.axis_index("ez") * ncore + core
    coef = importance * masked.astype(jnp.float32)
    factor = coef[:, None] * gates
    meta = [routes.astype(jnp.bfloat16)] + exact_pieces(factor) + exact_pieces(gates)
    meta_rows = jnp.concatenate([m.T for m in meta], axis=0)
    lines = -(-meta_rows.size // width)
    lines += (-(tok_rows + lines)) % 8
    flat_meta = jnp.pad(meta_rows.reshape(-1), (0, lines * width - meta_rows.size))
    packed = jnp.concatenate([tokens, flat_meta.reshape(lines, width)], axis=0)

    gathered = lax.all_gather(packed, ("ez", "core"), axis=0, tiled=True)
    gathered = gathered.reshape(experts, tok_rows + lines, width)
    cot_halves = ring_gather(cotangent)
    on_core0 = core == 0
    cot_by_core = [
        jnp.where(on_core0, cot_halves[0], cot_halves[1]),
        jnp.where(on_core0, cot_halves[1], cot_halves[0]),
    ]
    meta_all = gathered[:, tok_rows:].reshape(experts, lines * width)
    meta_all = meta_all[:, :meta_rows.size].reshape(experts, len(meta), topk, tok_rows)
    routes_t = meta_all[:, 0].astype(jnp.int32)
    hit = routes_t == me
    zero = jnp.zeros((), jnp.float32)
    fac = jnp.sum(jnp.where(hit, joined([meta_all[:, i] for i in (1, 2, 3)]), zero), axis=1)
    gate_t = joined([meta_all[:, i] for i in (4, 5, 6)])
    routed = jnp.any(hit, axis=1)
    ahead = (
        lax.broadcasted_iota(jnp.int32, (tok_rows, tok_rows), 0)
        < lax.broadcasted_iota(jnp.int32, (tok_rows, tok_rows), 1)
    ).astype(jnp.bfloat16)
    rank = jnp.dot(
        routed.astype(jnp.bfloat16), ahead, preferred_element_type=jnp.float32
    ).astype(jnp.int32)
    slot_ids = lax.broadcasted_iota(jnp.int32, (experts, capacity, tok_rows), 1)
    pick = (routed[:, None, :] & (rank[:, None, :] == slot_ids)).astype(jnp.bfloat16)

    rows_x = jnp.einsum(
        "sjt,std->sjd",
        pick,
        gathered[:, :tok_rows],
        preferred_element_type=jnp.float32,
    ).astype(jnp.bfloat16).reshape(experts * capacity, width)
    pick_by_core = pick.reshape(nchip, ncore, capacity, tok_rows)
    fac_by_core = fac.reshape(nchip, ncore, tok_rows)
    rows_q = []
    for k in range(ncore):
        scaled = fac_by_core[:, k, :, None] * cot_by_core[k].reshape(
            nchip, tok_rows, width
        ).astype(jnp.float32)
        rows_q.append(
            jnp.einsum(
                "sjt,std->sjd",
                pick_by_core[:, k],
                scaled.astype(jnp.bfloat16),
                preferred_element_type=jnp.float32,
            ).astype(jnp.bfloat16)
        )
    rows_q = jnp.stack(rows_q, axis=1).reshape(experts * capacity, width)
    wgate, wup, wdown = w_gate[0], w_up[0], w_down[0]
    gate_pre = contract_cols(rows_x, wgate)
    up_pre = contract_cols(rows_x, wup)
    sig = jax.nn.sigmoid(gate_pre)
    act = gate_pre * sig
    hidden = (act * up_pre).astype(jnp.bfloat16)
    expert_out = jnp.dot(hidden, wdown, preferred_element_type=jnp.float32).astype(
        jnp.bfloat16
    )

    pick_k = pick.reshape(nchip, ncore, capacity, tok_rows)
    out_k = expert_out.reshape(nchip, ncore, capacity, width)
    dense = [
        jnp.einsum(
            "sjt,sjd->std", pick_k[:, k], out_k[:, k], preferred_element_type=jnp.float32
        ).astype(jnp.bfloat16)
        for k in range(ncore)
    ]
    mine = jnp.where(on_core0, dense[0], dense[1])
    from_partner = lax.ppermute(
        jnp.where(on_core0, dense[1], dense[0]), "core", [(0, 1), (1, 0)]
    )
    gate_all = gate_t.reshape(nchip, ncore, topk, tok_rows)
    routes_all = routes_t.reshape(nchip, ncore, topk, tok_rows)
    gate_own = jnp.where(on_core0, gate_all[:, 0], gate_all[:, 1])
    routes_own = jnp.where(on_core0, routes_all[:, 0], routes_all[:, 1])
    gte = jnp.sum(jnp.where(routes_own == me, gate_own, zero), axis=1)
    gte_partner = jnp.sum(jnp.where(routes_own == (me ^ 1), gate_own, zero), axis=1)
    combined = (
        gte[:, :, None] * mine.astype(jnp.float32)
        + gte_partner[:, :, None] * from_partner.astype(jnp.float32)
    ).astype(jnp.bfloat16)
    returned = lax.all_to_all(combined, "ez", 0, 0, tiled=True)

    back = contract_cols(rows_q, wdown)
    d_gate = (back * up_pre * sig * (1.0 + gate_pre * (1.0 - sig))).astype(jnp.bfloat16)
    d_up = (back * act).astype(jnp.bfloat16)
    share = d_gate.shape[1] // lax.axis_size("dp")

    def grad_half(h):
        def part(v):
            return lax.dynamic_slice_in_dim(v, h * share, share, axis=1)

        return jnp.stack(
            [
                contract_rows(part(d_gate), rows_x),
                contract_rows(part(d_up), rows_x),
                contract_rows(part(hidden), rows_q),
            ],
            axis=1,
        )

    weight_grads = reduce_grads_dp(grad_half, width)

    summed = jnp.sum(returned.astype(jnp.float32), axis=0)
    return summed.astype(jnp.bfloat16), weight_grads


def specs(rows, experts):
    return (
        (P(rows, None), P(rows), P(rows), P(rows, None), P(rows, None), P(rows, None))
        + (P(experts, None, None),) * 3,
        (P(rows, None), P(experts, "dp", None, None)),
    )


def solution(mesh):
    ndp, nexp = mesh.shape["dp"], mesh.shape["expert"]
    split = jax.sharding.Mesh(mesh.devices.reshape(ndp, nexp // 2, 2), ("dp", "ez", "core"))
    ins, outs = specs(("dp", "ez", "core"), ("ez", "core"))
    gathered = jax.shard_map(local_gather, mesh=split, in_specs=ins, out_specs=outs, check_vma=False)
    ins, outs = specs(("dp", "expert"), "expert")
    routed = jax.shard_map(local_a2a, mesh=mesh, in_specs=ins, out_specs=outs, check_vma=False)

    def run(*args):
        if args[0].shape[0] // ndp <= GATHER_ROWS:
            return gathered(*args)
        return routed(*args)

    return run
```

```python
import jax
import jax.numpy as jnp
from jax import lax
from jax.sharding import PartitionSpec as P

GATHER_ROWS = 2048


def contract_rows(left, right):
    return lax.dot_general(
        left, right, (((0,), (0,)), ((), ())), preferred_element_type=jnp.float32
    )


def contract_cols(left, right):
    return lax.dot_general(
        left, right, (((1,), (1,)), ((), ())), preferred_element_type=jnp.float32
    )


def expert_math(rows_x, rows_q, wgate, wup, wdown):
    gate_pre = contract_cols(rows_x, wgate)
    up_pre = contract_cols(rows_x, wup)
    sig = jax.nn.sigmoid(gate_pre)
    act = gate_pre * sig
    hidden = (act * up_pre).astype(jnp.bfloat16)
    expert_out = jnp.dot(hidden, wdown, preferred_element_type=jnp.float32).astype(
        jnp.bfloat16
    )
    back = contract_cols(rows_q, wdown)
    d_gate = (back * up_pre * sig * (1.0 + gate_pre * (1.0 - sig))).astype(jnp.bfloat16)
    d_up = (back * act).astype(jnp.bfloat16)
    grad_gate = contract_rows(d_gate, rows_x)
    grad_up = contract_rows(d_up, rows_x)
    grad_down = contract_rows(hidden, rows_q)
    return expert_out, jnp.stack([grad_gate, grad_up, grad_down], axis=1)


def reduce_grads(grads, width):
    share = grads.shape[0] // lax.axis_size("dp")
    summed = lax.psum_scatter(grads, "dp", scatter_dimension=0, tiled=True)
    return summed.reshape(1, share, 3, width)


def source_slots(routes, experts):
    flat = routes.reshape(-1)
    onehot = (flat[:, None] == jnp.arange(experts, dtype=jnp.int32)[None, :]).astype(jnp.int32)
    before = jnp.cumsum(onehot, axis=0) - onehot
    return flat, jnp.sum(before * onehot, axis=1)


def local_a2a(tokens, masked, importance, routes, gates, cotangent, w_gate, w_up, w_down):
    tok_rows = tokens.shape[0]
    width = tokens.shape[1]
    topk = routes.shape[1]
    experts = lax.axis_size("expert")
    capacity = min(tok_rows, 3 * tok_rows * topk // (2 * experts))
    flat, slots = source_slots(routes, experts)
    target = flat * capacity + slots
    owner = jnp.arange(tok_rows * topk, dtype=jnp.int32) // topk
    coef = importance * masked.astype(jnp.float32)
    factor = (coef[:, None] * gates).reshape(-1)
    sent_x = jnp.zeros((experts * capacity, width), jnp.bfloat16).at[target].set(tokens[owner])
    scaled = (factor[:, None] * cotangent[owner].astype(jnp.float32)).astype(jnp.bfloat16)
    sent_q = jnp.zeros((experts * capacity, width), jnp.bfloat16).at[target].set(scaled)
    layout = (experts, capacity, width)
    recv_x = lax.all_to_all(sent_x.reshape(layout), "expert", 0, 0, tiled=True)
    recv_q = lax.all_to_all(sent_q.reshape(layout), "expert", 0, 0, tiled=True)
    expert_out, grads = expert_math(
        recv_x.reshape(-1, width), recv_q.reshape(-1, width), w_gate[0], w_up[0], w_down[0]
    )
    returned = lax.all_to_all(expert_out.reshape(layout), "expert", 0, 0, tiled=True)
    picked = returned.reshape(-1, width)[target].astype(jnp.float32)
    summed = jnp.sum(picked.reshape(tok_rows, topk, width) * gates[:, :, None], axis=1)
    return summed.astype(jnp.bfloat16), reduce_grads(grads, width)


def exact_pieces(values):
    high = lax.reduce_precision(values, exponent_bits=8, mantissa_bits=7)
    rest = values - high
    middle = lax.reduce_precision(rest, exponent_bits=8, mantissa_bits=7)
    low = rest - middle
    return [part.astype(jnp.bfloat16) for part in (high, middle, low)]


def joined(pieces):
    total = pieces[0].astype(jnp.float32) + pieces[1].astype(jnp.float32)
    return total + pieces[2].astype(jnp.float32)


def gather_replica(values):
    mine = lax.all_gather(values, "ez", axis=0, tiled=True)
    return [mine, lax.ppermute(mine, "core", [(0, 1), (1, 0)])]


def ring_gather(block):
    n = lax.axis_size("ez")
    order = [2 * i for i in range(n // 2)] + [2 * i + 1 for i in reversed(range(n // 2))]
    if n % 2:
        order = list(range(n))
    place = [0] * n
    for p, c in enumerate(order):
        place[c] = p
    me = lax.axis_index("ez")
    at = jnp.asarray(place, jnp.int32)[me]
    ring = jnp.asarray(order, jnp.int32)
    out = jnp.zeros((n,) + block.shape, block.dtype)
    out = lax.dynamic_update_index_in_dim(out, block, me, 0)
    ahead = [(order[i], order[(i + 1) % n]) for i in range(n)]
    behind = [(order[i], order[(i - 1) % n]) for i in range(n)]
    up, down = block, block
    for step in range(1, n // 2 + 1):
        up = lax.ppermute(up, "ez", ahead)
        out = lax.dynamic_update_index_in_dim(out, up, ring[(at - step) % n], 0)
        if step <= (n - 1) // 2:
            down = lax.ppermute(down, "ez", behind)
            out = lax.dynamic_update_index_in_dim(out, down, ring[(at + step) % n], 0)
    mine = out.reshape((n * block.shape[0],) + block.shape[1:])
    return [mine, lax.ppermute(mine, "core", [(0, 1), (1, 0)])]


def slots_by_rank(routes, experts):
    tok_rows = routes.shape[0]
    onehot = routes[:, :, None] == lax.broadcasted_iota(jnp.int32, (1, 1, experts), 2)
    hits = jnp.any(onehot, axis=1).astype(jnp.bfloat16)
    before = (
        lax.broadcasted_iota(jnp.int32, (tok_rows, tok_rows), 0)
        > lax.broadcasted_iota(jnp.int32, (tok_rows, tok_rows), 1)
    ).astype(jnp.bfloat16)
    rank = jnp.dot(before, hits, preferred_element_type=jnp.float32).astype(jnp.int32)
    return jnp.sum(jnp.where(onehot, rank[:, None, :], 0), axis=2)


def reduce_grads_dp(grad_half, width):
    ndp = lax.axis_size("dp")
    if ndp != 2:
        grads = jnp.concatenate([grad_half(h) for h in range(ndp)], axis=0)
        return reduce_grads(grads, width)
    d = lax.axis_index("dp")
    sent = lax.ppermute(grad_half(1 - d).astype(jnp.bfloat16), "dp", [(0, 1), (1, 0)])
    summed = grad_half(d) + sent.astype(jnp.float32)
    return summed.reshape(1, summed.shape[0], 3, width)


def local_gather(tokens, masked, importance, routes, gates, cotangent, w_gate, w_up, w_down):
    tok_rows = tokens.shape[0]
    width = tokens.shape[1]
    topk = routes.shape[1]
    ncore = lax.axis_size("core")
    nchip = lax.axis_size("ez")
    experts = nchip * ncore
    capacity = min(tok_rows, 3 * tok_rows * topk // (2 * experts))
    core = lax.axis_index("core")
    me = lax.axis_index("ez") * ncore + core
    coef = importance * masked.astype(jnp.float32)
    factor = coef[:, None] * gates
    meta = [routes.astype(jnp.bfloat16)] + exact_pieces(factor) + exact_pieces(gates)
    meta_rows = jnp.concatenate([m.T for m in meta], axis=0)
    lines = -(-meta_rows.size // width)
    lines += (-(tok_rows + lines)) % 8
    flat_meta = jnp.pad(meta_rows.reshape(-1), (0, lines * width - meta_rows.size))
    packed = jnp.concatenate([tokens, flat_meta.reshape(lines, width)], axis=0)

    gathered = lax.all_gather(packed, ("ez", "core"), axis=0, tiled=True)
    gathered = gathered.reshape(experts, tok_rows + lines, width)
    cot_halves = ring_gather(cotangent)
    on_core0 = core == 0
    cot_by_core = [
        jnp.where(on_core0, cot_halves[0], cot_halves[1]),
        jnp.where(on_core0, cot_halves[1], cot_halves[0]),
    ]
    meta_all = gathered[:, tok_rows:].reshape(experts, lines * width)
    meta_all = meta_all[:, :meta_rows.size].reshape(experts, len(meta), topk, tok_rows)
    routes_t = meta_all[:, 0].astype(jnp.int32)
    hit = routes_t == me
    zero = jnp.zeros((), jnp.float32)
    fac = jnp.sum(jnp.where(hit, joined([meta_all[:, i] for i in (1, 2, 3)]), zero), axis=1)
    gate_t = joined([meta_all[:, i] for i in (4, 5, 6)])
    routed = jnp.any(hit, axis=1)
    ahead = (
        lax.broadcasted_iota(jnp.int32, (tok_rows, tok_rows), 0)
        < lax.broadcasted_iota(jnp.int32, (tok_rows, tok_rows), 1)
    ).astype(jnp.bfloat16)
    rank = jnp.dot(
        routed.astype(jnp.bfloat16), ahead, preferred_element_type=jnp.float32
    ).astype(jnp.int32)
    slot_ids = lax.broadcasted_iota(jnp.int32, (experts, capacity, tok_rows), 1)
    pick = (routed[:, None, :] & (rank[:, None, :] == slot_ids)).astype(jnp.bfloat16)

    rows_x = jnp.einsum(
        "sjt,std->sjd",
        pick,
        gathered[:, :tok_rows],
        preferred_element_type=jnp.float32,
    ).astype(jnp.bfloat16).reshape(experts * capacity, width)
    pick_by_core = pick.reshape(nchip, ncore, capacity, tok_rows)
    fac_by_core = fac.reshape(nchip, ncore, tok_rows)
    rows_q = []
    for k in range(ncore):
        scaled = fac_by_core[:, k, :, None] * cot_by_core[k].reshape(
            nchip, tok_rows, width
        ).astype(jnp.float32)
        rows_q.append(
            jnp.einsum(
                "sjt,std->sjd",
                pick_by_core[:, k],
                scaled.astype(jnp.bfloat16),
                preferred_element_type=jnp.float32,
            ).astype(jnp.bfloat16)
        )
    rows_q = jnp.stack(rows_q, axis=1).reshape(experts * capacity, width)
    wgate, wup, wdown = w_gate[0], w_up[0], w_down[0]
    gate_pre = contract_cols(rows_x, wgate)
    up_pre = contract_cols(rows_x, wup)
    sig = jax.nn.sigmoid(gate_pre)
    act = gate_pre * sig
    hidden = (act * up_pre).astype(jnp.bfloat16)
    expert_out = jnp.dot(hidden, wdown, preferred_element_type=jnp.float32).astype(
        jnp.bfloat16
    )

    pick_k = pick.reshape(nchip, ncore, capacity, tok_rows)
    out_k = expert_out.reshape(nchip, ncore, capacity, width)
    def dense_for(k):
        return jnp.einsum(
            "sjt,sjd->std",
            lax.dynamic_index_in_dim(pick_k, k, 1, keepdims=False),
            lax.dynamic_index_in_dim(out_k, k, 1, keepdims=False),
            preferred_element_type=jnp.float32,
        ).astype(jnp.bfloat16)

    from_partner = lax.ppermute(dense_for(1 - core), "core", [(0, 1), (1, 0)])
    mine = dense_for(core)
    gate_all = gate_t.reshape(nchip, ncore, topk, tok_rows)
    routes_all = routes_t.reshape(nchip, ncore, topk, tok_rows)
    gate_own = jnp.where(on_core0, gate_all[:, 0], gate_all[:, 1])
    routes_own = jnp.where(on_core0, routes_all[:, 0], routes_all[:, 1])
    gte = jnp.sum(jnp.where(routes_own == me, gate_own, zero), axis=1)
    gte_partner = jnp.sum(jnp.where(routes_own == (me ^ 1), gate_own, zero), axis=1)
    combined = (
        gte[:, :, None] * mine.astype(jnp.float32)
        + gte_partner[:, :, None] * from_partner.astype(jnp.float32)
    ).astype(jnp.bfloat16)
    returned = lax.all_to_all(combined, "ez", 0, 0, tiled=True)

    back = contract_cols(rows_q, wdown)
    d_gate = (back * up_pre * sig * (1.0 + gate_pre * (1.0 - sig))).astype(jnp.bfloat16)
    d_up = (back * act).astype(jnp.bfloat16)
    share = d_gate.shape[1] // lax.axis_size("dp")

    def grad_half(h):
        def part(v):
            return lax.dynamic_slice_in_dim(v, h * share, share, axis=1)

        return jnp.stack(
            [
                contract_rows(part(d_gate), rows_x),
                contract_rows(part(d_up), rows_x),
                contract_rows(part(hidden), rows_q),
            ],
            axis=1,
        )

    weight_grads = reduce_grads_dp(grad_half, width)

    summed = jnp.sum(returned.astype(jnp.float32), axis=0)
    return summed.astype(jnp.bfloat16), weight_grads


def specs(rows, experts):
    return (
        (P(rows, None), P(rows), P(rows), P(rows, None), P(rows, None), P(rows, None))
        + (P(experts, None, None),) * 3,
        (P(rows, None), P(experts, "dp", None, None)),
    )


def solution(mesh):
    ndp, nexp = mesh.shape["dp"], mesh.shape["expert"]
    split = jax.sharding.Mesh(mesh.devices.reshape(ndp, nexp // 2, 2), ("dp", "ez", "core"))
    ins, outs = specs(("dp", "ez", "core"), ("ez", "core"))
    gathered = jax.shard_map(local_gather, mesh=split, in_specs=ins, out_specs=outs, check_vma=False)
    ins, outs = specs(("dp", "expert"), "expert")
    routed = jax.shard_map(local_a2a, mesh=mesh, in_specs=ins, out_specs=outs, check_vma=False)

    def run(*args):
        if args[0].shape[0] // ndp <= GATHER_ROWS:
            return gathered(*args)
        return routed(*args)

    return run
```

```python
import jax
import jax.numpy as jnp
from jax import lax
from jax.sharding import PartitionSpec as P

GATHER_ROWS = 2048


def contract_rows(left, right):
    return lax.dot_general(
        left, right, (((0,), (0,)), ((), ())), preferred_element_type=jnp.float32
    )


def contract_cols(left, right):
    return lax.dot_general(
        left, right, (((1,), (1,)), ((), ())), preferred_element_type=jnp.float32
    )


def expert_math(rows_x, rows_q, wgate, wup, wdown):
    gate_pre = contract_cols(rows_x, wgate)
    up_pre = contract_cols(rows_x, wup)
    sig = jax.nn.sigmoid(gate_pre)
    act = gate_pre * sig
    hidden = (act * up_pre).astype(jnp.bfloat16)
    expert_out = jnp.dot(hidden, wdown, preferred_element_type=jnp.float32).astype(
        jnp.bfloat16
    )
    back = contract_cols(rows_q, wdown)
    d_gate = (back * up_pre * sig * (1.0 + gate_pre * (1.0 - sig))).astype(jnp.bfloat16)
    d_up = (back * act).astype(jnp.bfloat16)
    grad_gate = contract_rows(d_gate, rows_x)
    grad_up = contract_rows(d_up, rows_x)
    grad_down = contract_rows(hidden, rows_q)
    return expert_out, jnp.stack([grad_gate, grad_up, grad_down], axis=1)


def reduce_grads(grads, width):
    share = grads.shape[0] // lax.axis_size("dp")
    summed = lax.psum_scatter(grads, "dp", scatter_dimension=0, tiled=True)
    return summed.reshape(1, share, 3, width)


def source_slots(routes, experts):
    flat = routes.reshape(-1)
    onehot = (flat[:, None] == jnp.arange(experts, dtype=jnp.int32)[None, :]).astype(jnp.int32)
    before = jnp.cumsum(onehot, axis=0) - onehot
    return flat, jnp.sum(before * onehot, axis=1)


def local_a2a(tokens, masked, importance, routes, gates, cotangent, w_gate, w_up, w_down):
    tok_rows = tokens.shape[0]
    width = tokens.shape[1]
    topk = routes.shape[1]
    experts = lax.axis_size("expert")
    capacity = min(tok_rows, 3 * tok_rows * topk // (2 * experts))
    flat, slots = source_slots(routes, experts)
    target = flat * capacity + slots
    owner = jnp.arange(tok_rows * topk, dtype=jnp.int32) // topk
    coef = importance * masked.astype(jnp.float32)
    factor = (coef[:, None] * gates).reshape(-1)
    sent_x = jnp.zeros((experts * capacity, width), jnp.bfloat16).at[target].set(tokens[owner])
    scaled = (factor[:, None] * cotangent[owner].astype(jnp.float32)).astype(jnp.bfloat16)
    sent_q = jnp.zeros((experts * capacity, width), jnp.bfloat16).at[target].set(scaled)
    layout = (experts, capacity, width)
    recv_x = lax.all_to_all(sent_x.reshape(layout), "expert", 0, 0, tiled=True)
    recv_q = lax.all_to_all(sent_q.reshape(layout), "expert", 0, 0, tiled=True)
    expert_out, grads = expert_math(
        recv_x.reshape(-1, width), recv_q.reshape(-1, width), w_gate[0], w_up[0], w_down[0]
    )
    returned = lax.all_to_all(expert_out.reshape(layout), "expert", 0, 0, tiled=True)
    picked = returned.reshape(-1, width)[target].astype(jnp.float32)
    summed = jnp.sum(picked.reshape(tok_rows, topk, width) * gates[:, :, None], axis=1)
    return summed.astype(jnp.bfloat16), reduce_grads(grads, width)


def exact_pieces(values):
    high = lax.reduce_precision(values, exponent_bits=8, mantissa_bits=7)
    rest = values - high
    middle = lax.reduce_precision(rest, exponent_bits=8, mantissa_bits=7)
    low = rest - middle
    return [part.astype(jnp.bfloat16) for part in (high, middle, low)]


def joined(pieces):
    total = pieces[0].astype(jnp.float32) + pieces[1].astype(jnp.float32)
    return total + pieces[2].astype(jnp.float32)


def gather_replica(values):
    mine = lax.all_gather(values, "ez", axis=0, tiled=True)
    return [mine, lax.ppermute(mine, "core", [(0, 1), (1, 0)])]


def ring_gather(block):
    n = lax.axis_size("ez")
    order = [2 * i for i in range(n // 2)] + [2 * i + 1 for i in reversed(range(n // 2))]
    if n % 2:
        order = list(range(n))
    place = [0] * n
    for p, c in enumerate(order):
        place[c] = p
    me = lax.axis_index("ez")
    at = jnp.asarray(place, jnp.int32)[me]
    ring = jnp.asarray(order, jnp.int32)
    out = jnp.zeros((n,) + block.shape, block.dtype)
    out = lax.dynamic_update_index_in_dim(out, block, me, 0)
    ahead = [(order[i], order[(i + 1) % n]) for i in range(n)]
    behind = [(order[i], order[(i - 1) % n]) for i in range(n)]
    up, down = block, block
    for step in range(1, n // 2 + 1):
        up = lax.ppermute(up, "ez", ahead)
        out = lax.dynamic_update_index_in_dim(out, up, ring[(at - step) % n], 0)
        if step <= (n - 1) // 2:
            down = lax.ppermute(down, "ez", behind)
            out = lax.dynamic_update_index_in_dim(out, down, ring[(at + step) % n], 0)
    mine = out.reshape((n * block.shape[0],) + block.shape[1:])
    return [mine, lax.ppermute(mine, "core", [(0, 1), (1, 0)])]


def slots_by_rank(routes, experts):
    tok_rows = routes.shape[0]
    onehot = routes[:, :, None] == lax.broadcasted_iota(jnp.int32, (1, 1, experts), 2)
    hits = jnp.any(onehot, axis=1).astype(jnp.bfloat16)
    before = (
        lax.broadcasted_iota(jnp.int32, (tok_rows, tok_rows), 0)
        > lax.broadcasted_iota(jnp.int32, (tok_rows, tok_rows), 1)
    ).astype(jnp.bfloat16)
    rank = jnp.dot(before, hits, preferred_element_type=jnp.float32).astype(jnp.int32)
    return jnp.sum(jnp.where(onehot, rank[:, None, :], 0), axis=2)


def reduce_grads_dp(grad_half, width):
    ndp = lax.axis_size("dp")
    if ndp != 2:
        grads = jnp.concatenate([grad_half(h) for h in range(ndp)], axis=0)
        return reduce_grads(grads, width)
    d = lax.axis_index("dp")
    sent = lax.ppermute(grad_half(1 - d).astype(jnp.bfloat16), "dp", [(0, 1), (1, 0)])
    summed = grad_half(d) + sent.astype(jnp.float32)
    return summed.reshape(1, summed.shape[0], 3, width)


def local_gather(tokens, masked, importance, routes, gates, cotangent, w_gate, w_up, w_down):
    tok_rows = tokens.shape[0]
    width = tokens.shape[1]
    topk = routes.shape[1]
    ncore = lax.axis_size("core")
    nchip = lax.axis_size("ez")
    experts = nchip * ncore
    capacity = min(tok_rows, 3 * tok_rows * topk // (2 * experts))
    core = lax.axis_index("core")
    me = lax.axis_index("ez") * ncore + core
    coef = importance * masked.astype(jnp.float32)
    factor = coef[:, None] * gates
    meta = [routes.astype(jnp.bfloat16)] + exact_pieces(factor) + exact_pieces(gates)
    meta_rows = jnp.concatenate([m.T for m in meta], axis=0)
    lines = -(-meta_rows.size // width)
    lines += (-(tok_rows + lines)) % 8
    flat_meta = jnp.pad(meta_rows.reshape(-1), (0, lines * width - meta_rows.size))
    packed = jnp.concatenate([tokens, flat_meta.reshape(lines, width)], axis=0)

    gathered = lax.all_gather(packed, ("ez", "core"), axis=0, tiled=True)
    gathered = gathered.reshape(experts, tok_rows + lines, width)
    all_cot = lax.all_gather(cotangent, ("ez", "core"), axis=0, tiled=True)
    on_core0 = core == 0
    meta_all = gathered[:, tok_rows:].reshape(experts, lines * width)
    meta_all = meta_all[:, :meta_rows.size].reshape(experts, len(meta), topk, tok_rows)
    routes_t = meta_all[:, 0].astype(jnp.int32)
    hit = routes_t == me
    zero = jnp.zeros((), jnp.float32)
    fac = jnp.sum(jnp.where(hit, joined([meta_all[:, i] for i in (1, 2, 3)]), zero), axis=1)
    gate_t = joined([meta_all[:, i] for i in (4, 5, 6)])
    routed = jnp.any(hit, axis=1)
    ahead = (
        lax.broadcasted_iota(jnp.int32, (tok_rows, tok_rows), 0)
        < lax.broadcasted_iota(jnp.int32, (tok_rows, tok_rows), 1)
    ).astype(jnp.bfloat16)
    rank = jnp.dot(
        routed.astype(jnp.bfloat16), ahead, preferred_element_type=jnp.float32
    ).astype(jnp.int32)
    slot_ids = lax.broadcasted_iota(jnp.int32, (experts, capacity, tok_rows), 1)
    pick = (routed[:, None, :] & (rank[:, None, :] == slot_ids)).astype(jnp.bfloat16)

    rows_x = jnp.einsum(
        "sjt,std->sjd",
        pick,
        gathered[:, :tok_rows],
        preferred_element_type=jnp.float32,
    ).astype(jnp.bfloat16).reshape(experts * capacity, width)
    scaled = fac[:, :, None] * all_cot.reshape(experts, tok_rows, width).astype(jnp.float32)
    rows_q = jnp.einsum(
        "sjt,std->sjd", pick, scaled.astype(jnp.bfloat16), preferred_element_type=jnp.float32
    ).astype(jnp.bfloat16).reshape(experts * capacity, width)
    wgate, wup, wdown = w_gate[0], w_up[0], w_down[0]
    gate_pre = contract_cols(rows_x, wgate)
    up_pre = contract_cols(rows_x, wup)
    sig = jax.nn.sigmoid(gate_pre)
    act = gate_pre * sig
    hidden = (act * up_pre).astype(jnp.bfloat16)
    expert_out = jnp.dot(hidden, wdown, preferred_element_type=jnp.float32).astype(
        jnp.bfloat16
    )

    pick_k = pick.reshape(nchip, ncore, capacity, tok_rows)
    out_k = expert_out.reshape(nchip, ncore, capacity, width)
    def dense_for(k):
        return jnp.einsum(
            "sjt,sjd->std",
            lax.dynamic_index_in_dim(pick_k, k, 1, keepdims=False),
            lax.dynamic_index_in_dim(out_k, k, 1, keepdims=False),
            preferred_element_type=jnp.float32,
        ).astype(jnp.bfloat16)

    from_partner = lax.ppermute(dense_for(1 - core), "core", [(0, 1), (1, 0)])
    mine = dense_for(core)
    gate_all = gate_t.reshape(nchip, ncore, topk, tok_rows)
    routes_all = routes_t.reshape(nchip, ncore, topk, tok_rows)
    gate_own = jnp.where(on_core0, gate_all[:, 0], gate_all[:, 1])
    routes_own = jnp.where(on_core0, routes_all[:, 0], routes_all[:, 1])
    gte = jnp.sum(jnp.where(routes_own == me, gate_own, zero), axis=1)
    gte_partner = jnp.sum(jnp.where(routes_own == (me ^ 1), gate_own, zero), axis=1)
    combined = (
        gte[:, :, None] * mine.astype(jnp.float32)
        + gte_partner[:, :, None] * from_partner.astype(jnp.float32)
    ).astype(jnp.bfloat16)
    returned = lax.all_to_all(combined, "ez", 0, 0, tiled=True)

    back = contract_cols(rows_q, wdown)
    d_gate = (back * up_pre * sig * (1.0 + gate_pre * (1.0 - sig))).astype(jnp.bfloat16)
    d_up = (back * act).astype(jnp.bfloat16)
    share = d_gate.shape[1] // lax.axis_size("dp")

    def grad_half(h):
        def part(v):
            return lax.dynamic_slice_in_dim(v, h * share, share, axis=1)

        return jnp.stack(
            [
                contract_rows(part(d_gate), rows_x),
                contract_rows(part(d_up), rows_x),
                contract_rows(part(hidden), rows_q),
            ],
            axis=1,
        )

    weight_grads = reduce_grads_dp(grad_half, width)

    summed = jnp.sum(returned.astype(jnp.float32), axis=0)
    return summed.astype(jnp.bfloat16), weight_grads


def specs(rows, experts):
    return (
        (P(rows, None), P(rows), P(rows), P(rows, None), P(rows, None), P(rows, None))
        + (P(experts, None, None),) * 3,
        (P(rows, None), P(experts, "dp", None, None)),
    )


def solution(mesh):
    ndp, nexp = mesh.shape["dp"], mesh.shape["expert"]
    split = jax.sharding.Mesh(mesh.devices.reshape(ndp, nexp // 2, 2), ("dp", "ez", "core"))
    ins, outs = specs(("dp", "ez", "core"), ("ez", "core"))
    gathered = jax.shard_map(local_gather, mesh=split, in_specs=ins, out_specs=outs, check_vma=False)
    ins, outs = specs(("dp", "expert"), "expert")
    routed = jax.shard_map(local_a2a, mesh=mesh, in_specs=ins, out_specs=outs, check_vma=False)

    def run(*args):
        if args[0].shape[0] // ndp <= GATHER_ROWS:
            return gathered(*args)
        return routed(*args)

    return run
```

```python
import jax
import jax.numpy as jnp
from jax import lax
from jax.sharding import PartitionSpec as P

GATHER_ROWS = 2048


def contract_rows(left, right):
    return lax.dot_general(
        left, right, (((0,), (0,)), ((), ())), preferred_element_type=jnp.float32
    )


def contract_cols(left, right):
    return lax.dot_general(
        left, right, (((1,), (1,)), ((), ())), preferred_element_type=jnp.float32
    )


def expert_math(rows_x, rows_q, wgate, wup, wdown):
    gate_pre = contract_cols(rows_x, wgate)
    up_pre = contract_cols(rows_x, wup)
    sig = jax.nn.sigmoid(gate_pre)
    act = gate_pre * sig
    hidden = (act * up_pre).astype(jnp.bfloat16)
    expert_out = jnp.dot(hidden, wdown, preferred_element_type=jnp.float32).astype(
        jnp.bfloat16
    )
    back = contract_cols(rows_q, wdown)
    d_gate = (back * up_pre * sig * (1.0 + gate_pre * (1.0 - sig))).astype(jnp.bfloat16)
    d_up = (back * act).astype(jnp.bfloat16)
    grad_gate = contract_rows(d_gate, rows_x)
    grad_up = contract_rows(d_up, rows_x)
    grad_down = contract_rows(hidden, rows_q)
    return expert_out, jnp.stack([grad_gate, grad_up, grad_down], axis=1)


def reduce_grads(grads, width):
    share = grads.shape[0] // lax.axis_size("dp")
    summed = lax.psum_scatter(grads, "dp", scatter_dimension=0, tiled=True)
    return summed.reshape(1, share, 3, width)


def source_slots(routes, experts):
    flat = routes.reshape(-1)
    onehot = (flat[:, None] == jnp.arange(experts, dtype=jnp.int32)[None, :]).astype(jnp.int32)
    before = jnp.cumsum(onehot, axis=0) - onehot
    return flat, jnp.sum(before * onehot, axis=1)


def local_a2a(tokens, masked, importance, routes, gates, cotangent, w_gate, w_up, w_down):
    tok_rows = tokens.shape[0]
    width = tokens.shape[1]
    topk = routes.shape[1]
    experts = lax.axis_size("expert")
    capacity = min(tok_rows, 3 * tok_rows * topk // (2 * experts))
    flat, slots = source_slots(routes, experts)
    target = flat * capacity + slots
    owner = jnp.arange(tok_rows * topk, dtype=jnp.int32) // topk
    coef = importance * masked.astype(jnp.float32)
    factor = (coef[:, None] * gates).reshape(-1)
    sent_x = jnp.zeros((experts * capacity, width), jnp.bfloat16).at[target].set(tokens[owner])
    scaled = (factor[:, None] * cotangent[owner].astype(jnp.float32)).astype(jnp.bfloat16)
    sent_q = jnp.zeros((experts * capacity, width), jnp.bfloat16).at[target].set(scaled)
    layout = (experts, capacity, width)
    recv_x = lax.all_to_all(sent_x.reshape(layout), "expert", 0, 0, tiled=True)
    recv_q = lax.all_to_all(sent_q.reshape(layout), "expert", 0, 0, tiled=True)
    expert_out, grads = expert_math(
        recv_x.reshape(-1, width), recv_q.reshape(-1, width), w_gate[0], w_up[0], w_down[0]
    )
    returned = lax.all_to_all(expert_out.reshape(layout), "expert", 0, 0, tiled=True)
    picked = returned.reshape(-1, width)[target].astype(jnp.float32)
    summed = jnp.sum(picked.reshape(tok_rows, topk, width) * gates[:, :, None], axis=1)
    return summed.astype(jnp.bfloat16), reduce_grads(grads, width)


def exact_pieces(values):
    high = lax.reduce_precision(values, exponent_bits=8, mantissa_bits=7)
    rest = values - high
    middle = lax.reduce_precision(rest, exponent_bits=8, mantissa_bits=7)
    low = rest - middle
    return [part.astype(jnp.bfloat16) for part in (high, middle, low)]


def joined(pieces):
    total = pieces[0].astype(jnp.float32) + pieces[1].astype(jnp.float32)
    return total + pieces[2].astype(jnp.float32)


def gather_replica(values):
    mine = lax.all_gather(values, "ez", axis=0, tiled=True)
    return [mine, lax.ppermute(mine, "core", [(0, 1), (1, 0)])]


def ring_gather(block):
    n = lax.axis_size("ez")
    order = [2 * i for i in range(n // 2)] + [2 * i + 1 for i in reversed(range(n // 2))]
    if n % 2:
        order = list(range(n))
    place = [0] * n
    for p, c in enumerate(order):
        place[c] = p
    me = lax.axis_index("ez")
    at = jnp.asarray(place, jnp.int32)[me]
    ring = jnp.asarray(order, jnp.int32)
    out = jnp.zeros((n,) + block.shape, block.dtype)
    out = lax.dynamic_update_index_in_dim(out, block, me, 0)
    ahead = [(order[i], order[(i + 1) % n]) for i in range(n)]
    behind = [(order[i], order[(i - 1) % n]) for i in range(n)]
    up, down = block, block
    both = (n - 1) // 2
    for step in range(1, both + 1):
        up = lax.ppermute(up, "ez", ahead)
        out = lax.dynamic_update_index_in_dim(out, up, ring[(at - step) % n], 0)
        down = lax.ppermute(down, "ez", behind)
        out = lax.dynamic_update_index_in_dim(out, down, ring[(at + step) % n], 0)

    def finish(after):
        last, held, _ = lax.optimization_barrier((up, out, after))
        for step in range(both + 1, n // 2 + 1):
            last = lax.ppermute(last, "ez", ahead)
            held = lax.dynamic_update_index_in_dim(held, last, ring[(at - step) % n], 0)
        mine = held.reshape((n * block.shape[0],) + block.shape[1:])
        return [mine, lax.ppermute(mine, "core", [(0, 1), (1, 0)])]

    return finish


def slots_by_rank(routes, experts):
    tok_rows = routes.shape[0]
    onehot = routes[:, :, None] == lax.broadcasted_iota(jnp.int32, (1, 1, experts), 2)
    hits = jnp.any(onehot, axis=1).astype(jnp.bfloat16)
    before = (
        lax.broadcasted_iota(jnp.int32, (tok_rows, tok_rows), 0)
        > lax.broadcasted_iota(jnp.int32, (tok_rows, tok_rows), 1)
    ).astype(jnp.bfloat16)
    rank = jnp.dot(before, hits, preferred_element_type=jnp.float32).astype(jnp.int32)
    return jnp.sum(jnp.where(onehot, rank[:, None, :], 0), axis=2)


def reduce_grads_dp(grad_half, width):
    ndp = lax.axis_size("dp")
    if ndp != 2:
        grads = jnp.concatenate([grad_half(h) for h in range(ndp)], axis=0)
        return reduce_grads(grads, width)
    d = lax.axis_index("dp")
    sent = lax.ppermute(grad_half(1 - d).astype(jnp.bfloat16), "dp", [(0, 1), (1, 0)])
    summed = grad_half(d) + sent.astype(jnp.float32)
    return summed.reshape(1, summed.shape[0], 3, width)


def local_gather(tokens, masked, importance, routes, gates, cotangent, w_gate, w_up, w_down):
    tok_rows = tokens.shape[0]
    width = tokens.shape[1]
    topk = routes.shape[1]
    ncore = lax.axis_size("core")
    nchip = lax.axis_size("ez")
    experts = nchip * ncore
    capacity = min(tok_rows, 3 * tok_rows * topk // (2 * experts))
    core = lax.axis_index("core")
    me = lax.axis_index("ez") * ncore + core
    coef = importance * masked.astype(jnp.float32)
    factor = coef[:, None] * gates
    meta = [routes.astype(jnp.bfloat16)] + exact_pieces(factor) + exact_pieces(gates)
    meta_rows = jnp.concatenate([m.T for m in meta], axis=0)
    lines = -(-meta_rows.size // width)
    lines += (-(tok_rows + lines)) % 8
    flat_meta = jnp.pad(meta_rows.reshape(-1), (0, lines * width - meta_rows.size))
    packed = jnp.concatenate([tokens, flat_meta.reshape(lines, width)], axis=0)

    gathered = lax.all_gather(packed, ("ez", "core"), axis=0, tiled=True)
    gathered = gathered.reshape(experts, tok_rows + lines, width)
    finish_cot = ring_gather(cotangent)
    on_core0 = core == 0
    meta_all = gathered[:, tok_rows:].reshape(experts, lines * width)
    meta_all = meta_all[:, :meta_rows.size].reshape(experts, len(meta), topk, tok_rows)
    routes_t = meta_all[:, 0].astype(jnp.int32)
    hit = routes_t == me
    zero = jnp.zeros((), jnp.float32)
    fac = jnp.sum(jnp.where(hit, joined([meta_all[:, i] for i in (1, 2, 3)]), zero), axis=1)
    gate_t = joined([meta_all[:, i] for i in (4, 5, 6)])
    routed = jnp.any(hit, axis=1)
    ahead = (
        lax.broadcasted_iota(jnp.int32, (tok_rows, tok_rows), 0)
        < lax.broadcasted_iota(jnp.int32, (tok_rows, tok_rows), 1)
    ).astype(jnp.bfloat16)
    rank = jnp.dot(
        routed.astype(jnp.bfloat16), ahead, preferred_element_type=jnp.float32
    ).astype(jnp.int32)
    slot_ids = lax.broadcasted_iota(jnp.int32, (experts, capacity, tok_rows), 1)
    pick = (routed[:, None, :] & (rank[:, None, :] == slot_ids)).astype(jnp.bfloat16)

    rows_x = jnp.einsum(
        "sjt,std->sjd",
        pick,
        gathered[:, :tok_rows],
        preferred_element_type=jnp.float32,
    ).astype(jnp.bfloat16).reshape(experts * capacity, width)
    cot_halves = finish_cot(rows_x)
    cot_by_core = [
        jnp.where(on_core0, cot_halves[0], cot_halves[1]),
        jnp.where(on_core0, cot_halves[1], cot_halves[0]),
    ]
    pick_by_core = pick.reshape(nchip, ncore, capacity, tok_rows)
    fac_by_core = fac.reshape(nchip, ncore, tok_rows)
    rows_q = []
    for k in range(ncore):
        scaled = fac_by_core[:, k, :, None] * cot_by_core[k].reshape(
            nchip, tok_rows, width
        ).astype(jnp.float32)
        rows_q.append(
            jnp.einsum(
                "sjt,std->sjd",
                pick_by_core[:, k],
                scaled.astype(jnp.bfloat16),
                preferred_element_type=jnp.float32,
            ).astype(jnp.bfloat16)
        )
    rows_q = jnp.stack(rows_q, axis=1).reshape(experts * capacity, width)
    wgate, wup, wdown = w_gate[0], w_up[0], w_down[0]
    gate_pre = contract_cols(rows_x, wgate)
    up_pre = contract_cols(rows_x, wup)
    sig = jax.nn.sigmoid(gate_pre)
    act = gate_pre * sig
    hidden = (act * up_pre).astype(jnp.bfloat16)
    expert_out = jnp.dot(hidden, wdown, preferred_element_type=jnp.float32).astype(
        jnp.bfloat16
    )

    pick_k = pick.reshape(nchip, ncore, capacity, tok_rows)
    out_k = expert_out.reshape(nchip, ncore, capacity, width)
    def dense_for(k):
        return jnp.einsum(
            "sjt,sjd->std",
            lax.dynamic_index_in_dim(pick_k, k, 1, keepdims=False),
            lax.dynamic_index_in_dim(out_k, k, 1, keepdims=False),
            preferred_element_type=jnp.float32,
        ).astype(jnp.bfloat16)

    from_partner = lax.ppermute(dense_for(1 - core), "core", [(0, 1), (1, 0)])
    mine = dense_for(core)
    gate_all = gate_t.reshape(nchip, ncore, topk, tok_rows)
    routes_all = routes_t.reshape(nchip, ncore, topk, tok_rows)
    gate_own = jnp.where(on_core0, gate_all[:, 0], gate_all[:, 1])
    routes_own = jnp.where(on_core0, routes_all[:, 0], routes_all[:, 1])
    gte = jnp.sum(jnp.where(routes_own == me, gate_own, zero), axis=1)
    gte_partner = jnp.sum(jnp.where(routes_own == (me ^ 1), gate_own, zero), axis=1)
    combined = (
        gte[:, :, None] * mine.astype(jnp.float32)
        + gte_partner[:, :, None] * from_partner.astype(jnp.float32)
    ).astype(jnp.bfloat16)
    returned = lax.all_to_all(combined, "ez", 0, 0, tiled=True)

    back = contract_cols(rows_q, wdown)
    d_gate = (back * up_pre * sig * (1.0 + gate_pre * (1.0 - sig))).astype(jnp.bfloat16)
    d_up = (back * act).astype(jnp.bfloat16)
    share = d_gate.shape[1] // lax.axis_size("dp")

    def grad_half(h):
        def part(v):
            return lax.dynamic_slice_in_dim(v, h * share, share, axis=1)

        return jnp.stack(
            [
                contract_rows(part(d_gate), rows_x),
                contract_rows(part(d_up), rows_x),
                contract_rows(part(hidden), rows_q),
            ],
            axis=1,
        )

    weight_grads = reduce_grads_dp(grad_half, width)

    summed = jnp.sum(returned.astype(jnp.float32), axis=0)
    return summed.astype(jnp.bfloat16), weight_grads


def specs(rows, experts):
    return (
        (P(rows, None), P(rows), P(rows), P(rows, None), P(rows, None), P(rows, None))
        + (P(experts, None, None),) * 3,
        (P(rows, None), P(experts, "dp", None, None)),
    )


def solution(mesh):
    ndp, nexp = mesh.shape["dp"], mesh.shape["expert"]
    split = jax.sharding.Mesh(mesh.devices.reshape(ndp, nexp // 2, 2), ("dp", "ez", "core"))
    ins, outs = specs(("dp", "ez", "core"), ("ez", "core"))
    gathered = jax.shard_map(local_gather, mesh=split, in_specs=ins, out_specs=outs, check_vma=False)
    ins, outs = specs(("dp", "expert"), "expert")
    routed = jax.shard_map(local_a2a, mesh=mesh, in_specs=ins, out_specs=outs, check_vma=False)

    def run(*args):
        if args[0].shape[0] // ndp <= GATHER_ROWS:
            return gathered(*args)
        return routed(*args)

    return run
```

```python
import jax
import jax.numpy as jnp
from jax import lax
from jax.sharding import PartitionSpec as P

GATHER_ROWS = 2048


def contract_rows(left, right):
    return lax.dot_general(
        left, right, (((0,), (0,)), ((), ())), preferred_element_type=jnp.float32
    )


def contract_cols(left, right):
    return lax.dot_general(
        left, right, (((1,), (1,)), ((), ())), preferred_element_type=jnp.float32
    )


def expert_math(rows_x, rows_q, wgate, wup, wdown):
    gate_pre = contract_cols(rows_x, wgate)
    up_pre = contract_cols(rows_x, wup)
    sig = jax.nn.sigmoid(gate_pre)
    act = gate_pre * sig
    hidden = (act * up_pre).astype(jnp.bfloat16)
    expert_out = jnp.dot(hidden, wdown, preferred_element_type=jnp.float32).astype(
        jnp.bfloat16
    )
    back = contract_cols(rows_q, wdown)
    d_gate = (back * up_pre * sig * (1.0 + gate_pre * (1.0 - sig))).astype(jnp.bfloat16)
    d_up = (back * act).astype(jnp.bfloat16)
    grad_gate = contract_rows(d_gate, rows_x)
    grad_up = contract_rows(d_up, rows_x)
    grad_down = contract_rows(hidden, rows_q)
    return expert_out, jnp.stack([grad_gate, grad_up, grad_down], axis=1)


def reduce_grads(grads, width):
    share = grads.shape[0] // lax.axis_size("dp")
    summed = lax.psum_scatter(grads, "dp", scatter_dimension=0, tiled=True)
    return summed.reshape(1, share, 3, width)


def source_slots(routes, experts):
    flat = routes.reshape(-1)
    onehot = (flat[:, None] == jnp.arange(experts, dtype=jnp.int32)[None, :]).astype(jnp.int32)
    before = jnp.cumsum(onehot, axis=0) - onehot
    return flat, jnp.sum(before * onehot, axis=1)


def local_a2a(tokens, masked, importance, routes, gates, cotangent, w_gate, w_up, w_down):
    tok_rows = tokens.shape[0]
    width = tokens.shape[1]
    topk = routes.shape[1]
    experts = lax.axis_size("expert")
    capacity = min(tok_rows, 3 * tok_rows * topk // (2 * experts))
    flat, slots = source_slots(routes, experts)
    target = flat * capacity + slots
    owner = jnp.arange(tok_rows * topk, dtype=jnp.int32) // topk
    coef = importance * masked.astype(jnp.float32)
    factor = (coef[:, None] * gates).reshape(-1)
    sent_x = jnp.zeros((experts * capacity, width), jnp.bfloat16).at[target].set(tokens[owner])
    scaled = (factor[:, None] * cotangent[owner].astype(jnp.float32)).astype(jnp.bfloat16)
    sent_q = jnp.zeros((experts * capacity, width), jnp.bfloat16).at[target].set(scaled)
    layout = (experts, capacity, width)
    recv_x = lax.all_to_all(sent_x.reshape(layout), "expert", 0, 0, tiled=True)
    recv_q = lax.all_to_all(sent_q.reshape(layout), "expert", 0, 0, tiled=True)
    expert_out, grads = expert_math(
        recv_x.reshape(-1, width), recv_q.reshape(-1, width), w_gate[0], w_up[0], w_down[0]
    )
    returned = lax.all_to_all(expert_out.reshape(layout), "expert", 0, 0, tiled=True)
    picked = returned.reshape(-1, width)[target].astype(jnp.float32)
    summed = jnp.sum(picked.reshape(tok_rows, topk, width) * gates[:, :, None], axis=1)
    return summed.astype(jnp.bfloat16), reduce_grads(grads, width)


def exact_pieces(values):
    high = lax.reduce_precision(values, exponent_bits=8, mantissa_bits=7)
    rest = values - high
    middle = lax.reduce_precision(rest, exponent_bits=8, mantissa_bits=7)
    low = rest - middle
    return [part.astype(jnp.bfloat16) for part in (high, middle, low)]


def joined(pieces):
    total = pieces[0].astype(jnp.float32) + pieces[1].astype(jnp.float32)
    return total + pieces[2].astype(jnp.float32)


def gather_replica(values):
    mine = lax.all_gather(values, "ez", axis=0, tiled=True)
    return [mine, lax.ppermute(mine, "core", [(0, 1), (1, 0)])]


def ring_gather(block):
    n = lax.axis_size("ez")
    order = [2 * i for i in range(n // 2)] + [2 * i + 1 for i in reversed(range(n // 2))]
    if n % 2:
        order = list(range(n))
    place = [0] * n
    for p, c in enumerate(order):
        place[c] = p
    me = lax.axis_index("ez")
    at = jnp.asarray(place, jnp.int32)[me]
    ring = jnp.asarray(order, jnp.int32)
    out = jnp.zeros((n,) + block.shape, block.dtype)
    out = lax.dynamic_update_index_in_dim(out, block, me, 0)
    ahead = [(order[i], order[(i + 1) % n]) for i in range(n)]
    behind = [(order[i], order[(i - 1) % n]) for i in range(n)]
    up, down = block, block
    for step in range(1, n // 2 + 1):
        up = lax.ppermute(up, "ez", ahead)
        out = lax.dynamic_update_index_in_dim(out, up, ring[(at - step) % n], 0)
        if step <= (n - 1) // 2:
            down = lax.ppermute(down, "ez", behind)
            out = lax.dynamic_update_index_in_dim(out, down, ring[(at + step) % n], 0)
    mine = out.reshape((n * block.shape[0],) + block.shape[1:])
    return [mine, lax.ppermute(mine, "core", [(0, 1), (1, 0)])]


def slots_by_rank(routes, experts):
    tok_rows = routes.shape[0]
    onehot = routes[:, :, None] == lax.broadcasted_iota(jnp.int32, (1, 1, experts), 2)
    hits = jnp.any(onehot, axis=1).astype(jnp.bfloat16)
    before = (
        lax.broadcasted_iota(jnp.int32, (tok_rows, tok_rows), 0)
        > lax.broadcasted_iota(jnp.int32, (tok_rows, tok_rows), 1)
    ).astype(jnp.bfloat16)
    rank = jnp.dot(before, hits, preferred_element_type=jnp.float32).astype(jnp.int32)
    return jnp.sum(jnp.where(onehot, rank[:, None, :], 0), axis=2)


def reduce_grads_dp(grad_half, width):
    ndp = lax.axis_size("dp")
    if ndp != 2:
        grads = jnp.concatenate([grad_half(h) for h in range(ndp)], axis=0)
        return reduce_grads(grads, width)
    d = lax.axis_index("dp")
    sent = lax.ppermute(grad_half(1 - d).astype(jnp.bfloat16), "dp", [(0, 1), (1, 0)])
    summed = grad_half(d) + sent.astype(jnp.float32)
    return summed.reshape(1, summed.shape[0], 3, width)


def local_gather(tokens, masked, importance, routes, gates, cotangent, w_gate, w_up, w_down):
    tok_rows = tokens.shape[0]
    width = tokens.shape[1]
    topk = routes.shape[1]
    ncore = lax.axis_size("core")
    nchip = lax.axis_size("ez")
    experts = nchip * ncore
    capacity = min(tok_rows, 3 * tok_rows * topk // (2 * experts))
    core = lax.axis_index("core")
    me = lax.axis_index("ez") * ncore + core
    coef = importance * masked.astype(jnp.float32)
    factor = coef[:, None] * gates
    meta = [routes.astype(jnp.bfloat16)] + exact_pieces(factor) + exact_pieces(gates)
    meta_rows = jnp.concatenate([m.T for m in meta], axis=0)
    lines = -(-meta_rows.size // width)
    lines += (-(tok_rows + lines)) % 8
    flat_meta = jnp.pad(meta_rows.reshape(-1), (0, lines * width - meta_rows.size))
    packed = jnp.concatenate([tokens, flat_meta.reshape(lines, width)], axis=0)

    gathered = lax.all_gather(packed, ("ez", "core"), axis=0, tiled=True)
    gathered = gathered.reshape(experts, tok_rows + lines, width)
    cot_halves = ring_gather(cotangent)
    on_core0 = core == 0
    meta_all = gathered[:, tok_rows:].reshape(experts, lines * width)
    meta_all = meta_all[:, :meta_rows.size].reshape(experts, len(meta), topk, tok_rows)
    routes_t = meta_all[:, 0].astype(jnp.int32)
    hit = routes_t == me
    zero = jnp.zeros((), jnp.float32)
    fac = jnp.sum(jnp.where(hit, joined([meta_all[:, i] for i in (1, 2, 3)]), zero), axis=1)
    gate_t = joined([meta_all[:, i] for i in (4, 5, 6)])
    routed = jnp.any(hit, axis=1)
    ahead = (
        lax.broadcasted_iota(jnp.int32, (tok_rows, tok_rows), 0)
        < lax.broadcasted_iota(jnp.int32, (tok_rows, tok_rows), 1)
    ).astype(jnp.bfloat16)
    rank = jnp.dot(
        routed.astype(jnp.bfloat16), ahead, preferred_element_type=jnp.float32
    ).astype(jnp.int32)
    slot_ids = lax.broadcasted_iota(jnp.int32, (experts, capacity, tok_rows), 1)
    pick = (routed[:, None, :] & (rank[:, None, :] == slot_ids)).astype(jnp.bfloat16)

    rows_x = jnp.einsum(
        "sjt,std->sjd",
        pick,
        gathered[:, :tok_rows],
        preferred_element_type=jnp.float32,
    ).astype(jnp.bfloat16).reshape(experts * capacity, width)
    pick_by_core = pick.reshape(nchip, ncore, capacity, tok_rows)
    fac_by_core = fac.reshape(nchip, ncore, tok_rows)
    core_ids = lax.broadcasted_iota(jnp.int32, (1, ncore, 1, 1), 1)
    rows_q = 0.0
    for h, half in enumerate(cot_halves):
        k = h ^ core
        scaled = lax.dynamic_index_in_dim(fac_by_core, k, 1, keepdims=False)[:, :, None] * half.reshape(
            nchip, tok_rows, width
        ).astype(jnp.float32)
        masked_pick = jnp.where(core_ids == k, pick_by_core, jnp.zeros((), pick_by_core.dtype))
        rows_q = rows_q + jnp.einsum(
            "ikjt,itd->ikjd",
            masked_pick,
            scaled.astype(jnp.bfloat16),
            preferred_element_type=jnp.float32,
        )
    rows_q = rows_q.astype(jnp.bfloat16).reshape(experts * capacity, width)
    wgate, wup, wdown = w_gate[0], w_up[0], w_down[0]
    gate_pre = contract_cols(rows_x, wgate)
    up_pre = contract_cols(rows_x, wup)
    sig = jax.nn.sigmoid(gate_pre)
    act = gate_pre * sig
    hidden = (act * up_pre).astype(jnp.bfloat16)
    expert_out = jnp.dot(hidden, wdown, preferred_element_type=jnp.float32).astype(
        jnp.bfloat16
    )

    pick_k = pick.reshape(nchip, ncore, capacity, tok_rows)
    out_k = expert_out.reshape(nchip, ncore, capacity, width)
    def dense_for(k):
        return jnp.einsum(
            "sjt,sjd->std",
            lax.dynamic_index_in_dim(pick_k, k, 1, keepdims=False),
            lax.dynamic_index_in_dim(out_k, k, 1, keepdims=False),
            preferred_element_type=jnp.float32,
        ).astype(jnp.bfloat16)

    from_partner = lax.ppermute(dense_for(1 - core), "core", [(0, 1), (1, 0)])
    mine = dense_for(core)
    gate_all = gate_t.reshape(nchip, ncore, topk, tok_rows)
    routes_all = routes_t.reshape(nchip, ncore, topk, tok_rows)
    gate_own = jnp.where(on_core0, gate_all[:, 0], gate_all[:, 1])
    routes_own = jnp.where(on_core0, routes_all[:, 0], routes_all[:, 1])
    gte = jnp.sum(jnp.where(routes_own == me, gate_own, zero), axis=1)
    gte_partner = jnp.sum(jnp.where(routes_own == (me ^ 1), gate_own, zero), axis=1)
    combined = (
        gte[:, :, None] * mine.astype(jnp.float32)
        + gte_partner[:, :, None] * from_partner.astype(jnp.float32)
    ).astype(jnp.bfloat16)
    returned = lax.all_to_all(combined, "ez", 0, 0, tiled=True)

    back = contract_cols(rows_q, wdown)
    d_gate = (back * up_pre * sig * (1.0 + gate_pre * (1.0 - sig))).astype(jnp.bfloat16)
    d_up = (back * act).astype(jnp.bfloat16)
    share = d_gate.shape[1] // lax.axis_size("dp")

    def grad_half(h):
        def part(v):
            return lax.dynamic_slice_in_dim(v, h * share, share, axis=1)

        return jnp.stack(
            [
                contract_rows(part(d_gate), rows_x),
                contract_rows(part(d_up), rows_x),
                contract_rows(part(hidden), rows_q),
            ],
            axis=1,
        )

    weight_grads = reduce_grads_dp(grad_half, width)

    summed = jnp.sum(returned.astype(jnp.float32), axis=0)
    return summed.astype(jnp.bfloat16), weight_grads


def specs(rows, experts):
    return (
        (P(rows, None), P(rows), P(rows), P(rows, None), P(rows, None), P(rows, None))
        + (P(experts, None, None),) * 3,
        (P(rows, None), P(experts, "dp", None, None)),
    )


def solution(mesh):
    ndp, nexp = mesh.shape["dp"], mesh.shape["expert"]
    split = jax.sharding.Mesh(mesh.devices.reshape(ndp, nexp // 2, 2), ("dp", "ez", "core"))
    ins, outs = specs(("dp", "ez", "core"), ("ez", "core"))
    gathered = jax.shard_map(local_gather, mesh=split, in_specs=ins, out_specs=outs, check_vma=False)
    ins, outs = specs(("dp", "expert"), "expert")
    routed = jax.shard_map(local_a2a, mesh=mesh, in_specs=ins, out_specs=outs, check_vma=False)

    def run(*args):
        if args[0].shape[0] // ndp <= GATHER_ROWS:
            return gathered(*args)
        return routed(*args)

    return run
```

```python
import jax
import jax.numpy as jnp
from jax import lax
from jax.sharding import PartitionSpec as P

GATHER_ROWS = 2048


def contract_rows(left, right):
    return lax.dot_general(
        left, right, (((0,), (0,)), ((), ())), preferred_element_type=jnp.float32
    )


def contract_cols(left, right):
    return lax.dot_general(
        left, right, (((1,), (1,)), ((), ())), preferred_element_type=jnp.float32
    )


def expert_math(rows_x, rows_q, wgate, wup, wdown):
    gate_pre = contract_cols(rows_x, wgate)
    up_pre = contract_cols(rows_x, wup)
    sig = jax.nn.sigmoid(gate_pre)
    act = gate_pre * sig
    hidden = (act * up_pre).astype(jnp.bfloat16)
    expert_out = jnp.dot(hidden, wdown, preferred_element_type=jnp.float32).astype(
        jnp.bfloat16
    )
    back = contract_cols(rows_q, wdown)
    d_gate = (back * up_pre * sig * (1.0 + gate_pre * (1.0 - sig))).astype(jnp.bfloat16)
    d_up = (back * act).astype(jnp.bfloat16)
    grad_gate = contract_rows(d_gate, rows_x)
    grad_up = contract_rows(d_up, rows_x)
    grad_down = contract_rows(hidden, rows_q)
    return expert_out, jnp.stack([grad_gate, grad_up, grad_down], axis=1)


def reduce_grads(grads, width):
    share = grads.shape[0] // lax.axis_size("dp")
    summed = lax.psum_scatter(grads, "dp", scatter_dimension=0, tiled=True)
    return summed.reshape(1, share, 3, width)


def source_slots(routes, experts):
    flat = routes.reshape(-1)
    onehot = (flat[:, None] == jnp.arange(experts, dtype=jnp.int32)[None, :]).astype(jnp.int32)
    before = jnp.cumsum(onehot, axis=0) - onehot
    return flat, jnp.sum(before * onehot, axis=1)


def local_a2a(tokens, masked, importance, routes, gates, cotangent, w_gate, w_up, w_down):
    tok_rows = tokens.shape[0]
    width = tokens.shape[1]
    topk = routes.shape[1]
    experts = lax.axis_size("expert")
    capacity = min(tok_rows, 3 * tok_rows * topk // (2 * experts))
    flat, slots = source_slots(routes, experts)
    target = flat * capacity + slots
    owner = jnp.arange(tok_rows * topk, dtype=jnp.int32) // topk
    coef = importance * masked.astype(jnp.float32)
    factor = (coef[:, None] * gates).reshape(-1)
    sent_x = jnp.zeros((experts * capacity, width), jnp.bfloat16).at[target].set(tokens[owner])
    scaled = (factor[:, None] * cotangent[owner].astype(jnp.float32)).astype(jnp.bfloat16)
    sent_q = jnp.zeros((experts * capacity, width), jnp.bfloat16).at[target].set(scaled)
    layout = (experts, capacity, width)
    recv_x = lax.all_to_all(sent_x.reshape(layout), "expert", 0, 0, tiled=True)
    recv_q = lax.all_to_all(sent_q.reshape(layout), "expert", 0, 0, tiled=True)
    expert_out, grads = expert_math(
        recv_x.reshape(-1, width), recv_q.reshape(-1, width), w_gate[0], w_up[0], w_down[0]
    )
    returned = lax.all_to_all(expert_out.reshape(layout), "expert", 0, 0, tiled=True)
    picked = returned.reshape(-1, width)[target].astype(jnp.float32)
    summed = jnp.sum(picked.reshape(tok_rows, topk, width) * gates[:, :, None], axis=1)
    return summed.astype(jnp.bfloat16), reduce_grads(grads, width)


def exact_pieces(values):
    high = lax.reduce_precision(values, exponent_bits=8, mantissa_bits=7)
    rest = values - high
    middle = lax.reduce_precision(rest, exponent_bits=8, mantissa_bits=7)
    low = rest - middle
    return [part.astype(jnp.bfloat16) for part in (high, middle, low)]


def joined(pieces):
    total = pieces[0].astype(jnp.float32) + pieces[1].astype(jnp.float32)
    return total + pieces[2].astype(jnp.float32)


def gather_replica(values):
    mine = lax.all_gather(values, "ez", axis=0, tiled=True)
    return [mine, lax.ppermute(mine, "core", [(0, 1), (1, 0)])]


def ring_gather(block):
    n = lax.axis_size("ez")
    order = [2 * i for i in range(n // 2)] + [2 * i + 1 for i in reversed(range(n // 2))]
    if n % 2:
        order = list(range(n))
    place = [0] * n
    for p, c in enumerate(order):
        place[c] = p
    me = lax.axis_index("ez")
    at = jnp.asarray(place, jnp.int32)[me]
    ring = jnp.asarray(order, jnp.int32)
    out = jnp.zeros((n,) + block.shape, block.dtype)
    out = lax.dynamic_update_index_in_dim(out, block, me, 0)
    ahead = [(order[i], order[(i + 1) % n]) for i in range(n)]
    behind = [(order[i], order[(i - 1) % n]) for i in range(n)]
    up, down = block, block
    for step in range(1, n // 2 + 1):
        up = lax.ppermute(up, "ez", ahead)
        out = lax.dynamic_update_index_in_dim(out, up, ring[(at - step) % n], 0)
        if step <= (n - 1) // 2:
            down = lax.ppermute(down, "ez", behind)
            out = lax.dynamic_update_index_in_dim(out, down, ring[(at + step) % n], 0)
    mine = out.reshape((n * block.shape[0],) + block.shape[1:])
    return [mine, lax.ppermute(mine, "core", [(0, 1), (1, 0)])]


def slots_by_rank(routes, experts):
    tok_rows = routes.shape[0]
    onehot = routes[:, :, None] == lax.broadcasted_iota(jnp.int32, (1, 1, experts), 2)
    hits = jnp.any(onehot, axis=1).astype(jnp.bfloat16)
    before = (
        lax.broadcasted_iota(jnp.int32, (tok_rows, tok_rows), 0)
        > lax.broadcasted_iota(jnp.int32, (tok_rows, tok_rows), 1)
    ).astype(jnp.bfloat16)
    rank = jnp.dot(before, hits, preferred_element_type=jnp.float32).astype(jnp.int32)
    return jnp.sum(jnp.where(onehot, rank[:, None, :], 0), axis=2)


def reduce_grads_dp(grad_half, width):
    ndp = lax.axis_size("dp")
    if ndp != 2:
        grads = jnp.concatenate([grad_half(h) for h in range(ndp)], axis=0)
        return reduce_grads(grads, width)
    d = lax.axis_index("dp")
    sent = lax.ppermute(grad_half(1 - d).astype(jnp.bfloat16), "dp", [(0, 1), (1, 0)])
    summed = grad_half(d) + sent.astype(jnp.float32)
    return summed.reshape(1, summed.shape[0], 3, width)


def local_gather(tokens, masked, importance, routes, gates, cotangent, w_gate, w_up, w_down):
    tok_rows = tokens.shape[0]
    width = tokens.shape[1]
    topk = routes.shape[1]
    ncore = lax.axis_size("core")
    nchip = lax.axis_size("ez")
    experts = nchip * ncore
    capacity = min(tok_rows, 3 * tok_rows * topk // (2 * experts))
    core = lax.axis_index("core")
    me = lax.axis_index("ez") * ncore + core
    coef = importance * masked.astype(jnp.float32)
    factor = coef[:, None] * gates
    meta = [routes.astype(jnp.bfloat16)] + exact_pieces(factor) + exact_pieces(gates)
    meta_rows = jnp.concatenate([m.T for m in meta], axis=0)
    lines = -(-meta_rows.size // width)
    lines += (-(tok_rows + lines)) % 8
    flat_meta = jnp.pad(meta_rows.reshape(-1), (0, lines * width - meta_rows.size))
    packed = jnp.concatenate([tokens, flat_meta.reshape(lines, width)], axis=0)

    gathered = lax.all_gather(packed, ("ez", "core"), axis=0, tiled=True)
    gathered = gathered.reshape(experts, tok_rows + lines, width)
    cot_halves = ring_gather(cotangent)
    on_core0 = core == 0
    meta_all = gathered[:, tok_rows:].reshape(experts, lines * width)
    meta_all = meta_all[:, :meta_rows.size].reshape(experts, len(meta), topk, tok_rows)
    routes_t = meta_all[:, 0].astype(jnp.int32)
    hit = routes_t == me
    zero = jnp.zeros((), jnp.float32)
    fac = jnp.sum(jnp.where(hit, joined([meta_all[:, i] for i in (1, 2, 3)]), zero), axis=1)
    gate_t = joined([meta_all[:, i] for i in (4, 5, 6)])
    routed = jnp.any(hit, axis=1)
    ahead = (
        lax.broadcasted_iota(jnp.int32, (tok_rows, tok_rows), 0)
        < lax.broadcasted_iota(jnp.int32, (tok_rows, tok_rows), 1)
    ).astype(jnp.bfloat16)
    rank = jnp.dot(
        routed.astype(jnp.bfloat16), ahead, preferred_element_type=jnp.float32
    ).astype(jnp.int32)
    slot_ids = lax.broadcasted_iota(jnp.int32, (experts, capacity, tok_rows), 1)
    pick = (routed[:, None, :] & (rank[:, None, :] == slot_ids)).astype(jnp.bfloat16)

    rows_x = jnp.einsum(
        "sjt,std->sjd",
        pick,
        gathered[:, :tok_rows],
        preferred_element_type=jnp.float32,
    ).astype(jnp.bfloat16).reshape(experts * capacity, width)
    wgate, wup, wdown = w_gate[0], w_up[0], w_down[0]
    gate_pre = contract_cols(rows_x, wgate)
    up_pre = contract_cols(rows_x, wup)
    sig = jax.nn.sigmoid(gate_pre)
    act = gate_pre * sig
    hidden = (act * up_pre).astype(jnp.bfloat16)
    expert_out = jnp.dot(hidden, wdown, preferred_element_type=jnp.float32).astype(
        jnp.bfloat16
    )

    pick_k = pick.reshape(nchip, ncore, capacity, tok_rows)
    out_k = expert_out.reshape(nchip, ncore, capacity, width)
    def dense_for(k):
        return jnp.einsum(
            "sjt,sjd->std",
            lax.dynamic_index_in_dim(pick_k, k, 1, keepdims=False),
            lax.dynamic_index_in_dim(out_k, k, 1, keepdims=False),
            preferred_element_type=jnp.float32,
        ).astype(jnp.bfloat16)

    from_partner = lax.ppermute(dense_for(1 - core), "core", [(0, 1), (1, 0)])
    mine = dense_for(core)
    gate_all = gate_t.reshape(nchip, ncore, topk, tok_rows)
    routes_all = routes_t.reshape(nchip, ncore, topk, tok_rows)
    gate_own = jnp.where(on_core0, gate_all[:, 0], gate_all[:, 1])
    routes_own = jnp.where(on_core0, routes_all[:, 0], routes_all[:, 1])
    gte = jnp.sum(jnp.where(routes_own == me, gate_own, zero), axis=1)
    gte_partner = jnp.sum(jnp.where(routes_own == (me ^ 1), gate_own, zero), axis=1)
    combined = (
        gte[:, :, None] * mine.astype(jnp.float32)
        + gte_partner[:, :, None] * from_partner.astype(jnp.float32)
    ).astype(jnp.bfloat16)
    returned = lax.all_to_all(combined, "ez", 0, 0, tiled=True)

    cot_halves, _ = lax.optimization_barrier((cot_halves, expert_out))
    pick_by_core = pick.reshape(nchip, ncore, capacity, tok_rows)
    fac_by_core = fac.reshape(nchip, ncore, tok_rows)
    core_ids = lax.broadcasted_iota(jnp.int32, (1, ncore, 1, 1), 1)
    rows_q = 0.0
    for h, half in enumerate(cot_halves):
        k = h ^ core
        scaled = lax.dynamic_index_in_dim(fac_by_core, k, 1, keepdims=False)[:, :, None] * half.reshape(
            nchip, tok_rows, width
        ).astype(jnp.float32)
        masked_pick = jnp.where(core_ids == k, pick_by_core, jnp.zeros((), pick_by_core.dtype))
        rows_q = rows_q + jnp.einsum(
            "ikjt,itd->ikjd",
            masked_pick,
            scaled.astype(jnp.bfloat16),
            preferred_element_type=jnp.float32,
        )
    rows_q = rows_q.astype(jnp.bfloat16).reshape(experts * capacity, width)
    back = contract_cols(rows_q, wdown)
    d_gate = (back * up_pre * sig * (1.0 + gate_pre * (1.0 - sig))).astype(jnp.bfloat16)
    d_up = (back * act).astype(jnp.bfloat16)
    share = d_gate.shape[1] // lax.axis_size("dp")

    def grad_half(h):
        def part(v):
            return lax.dynamic_slice_in_dim(v, h * share, share, axis=1)

        return jnp.stack(
            [
                contract_rows(part(d_gate), rows_x),
                contract_rows(part(d_up), rows_x),
                contract_rows(part(hidden), rows_q),
            ],
            axis=1,
        )

    weight_grads = reduce_grads_dp(grad_half, width)

    summed = jnp.sum(returned.astype(jnp.float32), axis=0)
    return summed.astype(jnp.bfloat16), weight_grads


def specs(rows, experts):
    return (
        (P(rows, None), P(rows), P(rows), P(rows, None), P(rows, None), P(rows, None))
        + (P(experts, None, None),) * 3,
        (P(rows, None), P(experts, "dp", None, None)),
    )


def solution(mesh):
    ndp, nexp = mesh.shape["dp"], mesh.shape["expert"]
    split = jax.sharding.Mesh(mesh.devices.reshape(ndp, nexp // 2, 2), ("dp", "ez", "core"))
    ins, outs = specs(("dp", "ez", "core"), ("ez", "core"))
    gathered = jax.shard_map(local_gather, mesh=split, in_specs=ins, out_specs=outs, check_vma=False)
    ins, outs = specs(("dp", "expert"), "expert")
    routed = jax.shard_map(local_a2a, mesh=mesh, in_specs=ins, out_specs=outs, check_vma=False)

    def run(*args):
        if args[0].shape[0] // ndp <= GATHER_ROWS:
            return gathered(*args)
        return routed(*args)

    return run
```

```python
import jax
import jax.numpy as jnp
from jax import lax
from jax.sharding import PartitionSpec as P

GATHER_ROWS = 2048


def contract_rows(left, right):
    return lax.dot_general(
        left, right, (((0,), (0,)), ((), ())), preferred_element_type=jnp.float32
    )


def contract_cols(left, right):
    return lax.dot_general(
        left, right, (((1,), (1,)), ((), ())), preferred_element_type=jnp.float32
    )


def expert_math(rows_x, rows_q, wgate, wup, wdown):
    gate_pre = contract_cols(rows_x, wgate)
    up_pre = contract_cols(rows_x, wup)
    sig = jax.nn.sigmoid(gate_pre)
    act = gate_pre * sig
    hidden = (act * up_pre).astype(jnp.bfloat16)
    expert_out = jnp.dot(hidden, wdown, preferred_element_type=jnp.float32).astype(
        jnp.bfloat16
    )
    back = contract_cols(rows_q, wdown)
    d_gate = (back * up_pre * sig * (1.0 + gate_pre * (1.0 - sig))).astype(jnp.bfloat16)
    d_up = (back * act).astype(jnp.bfloat16)
    grad_gate = contract_rows(d_gate, rows_x)
    grad_up = contract_rows(d_up, rows_x)
    grad_down = contract_rows(hidden, rows_q)
    return expert_out, jnp.stack([grad_gate, grad_up, grad_down], axis=1)


def reduce_grads(grads, width):
    share = grads.shape[0] // lax.axis_size("dp")
    summed = lax.psum_scatter(grads, "dp", scatter_dimension=0, tiled=True)
    return summed.reshape(1, share, 3, width)


def source_slots(routes, experts):
    flat = routes.reshape(-1)
    onehot = (flat[:, None] == jnp.arange(experts, dtype=jnp.int32)[None, :]).astype(jnp.int32)
    before = jnp.cumsum(onehot, axis=0) - onehot
    return flat, jnp.sum(before * onehot, axis=1)


def local_a2a(tokens, masked, importance, routes, gates, cotangent, w_gate, w_up, w_down):
    tok_rows = tokens.shape[0]
    width = tokens.shape[1]
    topk = routes.shape[1]
    experts = lax.axis_size("expert")
    capacity = min(tok_rows, 3 * tok_rows * topk // (2 * experts))
    flat, slots = source_slots(routes, experts)
    target = flat * capacity + slots
    owner = jnp.arange(tok_rows * topk, dtype=jnp.int32) // topk
    coef = importance * masked.astype(jnp.float32)
    factor = (coef[:, None] * gates).reshape(-1)
    sent_x = jnp.zeros((experts * capacity, width), jnp.bfloat16).at[target].set(tokens[owner])
    scaled = (factor[:, None] * cotangent[owner].astype(jnp.float32)).astype(jnp.bfloat16)
    sent_q = jnp.zeros((experts * capacity, width), jnp.bfloat16).at[target].set(scaled)
    layout = (experts, capacity, width)
    recv_x = lax.all_to_all(sent_x.reshape(layout), "expert", 0, 0, tiled=True)
    recv_q = lax.all_to_all(sent_q.reshape(layout), "expert", 0, 0, tiled=True)
    expert_out, grads = expert_math(
        recv_x.reshape(-1, width), recv_q.reshape(-1, width), w_gate[0], w_up[0], w_down[0]
    )
    returned = lax.all_to_all(expert_out.reshape(layout), "expert", 0, 0, tiled=True)
    picked = returned.reshape(-1, width)[target].astype(jnp.float32)
    summed = jnp.sum(picked.reshape(tok_rows, topk, width) * gates[:, :, None], axis=1)
    return summed.astype(jnp.bfloat16), reduce_grads(grads, width)


def exact_pieces(values):
    high = lax.reduce_precision(values, exponent_bits=8, mantissa_bits=7)
    rest = values - high
    middle = lax.reduce_precision(rest, exponent_bits=8, mantissa_bits=7)
    low = rest - middle
    return [part.astype(jnp.bfloat16) for part in (high, middle, low)]


def joined(pieces):
    total = pieces[0].astype(jnp.float32) + pieces[1].astype(jnp.float32)
    return total + pieces[2].astype(jnp.float32)


def gather_replica(values):
    mine = lax.all_gather(values, "ez", axis=0, tiled=True)
    return [mine, lax.ppermute(mine, "core", [(0, 1), (1, 0)])]


def ring_gather(block):
    n = lax.axis_size("ez")
    order = [2 * i for i in range(n // 2)] + [2 * i + 1 for i in reversed(range(n // 2))]
    if n % 2:
        order = list(range(n))
    place = [0] * n
    for p, c in enumerate(order):
        place[c] = p
    me = lax.axis_index("ez")
    at = jnp.asarray(place, jnp.int32)[me]
    ring = jnp.asarray(order, jnp.int32)
    out = jnp.zeros((n,) + block.shape, block.dtype)
    out = lax.dynamic_update_index_in_dim(out, block, me, 0)
    ahead = [(order[i], order[(i + 1) % n]) for i in range(n)]
    behind = [(order[i], order[(i - 1) % n]) for i in range(n)]
    up, down = block, block
    for step in range(1, n // 2 + 1):
        up = lax.ppermute(up, "ez", ahead)
        out = lax.dynamic_update_index_in_dim(out, up, ring[(at - step) % n], 0)
        if step <= (n - 1) // 2:
            down = lax.ppermute(down, "ez", behind)
            out = lax.dynamic_update_index_in_dim(out, down, ring[(at + step) % n], 0)
    mine = out.reshape((n * block.shape[0],) + block.shape[1:])
    return [mine, lax.ppermute(mine, "core", [(0, 1), (1, 0)])]


def slots_by_rank(routes, experts):
    tok_rows = routes.shape[0]
    onehot = routes[:, :, None] == lax.broadcasted_iota(jnp.int32, (1, 1, experts), 2)
    hits = jnp.any(onehot, axis=1).astype(jnp.bfloat16)
    before = (
        lax.broadcasted_iota(jnp.int32, (tok_rows, tok_rows), 0)
        > lax.broadcasted_iota(jnp.int32, (tok_rows, tok_rows), 1)
    ).astype(jnp.bfloat16)
    rank = jnp.dot(before, hits, preferred_element_type=jnp.float32).astype(jnp.int32)
    return jnp.sum(jnp.where(onehot, rank[:, None, :], 0), axis=2)


def reduce_grads_dp(grad_half, width):
    ndp = lax.axis_size("dp")
    if ndp != 2:
        grads = jnp.concatenate([grad_half(h) for h in range(ndp)], axis=0)
        return reduce_grads(grads, width)
    d = lax.axis_index("dp")
    sent = lax.ppermute(grad_half(1 - d).astype(jnp.bfloat16), "dp", [(0, 1), (1, 0)])
    summed = grad_half(d) + sent.astype(jnp.float32)
    return summed.reshape(1, summed.shape[0], 3, width)


def local_gather(tokens, masked, importance, routes, gates, cotangent, w_gate, w_up, w_down):
    tok_rows = tokens.shape[0]
    width = tokens.shape[1]
    topk = routes.shape[1]
    ncore = lax.axis_size("core")
    nchip = lax.axis_size("ez")
    experts = nchip * ncore
    capacity = min(tok_rows, 3 * tok_rows * topk // (2 * experts))
    core = lax.axis_index("core")
    me = lax.axis_index("ez") * ncore + core
    coef = importance * masked.astype(jnp.float32)
    factor = coef[:, None] * gates
    meta = [routes.astype(jnp.bfloat16)] + exact_pieces(factor) + exact_pieces(gates)
    meta_rows = jnp.concatenate([m.T for m in meta], axis=0)
    lines = -(-meta_rows.size // width)
    lines += (-(tok_rows + lines)) % 8
    flat_meta = jnp.pad(meta_rows.reshape(-1), (0, lines * width - meta_rows.size))
    packed = jnp.concatenate([tokens, flat_meta.reshape(lines, width)], axis=0)

    gathered = lax.all_gather(packed, ("ez", "core"), axis=0, tiled=True)
    gathered = gathered.reshape(experts, tok_rows + lines, width)
    cot_halves = ring_gather(cotangent)
    on_core0 = core == 0
    meta_all = gathered[:, tok_rows:].reshape(experts, lines * width)
    meta_all = meta_all[:, :meta_rows.size].reshape(experts, len(meta), topk, tok_rows)
    routes_t = meta_all[:, 0].astype(jnp.int32)
    hit = routes_t == me
    zero = jnp.zeros((), jnp.float32)
    fac = jnp.sum(jnp.where(hit, joined([meta_all[:, i] for i in (1, 2, 3)]), zero), axis=1)
    gate_t = joined([meta_all[:, i] for i in (4, 5, 6)])
    routed = jnp.any(hit, axis=1)
    ahead = (
        lax.broadcasted_iota(jnp.int32, (tok_rows, tok_rows), 0)
        < lax.broadcasted_iota(jnp.int32, (tok_rows, tok_rows), 1)
    ).astype(jnp.bfloat16)
    rank = jnp.dot(
        routed.astype(jnp.bfloat16), ahead, preferred_element_type=jnp.float32
    ).astype(jnp.int32)
    slot_ids = lax.broadcasted_iota(jnp.int32, (experts, capacity, tok_rows), 1)
    pick = (routed[:, None, :] & (rank[:, None, :] == slot_ids)).astype(jnp.bfloat16)

    rows_x = jnp.einsum(
        "sjt,std->sjd",
        pick,
        gathered[:, :tok_rows],
        preferred_element_type=jnp.float32,
    ).astype(jnp.bfloat16).reshape(experts * capacity, width)
    wgate, wup, wdown = w_gate[0], w_up[0], w_down[0]
    gate_pre = contract_cols(rows_x, wgate)
    up_pre = contract_cols(rows_x, wup)
    sig = jax.nn.sigmoid(gate_pre)
    act = gate_pre * sig
    hidden = (act * up_pre).astype(jnp.bfloat16)
    expert_out = jnp.dot(hidden, wdown, preferred_element_type=jnp.float32).astype(
        jnp.bfloat16
    )

    pick_k = pick.reshape(nchip, ncore, capacity, tok_rows)
    out_k = expert_out.reshape(nchip, ncore, capacity, width)
    def dense_for(k):
        return jnp.einsum(
            "sjt,sjd->std",
            lax.dynamic_index_in_dim(pick_k, k, 1, keepdims=False),
            lax.dynamic_index_in_dim(out_k, k, 1, keepdims=False),
            preferred_element_type=jnp.float32,
        ).astype(jnp.bfloat16)

    from_partner = lax.ppermute(dense_for(1 - core), "core", [(0, 1), (1, 0)])
    mine = dense_for(core)
    gate_all = gate_t.reshape(nchip, ncore, topk, tok_rows)
    routes_all = routes_t.reshape(nchip, ncore, topk, tok_rows)
    gate_own = jnp.where(on_core0, gate_all[:, 0], gate_all[:, 1])
    routes_own = jnp.where(on_core0, routes_all[:, 0], routes_all[:, 1])
    gte = jnp.sum(jnp.where(routes_own == me, gate_own, zero), axis=1)
    gte_partner = jnp.sum(jnp.where(routes_own == (me ^ 1), gate_own, zero), axis=1)
    combined = (
        gte[:, :, None] * mine.astype(jnp.float32)
        + gte_partner[:, :, None] * from_partner.astype(jnp.float32)
    ).astype(jnp.bfloat16)
    returned = lax.all_to_all(combined, "ez", 0, 0, tiled=True)

    cot_halves, _ = lax.optimization_barrier((cot_halves, combined))
    pick_by_core = pick.reshape(nchip, ncore, capacity, tok_rows)
    fac_by_core = fac.reshape(nchip, ncore, tok_rows)
    core_ids = lax.broadcasted_iota(jnp.int32, (1, ncore, 1, 1), 1)
    rows_q = 0.0
    for h, half in enumerate(cot_halves):
        k = h ^ core
        scaled = lax.dynamic_index_in_dim(fac_by_core, k, 1, keepdims=False)[:, :, None] * half.reshape(
            nchip, tok_rows, width
        ).astype(jnp.float32)
        masked_pick = jnp.where(core_ids == k, pick_by_core, jnp.zeros((), pick_by_core.dtype))
        rows_q = rows_q + jnp.einsum(
            "ikjt,itd->ikjd",
            masked_pick,
            scaled.astype(jnp.bfloat16),
            preferred_element_type=jnp.float32,
        )
    rows_q = rows_q.astype(jnp.bfloat16).reshape(experts * capacity, width)
    back = contract_cols(rows_q, wdown)
    d_gate = (back * up_pre * sig * (1.0 + gate_pre * (1.0 - sig))).astype(jnp.bfloat16)
    d_up = (back * act).astype(jnp.bfloat16)
    share = d_gate.shape[1] // lax.axis_size("dp")

    def grad_half(h):
        def part(v):
            return lax.dynamic_slice_in_dim(v, h * share, share, axis=1)

        return jnp.stack(
            [
                contract_rows(part(d_gate), rows_x),
                contract_rows(part(d_up), rows_x),
                contract_rows(part(hidden), rows_q),
            ],
            axis=1,
        )

    weight_grads = reduce_grads_dp(grad_half, width)

    summed = jnp.sum(returned.astype(jnp.float32), axis=0)
    return summed.astype(jnp.bfloat16), weight_grads


def specs(rows, experts):
    return (
        (P(rows, None), P(rows), P(rows), P(rows, None), P(rows, None), P(rows, None))
        + (P(experts, None, None),) * 3,
        (P(rows, None), P(experts, "dp", None, None)),
    )


def solution(mesh):
    ndp, nexp = mesh.shape["dp"], mesh.shape["expert"]
    split = jax.sharding.Mesh(mesh.devices.reshape(ndp, nexp // 2, 2), ("dp", "ez", "core"))
    ins, outs = specs(("dp", "ez", "core"), ("ez", "core"))
    gathered = jax.shard_map(local_gather, mesh=split, in_specs=ins, out_specs=outs, check_vma=False)
    ins, outs = specs(("dp", "expert"), "expert")
    routed = jax.shard_map(local_a2a, mesh=mesh, in_specs=ins, out_specs=outs, check_vma=False)

    def run(*args):
        if args[0].shape[0] // ndp <= GATHER_ROWS:
            return gathered(*args)
        return routed(*args)

    return run
```

```python
import jax
import jax.numpy as jnp
from jax import lax
from jax.sharding import PartitionSpec as P

GATHER_ROWS = 2048


def contract_rows(left, right):
    return lax.dot_general(
        left, right, (((0,), (0,)), ((), ())), preferred_element_type=jnp.float32
    )


def contract_cols(left, right):
    return lax.dot_general(
        left, right, (((1,), (1,)), ((), ())), preferred_element_type=jnp.float32
    )


def expert_math(rows_x, rows_q, wgate, wup, wdown):
    gate_pre = contract_cols(rows_x, wgate)
    up_pre = contract_cols(rows_x, wup)
    sig = jax.nn.sigmoid(gate_pre)
    act = gate_pre * sig
    hidden = (act * up_pre).astype(jnp.bfloat16)
    expert_out = jnp.dot(hidden, wdown, preferred_element_type=jnp.float32).astype(
        jnp.bfloat16
    )
    back = contract_cols(rows_q, wdown)
    d_gate = (back * up_pre * sig * (1.0 + gate_pre * (1.0 - sig))).astype(jnp.bfloat16)
    d_up = (back * act).astype(jnp.bfloat16)
    grad_gate = contract_rows(d_gate, rows_x)
    grad_up = contract_rows(d_up, rows_x)
    grad_down = contract_rows(hidden, rows_q)
    return expert_out, jnp.stack([grad_gate, grad_up, grad_down], axis=1)


def reduce_grads(grads, width):
    share = grads.shape[0] // lax.axis_size("dp")
    summed = lax.psum_scatter(grads, "dp", scatter_dimension=0, tiled=True)
    return summed.reshape(1, share, 3, width)


def source_slots(routes, experts):
    flat = routes.reshape(-1)
    onehot = (flat[:, None] == jnp.arange(experts, dtype=jnp.int32)[None, :]).astype(jnp.int32)
    before = jnp.cumsum(onehot, axis=0) - onehot
    return flat, jnp.sum(before * onehot, axis=1)


def local_a2a(tokens, masked, importance, routes, gates, cotangent, w_gate, w_up, w_down):
    tok_rows = tokens.shape[0]
    width = tokens.shape[1]
    topk = routes.shape[1]
    experts = lax.axis_size("expert")
    capacity = min(tok_rows, 3 * tok_rows * topk // (2 * experts))
    flat, slots = source_slots(routes, experts)
    target = flat * capacity + slots
    owner = jnp.arange(tok_rows * topk, dtype=jnp.int32) // topk
    coef = importance * masked.astype(jnp.float32)
    factor = (coef[:, None] * gates).reshape(-1)
    sent_x = jnp.zeros((experts * capacity, width), jnp.bfloat16).at[target].set(tokens[owner])
    scaled = (factor[:, None] * cotangent[owner].astype(jnp.float32)).astype(jnp.bfloat16)
    sent_q = jnp.zeros((experts * capacity, width), jnp.bfloat16).at[target].set(scaled)
    layout = (experts, capacity, width)
    recv_x = lax.all_to_all(sent_x.reshape(layout), "expert", 0, 0, tiled=True)
    recv_q = lax.all_to_all(sent_q.reshape(layout), "expert", 0, 0, tiled=True)
    expert_out, grads = expert_math(
        recv_x.reshape(-1, width), recv_q.reshape(-1, width), w_gate[0], w_up[0], w_down[0]
    )
    returned = lax.all_to_all(expert_out.reshape(layout), "expert", 0, 0, tiled=True)
    picked = returned.reshape(-1, width)[target].astype(jnp.float32)
    summed = jnp.sum(picked.reshape(tok_rows, topk, width) * gates[:, :, None], axis=1)
    return summed.astype(jnp.bfloat16), reduce_grads(grads, width)


def exact_pieces(values):
    high = lax.reduce_precision(values, exponent_bits=8, mantissa_bits=7)
    rest = values - high
    middle = lax.reduce_precision(rest, exponent_bits=8, mantissa_bits=7)
    low = rest - middle
    return [part.astype(jnp.bfloat16) for part in (high, middle, low)]


def joined(pieces):
    total = pieces[0].astype(jnp.float32) + pieces[1].astype(jnp.float32)
    return total + pieces[2].astype(jnp.float32)


def gather_replica(values):
    mine = lax.all_gather(values, "ez", axis=0, tiled=True)
    return [mine, lax.ppermute(mine, "core", [(0, 1), (1, 0)])]


def ring_gather(block):
    n = lax.axis_size("ez")
    order = [2 * i for i in range(n // 2)] + [2 * i + 1 for i in reversed(range(n // 2))]
    if n % 2:
        order = list(range(n))
    place = [0] * n
    for p, c in enumerate(order):
        place[c] = p
    me = lax.axis_index("ez")
    at = jnp.asarray(place, jnp.int32)[me]
    ring = jnp.asarray(order, jnp.int32)
    out = jnp.zeros((n,) + block.shape, block.dtype)
    out = lax.dynamic_update_index_in_dim(out, block, me, 0)
    ahead = [(order[i], order[(i + 1) % n]) for i in range(n)]
    behind = [(order[i], order[(i - 1) % n]) for i in range(n)]
    up, down = block, block
    for step in range(1, n // 2 + 1):
        up = lax.ppermute(up, "ez", ahead)
        out = lax.dynamic_update_index_in_dim(out, up, ring[(at - step) % n], 0)
        if step <= (n - 1) // 2:
            down = lax.ppermute(down, "ez", behind)
            out = lax.dynamic_update_index_in_dim(out, down, ring[(at + step) % n], 0)
    mine = out.reshape((n * block.shape[0],) + block.shape[1:])
    return [mine, lax.ppermute(mine, "core", [(0, 1), (1, 0)])]


def slots_by_rank(routes, experts):
    tok_rows = routes.shape[0]
    onehot = routes[:, :, None] == lax.broadcasted_iota(jnp.int32, (1, 1, experts), 2)
    hits = jnp.any(onehot, axis=1).astype(jnp.bfloat16)
    before = (
        lax.broadcasted_iota(jnp.int32, (tok_rows, tok_rows), 0)
        > lax.broadcasted_iota(jnp.int32, (tok_rows, tok_rows), 1)
    ).astype(jnp.bfloat16)
    rank = jnp.dot(before, hits, preferred_element_type=jnp.float32).astype(jnp.int32)
    return jnp.sum(jnp.where(onehot, rank[:, None, :], 0), axis=2)


def reduce_grads_dp(grad_half, width):
    ndp = lax.axis_size("dp")
    if ndp != 2:
        grads = jnp.concatenate([grad_half(h) for h in range(ndp)], axis=0)
        return reduce_grads(grads, width)
    d = lax.axis_index("dp")
    theirs = grad_half(1 - d)
    sent = [
        lax.ppermute(theirs[:, :2].astype(jnp.bfloat16), "dp", [(0, 1), (1, 0)]),
        lax.ppermute(theirs[:, 2:].astype(jnp.bfloat16), "dp", [(0, 1), (1, 0)]),
    ]
    summed = grad_half(d) + jnp.concatenate(sent, axis=1).astype(jnp.float32)
    return summed.reshape(1, summed.shape[0], 3, width)


def local_gather(tokens, masked, importance, routes, gates, cotangent, w_gate, w_up, w_down):
    tok_rows = tokens.shape[0]
    width = tokens.shape[1]
    topk = routes.shape[1]
    ncore = lax.axis_size("core")
    nchip = lax.axis_size("ez")
    experts = nchip * ncore
    capacity = min(tok_rows, 3 * tok_rows * topk // (2 * experts))
    core = lax.axis_index("core")
    me = lax.axis_index("ez") * ncore + core
    coef = importance * masked.astype(jnp.float32)
    factor = coef[:, None] * gates
    meta = [routes.astype(jnp.bfloat16)] + exact_pieces(factor) + exact_pieces(gates)
    meta_rows = jnp.concatenate([m.T for m in meta], axis=0)
    lines = -(-meta_rows.size // width)
    lines += (-(tok_rows + lines)) % 8
    flat_meta = jnp.pad(meta_rows.reshape(-1), (0, lines * width - meta_rows.size))
    packed = jnp.concatenate([tokens, flat_meta.reshape(lines, width)], axis=0)

    gathered = lax.all_gather(packed, ("ez", "core"), axis=0, tiled=True)
    gathered = gathered.reshape(experts, tok_rows + lines, width)
    cot_halves = ring_gather(cotangent)
    on_core0 = core == 0
    meta_all = gathered[:, tok_rows:].reshape(experts, lines * width)
    meta_all = meta_all[:, :meta_rows.size].reshape(experts, len(meta), topk, tok_rows)
    routes_t = meta_all[:, 0].astype(jnp.int32)
    hit = routes_t == me
    zero = jnp.zeros((), jnp.float32)
    fac = jnp.sum(jnp.where(hit, joined([meta_all[:, i] for i in (1, 2, 3)]), zero), axis=1)
    gate_t = joined([meta_all[:, i] for i in (4, 5, 6)])
    routed = jnp.any(hit, axis=1)
    ahead = (
        lax.broadcasted_iota(jnp.int32, (tok_rows, tok_rows), 0)
        < lax.broadcasted_iota(jnp.int32, (tok_rows, tok_rows), 1)
    ).astype(jnp.bfloat16)
    rank = jnp.dot(
        routed.astype(jnp.bfloat16), ahead, preferred_element_type=jnp.float32
    ).astype(jnp.int32)
    slot_ids = lax.broadcasted_iota(jnp.int32, (experts, capacity, tok_rows), 1)
    pick = (routed[:, None, :] & (rank[:, None, :] == slot_ids)).astype(jnp.bfloat16)

    rows_x = jnp.einsum(
        "sjt,std->sjd",
        pick,
        gathered[:, :tok_rows],
        preferred_element_type=jnp.float32,
    ).astype(jnp.bfloat16).reshape(experts * capacity, width)
    wgate, wup, wdown = w_gate[0], w_up[0], w_down[0]
    gate_pre = contract_cols(rows_x, wgate)
    up_pre = contract_cols(rows_x, wup)
    sig = jax.nn.sigmoid(gate_pre)
    act = gate_pre * sig
    hidden = (act * up_pre).astype(jnp.bfloat16)
    expert_out = jnp.dot(hidden, wdown, preferred_element_type=jnp.float32).astype(
        jnp.bfloat16
    )

    pick_k = pick.reshape(nchip, ncore, capacity, tok_rows)
    out_k = expert_out.reshape(nchip, ncore, capacity, width)
    def dense_for(k):
        return jnp.einsum(
            "sjt,sjd->std",
            lax.dynamic_index_in_dim(pick_k, k, 1, keepdims=False),
            lax.dynamic_index_in_dim(out_k, k, 1, keepdims=False),
            preferred_element_type=jnp.float32,
        ).astype(jnp.bfloat16)

    from_partner = lax.ppermute(dense_for(1 - core), "core", [(0, 1), (1, 0)])
    mine = dense_for(core)
    gate_all = gate_t.reshape(nchip, ncore, topk, tok_rows)
    routes_all = routes_t.reshape(nchip, ncore, topk, tok_rows)
    gate_own = jnp.where(on_core0, gate_all[:, 0], gate_all[:, 1])
    routes_own = jnp.where(on_core0, routes_all[:, 0], routes_all[:, 1])
    gte = jnp.sum(jnp.where(routes_own == me, gate_own, zero), axis=1)
    gte_partner = jnp.sum(jnp.where(routes_own == (me ^ 1), gate_own, zero), axis=1)
    combined = (
        gte[:, :, None] * mine.astype(jnp.float32)
        + gte_partner[:, :, None] * from_partner.astype(jnp.float32)
    ).astype(jnp.bfloat16)
    returned = lax.all_to_all(combined, "ez", 0, 0, tiled=True)

    cot_halves, _ = lax.optimization_barrier((cot_halves, expert_out))
    pick_by_core = pick.reshape(nchip, ncore, capacity, tok_rows)
    fac_by_core = fac.reshape(nchip, ncore, tok_rows)
    core_ids = lax.broadcasted_iota(jnp.int32, (1, ncore, 1, 1), 1)
    rows_q = 0.0
    for h, half in enumerate(cot_halves):
        k = h ^ core
        scaled = lax.dynamic_index_in_dim(fac_by_core, k, 1, keepdims=False)[:, :, None] * half.reshape(
            nchip, tok_rows, width
        ).astype(jnp.float32)
        masked_pick = jnp.where(core_ids == k, pick_by_core, jnp.zeros((), pick_by_core.dtype))
        rows_q = rows_q + jnp.einsum(
            "ikjt,itd->ikjd",
            masked_pick,
            scaled.astype(jnp.bfloat16),
            preferred_element_type=jnp.float32,
        )
    rows_q = rows_q.astype(jnp.bfloat16).reshape(experts * capacity, width)
    back = contract_cols(rows_q, wdown)
    d_gate = (back * up_pre * sig * (1.0 + gate_pre * (1.0 - sig))).astype(jnp.bfloat16)
    d_up = (back * act).astype(jnp.bfloat16)
    share = d_gate.shape[1] // lax.axis_size("dp")

    def grad_half(h):
        def part(v):
            return lax.dynamic_slice_in_dim(v, h * share, share, axis=1)

        return jnp.stack(
            [
                contract_rows(part(d_gate), rows_x),
                contract_rows(part(d_up), rows_x),
                contract_rows(part(hidden), rows_q),
            ],
            axis=1,
        )

    weight_grads = reduce_grads_dp(grad_half, width)

    summed = jnp.sum(returned.astype(jnp.float32), axis=0)
    return summed.astype(jnp.bfloat16), weight_grads


def specs(rows, experts):
    return (
        (P(rows, None), P(rows), P(rows), P(rows, None), P(rows, None), P(rows, None))
        + (P(experts, None, None),) * 3,
        (P(rows, None), P(experts, "dp", None, None)),
    )


def solution(mesh):
    ndp, nexp = mesh.shape["dp"], mesh.shape["expert"]
    split = jax.sharding.Mesh(mesh.devices.reshape(ndp, nexp // 2, 2), ("dp", "ez", "core"))
    ins, outs = specs(("dp", "ez", "core"), ("ez", "core"))
    gathered = jax.shard_map(local_gather, mesh=split, in_specs=ins, out_specs=outs, check_vma=False)
    ins, outs = specs(("dp", "expert"), "expert")
    routed = jax.shard_map(local_a2a, mesh=mesh, in_specs=ins, out_specs=outs, check_vma=False)

    def run(*args):
        if args[0].shape[0] // ndp <= GATHER_ROWS:
            return gathered(*args)
        return routed(*args)

    return run
```

```python
import jax
import jax.numpy as jnp
from jax import lax
from jax.sharding import PartitionSpec as P

GATHER_ROWS = 2048


def contract_rows(left, right):
    return lax.dot_general(
        left, right, (((0,), (0,)), ((), ())), preferred_element_type=jnp.float32
    )


def contract_cols(left, right):
    return lax.dot_general(
        left, right, (((1,), (1,)), ((), ())), preferred_element_type=jnp.float32
    )


def expert_math(rows_x, rows_q, wgate, wup, wdown):
    gate_pre = contract_cols(rows_x, wgate)
    up_pre = contract_cols(rows_x, wup)
    sig = jax.nn.sigmoid(gate_pre)
    act = gate_pre * sig
    hidden = (act * up_pre).astype(jnp.bfloat16)
    expert_out = jnp.dot(hidden, wdown, preferred_element_type=jnp.float32).astype(
        jnp.bfloat16
    )
    back = contract_cols(rows_q, wdown)
    d_gate = (back * up_pre * sig * (1.0 + gate_pre * (1.0 - sig))).astype(jnp.bfloat16)
    d_up = (back * act).astype(jnp.bfloat16)
    grad_gate = contract_rows(d_gate, rows_x)
    grad_up = contract_rows(d_up, rows_x)
    grad_down = contract_rows(hidden, rows_q)
    return expert_out, jnp.stack([grad_gate, grad_up, grad_down], axis=1)


def reduce_grads(grads, width):
    share = grads.shape[0] // lax.axis_size("dp")
    summed = lax.psum_scatter(grads, "dp", scatter_dimension=0, tiled=True)
    return summed.reshape(1, share, 3, width)


def source_slots(routes, experts):
    flat = routes.reshape(-1)
    onehot = (flat[:, None] == jnp.arange(experts, dtype=jnp.int32)[None, :]).astype(jnp.int32)
    before = jnp.cumsum(onehot, axis=0) - onehot
    return flat, jnp.sum(before * onehot, axis=1)


def local_a2a(tokens, masked, importance, routes, gates, cotangent, w_gate, w_up, w_down):
    tok_rows = tokens.shape[0]
    width = tokens.shape[1]
    topk = routes.shape[1]
    experts = lax.axis_size("expert")
    capacity = min(tok_rows, 3 * tok_rows * topk // (2 * experts))
    flat, slots = source_slots(routes, experts)
    target = flat * capacity + slots
    owner = jnp.arange(tok_rows * topk, dtype=jnp.int32) // topk
    coef = importance * masked.astype(jnp.float32)
    factor = (coef[:, None] * gates).reshape(-1)
    sent_x = jnp.zeros((experts * capacity, width), jnp.bfloat16).at[target].set(tokens[owner])
    scaled = (factor[:, None] * cotangent[owner].astype(jnp.float32)).astype(jnp.bfloat16)
    sent_q = jnp.zeros((experts * capacity, width), jnp.bfloat16).at[target].set(scaled)
    layout = (experts, capacity, width)
    recv_x = lax.all_to_all(sent_x.reshape(layout), "expert", 0, 0, tiled=True)
    recv_q = lax.all_to_all(sent_q.reshape(layout), "expert", 0, 0, tiled=True)
    expert_out, grads = expert_math(
        recv_x.reshape(-1, width), recv_q.reshape(-1, width), w_gate[0], w_up[0], w_down[0]
    )
    returned = lax.all_to_all(expert_out.reshape(layout), "expert", 0, 0, tiled=True)
    picked = returned.reshape(-1, width)[target].astype(jnp.float32)
    summed = jnp.sum(picked.reshape(tok_rows, topk, width) * gates[:, :, None], axis=1)
    return summed.astype(jnp.bfloat16), reduce_grads(grads, width)


def exact_pieces(values):
    high = lax.reduce_precision(values, exponent_bits=8, mantissa_bits=7)
    rest = values - high
    middle = lax.reduce_precision(rest, exponent_bits=8, mantissa_bits=7)
    low = rest - middle
    return [part.astype(jnp.bfloat16) for part in (high, middle, low)]


def joined(pieces):
    total = pieces[0].astype(jnp.float32) + pieces[1].astype(jnp.float32)
    return total + pieces[2].astype(jnp.float32)


def gather_replica(values):
    mine = lax.all_gather(values, "ez", axis=0, tiled=True)
    return [mine, lax.ppermute(mine, "core", [(0, 1), (1, 0)])]


def ring_gather(block):
    n = lax.axis_size("ez")
    order = [2 * i for i in range(n // 2)] + [2 * i + 1 for i in reversed(range(n // 2))]
    if n % 2:
        order = list(range(n))
    place = [0] * n
    for p, c in enumerate(order):
        place[c] = p
    me = lax.axis_index("ez")
    at = jnp.asarray(place, jnp.int32)[me]
    ring = jnp.asarray(order, jnp.int32)
    out = jnp.zeros((n,) + block.shape, block.dtype)
    out = lax.dynamic_update_index_in_dim(out, block, me, 0)
    ahead = [(order[i], order[(i + 1) % n]) for i in range(n)]
    behind = [(order[i], order[(i - 1) % n]) for i in range(n)]
    up, down = block, block
    for step in range(1, n // 2 + 1):
        up = lax.ppermute(up, "ez", ahead)
        out = lax.dynamic_update_index_in_dim(out, up, ring[(at - step) % n], 0)
        if step <= (n - 1) // 2:
            down = lax.ppermute(down, "ez", behind)
            out = lax.dynamic_update_index_in_dim(out, down, ring[(at + step) % n], 0)
    mine = out.reshape((n * block.shape[0],) + block.shape[1:])
    return [mine, lax.ppermute(mine, "core", [(0, 1), (1, 0)])]


def slots_by_rank(routes, experts):
    tok_rows = routes.shape[0]
    onehot = routes[:, :, None] == lax.broadcasted_iota(jnp.int32, (1, 1, experts), 2)
    hits = jnp.any(onehot, axis=1).astype(jnp.bfloat16)
    before = (
        lax.broadcasted_iota(jnp.int32, (tok_rows, tok_rows), 0)
        > lax.broadcasted_iota(jnp.int32, (tok_rows, tok_rows), 1)
    ).astype(jnp.bfloat16)
    rank = jnp.dot(before, hits, preferred_element_type=jnp.float32).astype(jnp.int32)
    return jnp.sum(jnp.where(onehot, rank[:, None, :], 0), axis=2)


def reduce_grads_dp(grad_half, width):
    ndp = lax.axis_size("dp")
    if ndp != 2:
        grads = jnp.concatenate([grad_half(h) for h in range(ndp)], axis=0)
        return reduce_grads(grads, width)
    d = lax.axis_index("dp")
    theirs = grad_half(1 - d)
    sent = [
        lax.ppermute(theirs[:, i:i + 1].astype(jnp.bfloat16), "dp", [(0, 1), (1, 0)])
        for i in range(theirs.shape[1])
    ]
    summed = grad_half(d) + jnp.concatenate(sent, axis=1).astype(jnp.float32)
    return summed.reshape(1, summed.shape[0], 3, width)


def local_gather(tokens, masked, importance, routes, gates, cotangent, w_gate, w_up, w_down):
    tok_rows = tokens.shape[0]
    width = tokens.shape[1]
    topk = routes.shape[1]
    ncore = lax.axis_size("core")
    nchip = lax.axis_size("ez")
    experts = nchip * ncore
    capacity = min(tok_rows, 3 * tok_rows * topk // (2 * experts))
    core = lax.axis_index("core")
    me = lax.axis_index("ez") * ncore + core
    coef = importance * masked.astype(jnp.float32)
    factor = coef[:, None] * gates
    meta = [routes.astype(jnp.bfloat16)] + exact_pieces(factor) + exact_pieces(gates)
    meta_rows = jnp.concatenate([m.T for m in meta], axis=0)
    lines = -(-meta_rows.size // width)
    lines += (-(tok_rows + lines)) % 8
    flat_meta = jnp.pad(meta_rows.reshape(-1), (0, lines * width - meta_rows.size))
    packed = jnp.concatenate([tokens, flat_meta.reshape(lines, width)], axis=0)

    gathered = lax.all_gather(packed, ("ez", "core"), axis=0, tiled=True)
    gathered = gathered.reshape(experts, tok_rows + lines, width)
    cot_halves = ring_gather(cotangent)
    on_core0 = core == 0
    meta_all = gathered[:, tok_rows:].reshape(experts, lines * width)
    meta_all = meta_all[:, :meta_rows.size].reshape(experts, len(meta), topk, tok_rows)
    routes_t = meta_all[:, 0].astype(jnp.int32)
    hit = routes_t == me
    zero = jnp.zeros((), jnp.float32)
    fac = jnp.sum(jnp.where(hit, joined([meta_all[:, i] for i in (1, 2, 3)]), zero), axis=1)
    gate_t = joined([meta_all[:, i] for i in (4, 5, 6)])
    routed = jnp.any(hit, axis=1)
    ahead = (
        lax.broadcasted_iota(jnp.int32, (tok_rows, tok_rows), 0)
        < lax.broadcasted_iota(jnp.int32, (tok_rows, tok_rows), 1)
    ).astype(jnp.bfloat16)
    rank = jnp.dot(
        routed.astype(jnp.bfloat16), ahead, preferred_element_type=jnp.float32
    ).astype(jnp.int32)
    slot_ids = lax.broadcasted_iota(jnp.int32, (experts, capacity, tok_rows), 1)
    pick = (routed[:, None, :] & (rank[:, None, :] == slot_ids)).astype(jnp.bfloat16)

    rows_x = jnp.einsum(
        "sjt,std->sjd",
        pick,
        gathered[:, :tok_rows],
        preferred_element_type=jnp.float32,
    ).astype(jnp.bfloat16).reshape(experts * capacity, width)
    wgate, wup, wdown = w_gate[0], w_up[0], w_down[0]
    gate_pre = contract_cols(rows_x, wgate)
    up_pre = contract_cols(rows_x, wup)
    sig = jax.nn.sigmoid(gate_pre)
    act = gate_pre * sig
    hidden = (act * up_pre).astype(jnp.bfloat16)
    expert_out = jnp.dot(hidden, wdown, preferred_element_type=jnp.float32).astype(
        jnp.bfloat16
    )

    pick_k = pick.reshape(nchip, ncore, capacity, tok_rows)
    out_k = expert_out.reshape(nchip, ncore, capacity, width)
    def dense_for(k):
        return jnp.einsum(
            "sjt,sjd->std",
            lax.dynamic_index_in_dim(pick_k, k, 1, keepdims=False),
            lax.dynamic_index_in_dim(out_k, k, 1, keepdims=False),
            preferred_element_type=jnp.float32,
        ).astype(jnp.bfloat16)

    from_partner = lax.ppermute(dense_for(1 - core), "core", [(0, 1), (1, 0)])
    mine = dense_for(core)
    gate_all = gate_t.reshape(nchip, ncore, topk, tok_rows)
    routes_all = routes_t.reshape(nchip, ncore, topk, tok_rows)
    gate_own = jnp.where(on_core0, gate_all[:, 0], gate_all[:, 1])
    routes_own = jnp.where(on_core0, routes_all[:, 0], routes_all[:, 1])
    gte = jnp.sum(jnp.where(routes_own == me, gate_own, zero), axis=1)
    gte_partner = jnp.sum(jnp.where(routes_own == (me ^ 1), gate_own, zero), axis=1)
    combined = (
        gte[:, :, None] * mine.astype(jnp.float32)
        + gte_partner[:, :, None] * from_partner.astype(jnp.float32)
    ).astype(jnp.bfloat16)
    returned = lax.all_to_all(combined, "ez", 0, 0, tiled=True)

    cot_halves, _ = lax.optimization_barrier((cot_halves, expert_out))
    pick_by_core = pick.reshape(nchip, ncore, capacity, tok_rows)
    fac_by_core = fac.reshape(nchip, ncore, tok_rows)
    core_ids = lax.broadcasted_iota(jnp.int32, (1, ncore, 1, 1), 1)
    rows_q = 0.0
    for h, half in enumerate(cot_halves):
        k = h ^ core
        scaled = lax.dynamic_index_in_dim(fac_by_core, k, 1, keepdims=False)[:, :, None] * half.reshape(
            nchip, tok_rows, width
        ).astype(jnp.float32)
        masked_pick = jnp.where(core_ids == k, pick_by_core, jnp.zeros((), pick_by_core.dtype))
        rows_q = rows_q + jnp.einsum(
            "ikjt,itd->ikjd",
            masked_pick,
            scaled.astype(jnp.bfloat16),
            preferred_element_type=jnp.float32,
        )
    rows_q = rows_q.astype(jnp.bfloat16).reshape(experts * capacity, width)
    back = contract_cols(rows_q, wdown)
    d_gate = (back * up_pre * sig * (1.0 + gate_pre * (1.0 - sig))).astype(jnp.bfloat16)
    d_up = (back * act).astype(jnp.bfloat16)
    share = d_gate.shape[1] // lax.axis_size("dp")

    def grad_half(h):
        def part(v):
            return lax.dynamic_slice_in_dim(v, h * share, share, axis=1)

        return jnp.stack(
            [
                contract_rows(part(d_gate), rows_x),
                contract_rows(part(d_up), rows_x),
                contract_rows(part(hidden), rows_q),
            ],
            axis=1,
        )

    weight_grads = reduce_grads_dp(grad_half, width)

    summed = jnp.sum(returned.astype(jnp.float32), axis=0)
    return summed.astype(jnp.bfloat16), weight_grads


def specs(rows, experts):
    return (
        (P(rows, None), P(rows), P(rows), P(rows, None), P(rows, None), P(rows, None))
        + (P(experts, None, None),) * 3,
        (P(rows, None), P(experts, "dp", None, None)),
    )


def solution(mesh):
    ndp, nexp = mesh.shape["dp"], mesh.shape["expert"]
    split = jax.sharding.Mesh(mesh.devices.reshape(ndp, nexp // 2, 2), ("dp", "ez", "core"))
    ins, outs = specs(("dp", "ez", "core"), ("ez", "core"))
    gathered = jax.shard_map(local_gather, mesh=split, in_specs=ins, out_specs=outs, check_vma=False)
    ins, outs = specs(("dp", "expert"), "expert")
    routed = jax.shard_map(local_a2a, mesh=mesh, in_specs=ins, out_specs=outs, check_vma=False)

    def run(*args):
        if args[0].shape[0] // ndp <= GATHER_ROWS:
            return gathered(*args)
        return routed(*args)

    return run
```

```python
import jax
import jax.numpy as jnp
from jax import lax
from jax.sharding import PartitionSpec as P

GATHER_ROWS = 2048


def contract_rows(left, right):
    return lax.dot_general(
        left, right, (((0,), (0,)), ((), ())), preferred_element_type=jnp.float32
    )


def contract_cols(left, right):
    return lax.dot_general(
        left, right, (((1,), (1,)), ((), ())), preferred_element_type=jnp.float32
    )


def expert_math(rows_x, rows_q, wgate, wup, wdown):
    gate_pre = contract_cols(rows_x, wgate)
    up_pre = contract_cols(rows_x, wup)
    sig = jax.nn.sigmoid(gate_pre)
    act = gate_pre * sig
    hidden = (act * up_pre).astype(jnp.bfloat16)
    expert_out = jnp.dot(hidden, wdown, preferred_element_type=jnp.float32).astype(
        jnp.bfloat16
    )
    back = contract_cols(rows_q, wdown)
    d_gate = (back * up_pre * sig * (1.0 + gate_pre * (1.0 - sig))).astype(jnp.bfloat16)
    d_up = (back * act).astype(jnp.bfloat16)
    grad_gate = contract_rows(d_gate, rows_x)
    grad_up = contract_rows(d_up, rows_x)
    grad_down = contract_rows(hidden, rows_q)
    return expert_out, jnp.stack([grad_gate, grad_up, grad_down], axis=1)


def reduce_grads(grads, width):
    share = grads.shape[0] // lax.axis_size("dp")
    summed = lax.psum_scatter(grads, "dp", scatter_dimension=0, tiled=True)
    return summed.reshape(1, share, 3, width)


def source_slots(routes, experts):
    flat = routes.reshape(-1)
    onehot = (flat[:, None] == jnp.arange(experts, dtype=jnp.int32)[None, :]).astype(jnp.int32)
    before = jnp.cumsum(onehot, axis=0) - onehot
    return flat, jnp.sum(before * onehot, axis=1)


def local_a2a(tokens, masked, importance, routes, gates, cotangent, w_gate, w_up, w_down):
    tok_rows = tokens.shape[0]
    width = tokens.shape[1]
    topk = routes.shape[1]
    experts = lax.axis_size("expert")
    capacity = min(tok_rows, 3 * tok_rows * topk // (2 * experts))
    flat, slots = source_slots(routes, experts)
    target = flat * capacity + slots
    owner = jnp.arange(tok_rows * topk, dtype=jnp.int32) // topk
    coef = importance * masked.astype(jnp.float32)
    factor = (coef[:, None] * gates).reshape(-1)
    sent_x = jnp.zeros((experts * capacity, width), jnp.bfloat16).at[target].set(tokens[owner])
    scaled = (factor[:, None] * cotangent[owner].astype(jnp.float32)).astype(jnp.bfloat16)
    sent_q = jnp.zeros((experts * capacity, width), jnp.bfloat16).at[target].set(scaled)
    layout = (experts, capacity, width)
    recv_x = lax.all_to_all(sent_x.reshape(layout), "expert", 0, 0, tiled=True)
    recv_q = lax.all_to_all(sent_q.reshape(layout), "expert", 0, 0, tiled=True)
    expert_out, grads = expert_math(
        recv_x.reshape(-1, width), recv_q.reshape(-1, width), w_gate[0], w_up[0], w_down[0]
    )
    returned = lax.all_to_all(expert_out.reshape(layout), "expert", 0, 0, tiled=True)
    picked = returned.reshape(-1, width)[target].astype(jnp.float32)
    summed = jnp.sum(picked.reshape(tok_rows, topk, width) * gates[:, :, None], axis=1)
    return summed.astype(jnp.bfloat16), reduce_grads(grads, width)


def exact_pieces(values):
    high = lax.reduce_precision(values, exponent_bits=8, mantissa_bits=7)
    rest = values - high
    middle = lax.reduce_precision(rest, exponent_bits=8, mantissa_bits=7)
    low = rest - middle
    return [part.astype(jnp.bfloat16) for part in (high, middle, low)]


def joined(pieces):
    total = pieces[0].astype(jnp.float32) + pieces[1].astype(jnp.float32)
    return total + pieces[2].astype(jnp.float32)


def gather_replica(values):
    mine = lax.all_gather(values, "ez", axis=0, tiled=True)
    return [mine, lax.ppermute(mine, "core", [(0, 1), (1, 0)])]


def ring_gather(block):
    n = lax.axis_size("ez")
    order = [2 * i for i in range(n // 2)] + [2 * i + 1 for i in reversed(range(n // 2))]
    if n % 2:
        order = list(range(n))
    place = [0] * n
    for p, c in enumerate(order):
        place[c] = p
    me = lax.axis_index("ez")
    at = jnp.asarray(place, jnp.int32)[me]
    ring = jnp.asarray(order, jnp.int32)
    out = jnp.zeros((n,) + block.shape, block.dtype)
    out = lax.dynamic_update_index_in_dim(out, block, me, 0)
    ahead = [(order[i], order[(i + 1) % n]) for i in range(n)]
    behind = [(order[i], order[(i - 1) % n]) for i in range(n)]
    up, down = block, block
    for step in range(1, n // 2 + 1):
        up = lax.ppermute(up, "ez", ahead)
        out = lax.dynamic_update_index_in_dim(out, up, ring[(at - step) % n], 0)
        if step <= (n - 1) // 2:
            down = lax.ppermute(down, "ez", behind)
            out = lax.dynamic_update_index_in_dim(out, down, ring[(at + step) % n], 0)
    mine = out.reshape((n * block.shape[0],) + block.shape[1:])
    return [mine, lax.ppermute(mine, "core", [(0, 1), (1, 0)])]


def slots_by_rank(routes, experts):
    tok_rows = routes.shape[0]
    onehot = routes[:, :, None] == lax.broadcasted_iota(jnp.int32, (1, 1, experts), 2)
    hits = jnp.any(onehot, axis=1).astype(jnp.bfloat16)
    before = (
        lax.broadcasted_iota(jnp.int32, (tok_rows, tok_rows), 0)
        > lax.broadcasted_iota(jnp.int32, (tok_rows, tok_rows), 1)
    ).astype(jnp.bfloat16)
    rank = jnp.dot(before, hits, preferred_element_type=jnp.float32).astype(jnp.int32)
    return jnp.sum(jnp.where(onehot, rank[:, None, :], 0), axis=2)


def reduce_grads_dp(grad_half, width):
    ndp = lax.axis_size("dp")
    if ndp != 2:
        grads = jnp.concatenate([grad_half(h) for h in range(ndp)], axis=0)
        return reduce_grads(grads, width)
    d = lax.axis_index("dp")
    sent = [
        lax.ppermute(g.astype(jnp.bfloat16), "dp", [(0, 1), (1, 0)])
        for g in grad_half(1 - d, False)
    ]
    summed = grad_half(d) + jnp.stack(sent, axis=1).astype(jnp.float32)
    return summed.reshape(1, summed.shape[0], 3, width)


def local_gather(tokens, masked, importance, routes, gates, cotangent, w_gate, w_up, w_down):
    tok_rows = tokens.shape[0]
    width = tokens.shape[1]
    topk = routes.shape[1]
    ncore = lax.axis_size("core")
    nchip = lax.axis_size("ez")
    experts = nchip * ncore
    capacity = min(tok_rows, 3 * tok_rows * topk // (2 * experts))
    core = lax.axis_index("core")
    me = lax.axis_index("ez") * ncore + core
    coef = importance * masked.astype(jnp.float32)
    factor = coef[:, None] * gates
    meta = [routes.astype(jnp.bfloat16)] + exact_pieces(factor) + exact_pieces(gates)
    meta_rows = jnp.concatenate([m.T for m in meta], axis=0)
    lines = -(-meta_rows.size // width)
    lines += (-(tok_rows + lines)) % 8
    flat_meta = jnp.pad(meta_rows.reshape(-1), (0, lines * width - meta_rows.size))
    packed = jnp.concatenate([tokens, flat_meta.reshape(lines, width)], axis=0)

    gathered = lax.all_gather(packed, ("ez", "core"), axis=0, tiled=True)
    gathered = gathered.reshape(experts, tok_rows + lines, width)
    cot_halves = ring_gather(cotangent)
    on_core0 = core == 0
    meta_all = gathered[:, tok_rows:].reshape(experts, lines * width)
    meta_all = meta_all[:, :meta_rows.size].reshape(experts, len(meta), topk, tok_rows)
    routes_t = meta_all[:, 0].astype(jnp.int32)
    hit = routes_t == me
    zero = jnp.zeros((), jnp.float32)
    fac = jnp.sum(jnp.where(hit, joined([meta_all[:, i] for i in (1, 2, 3)]), zero), axis=1)
    gate_t = joined([meta_all[:, i] for i in (4, 5, 6)])
    routed = jnp.any(hit, axis=1)
    ahead = (
        lax.broadcasted_iota(jnp.int32, (tok_rows, tok_rows), 0)
        < lax.broadcasted_iota(jnp.int32, (tok_rows, tok_rows), 1)
    ).astype(jnp.bfloat16)
    rank = jnp.dot(
        routed.astype(jnp.bfloat16), ahead, preferred_element_type=jnp.float32
    ).astype(jnp.int32)
    slot_ids = lax.broadcasted_iota(jnp.int32, (experts, capacity, tok_rows), 1)
    pick = (routed[:, None, :] & (rank[:, None, :] == slot_ids)).astype(jnp.bfloat16)

    rows_x = jnp.einsum(
        "sjt,std->sjd",
        pick,
        gathered[:, :tok_rows],
        preferred_element_type=jnp.float32,
    ).astype(jnp.bfloat16).reshape(experts * capacity, width)
    wgate, wup, wdown = w_gate[0], w_up[0], w_down[0]
    gate_pre = contract_cols(rows_x, wgate)
    up_pre = contract_cols(rows_x, wup)
    sig = jax.nn.sigmoid(gate_pre)
    act = gate_pre * sig
    hidden = (act * up_pre).astype(jnp.bfloat16)
    expert_out = jnp.dot(hidden, wdown, preferred_element_type=jnp.float32).astype(
        jnp.bfloat16
    )

    pick_k = pick.reshape(nchip, ncore, capacity, tok_rows)
    out_k = expert_out.reshape(nchip, ncore, capacity, width)
    def dense_for(k):
        return jnp.einsum(
            "sjt,sjd->std",
            lax.dynamic_index_in_dim(pick_k, k, 1, keepdims=False),
            lax.dynamic_index_in_dim(out_k, k, 1, keepdims=False),
            preferred_element_type=jnp.float32,
        ).astype(jnp.bfloat16)

    from_partner = lax.ppermute(dense_for(1 - core), "core", [(0, 1), (1, 0)])
    mine = dense_for(core)
    gate_all = gate_t.reshape(nchip, ncore, topk, tok_rows)
    routes_all = routes_t.reshape(nchip, ncore, topk, tok_rows)
    gate_own = jnp.where(on_core0, gate_all[:, 0], gate_all[:, 1])
    routes_own = jnp.where(on_core0, routes_all[:, 0], routes_all[:, 1])
    gte = jnp.sum(jnp.where(routes_own == me, gate_own, zero), axis=1)
    gte_partner = jnp.sum(jnp.where(routes_own == (me ^ 1), gate_own, zero), axis=1)
    combined = (
        gte[:, :, None] * mine.astype(jnp.float32)
        + gte_partner[:, :, None] * from_partner.astype(jnp.float32)
    ).astype(jnp.bfloat16)
    returned = lax.all_to_all(combined, "ez", 0, 0, tiled=True)

    cot_halves, _ = lax.optimization_barrier((cot_halves, expert_out))
    pick_by_core = pick.reshape(nchip, ncore, capacity, tok_rows)
    fac_by_core = fac.reshape(nchip, ncore, tok_rows)
    core_ids = lax.broadcasted_iota(jnp.int32, (1, ncore, 1, 1), 1)
    rows_q = 0.0
    for h, half in enumerate(cot_halves):
        k = h ^ core
        scaled = lax.dynamic_index_in_dim(fac_by_core, k, 1, keepdims=False)[:, :, None] * half.reshape(
            nchip, tok_rows, width
        ).astype(jnp.float32)
        masked_pick = jnp.where(core_ids == k, pick_by_core, jnp.zeros((), pick_by_core.dtype))
        rows_q = rows_q + jnp.einsum(
            "ikjt,itd->ikjd",
            masked_pick,
            scaled.astype(jnp.bfloat16),
            preferred_element_type=jnp.float32,
        )
    rows_q = rows_q.astype(jnp.bfloat16).reshape(experts * capacity, width)
    back = contract_cols(rows_q, wdown)
    d_gate = (back * up_pre * sig * (1.0 + gate_pre * (1.0 - sig))).astype(jnp.bfloat16)
    d_up = (back * act).astype(jnp.bfloat16)
    share = d_gate.shape[1] // lax.axis_size("dp")

    def grad_half(h, stacked=True):
        def part(v):
            return lax.dynamic_slice_in_dim(v, h * share, share, axis=1)

        kinds = [
            contract_rows(part(d_gate), rows_x),
            contract_rows(part(d_up), rows_x),
            contract_rows(part(hidden), rows_q),
        ]
        return jnp.stack(kinds, axis=1) if stacked else kinds

    weight_grads = reduce_grads_dp(grad_half, width)

    summed = jnp.sum(returned.astype(jnp.float32), axis=0)
    return summed.astype(jnp.bfloat16), weight_grads


def specs(rows, experts):
    return (
        (P(rows, None), P(rows), P(rows), P(rows, None), P(rows, None), P(rows, None))
        + (P(experts, None, None),) * 3,
        (P(rows, None), P(experts, "dp", None, None)),
    )


def solution(mesh):
    ndp, nexp = mesh.shape["dp"], mesh.shape["expert"]
    split = jax.sharding.Mesh(mesh.devices.reshape(ndp, nexp // 2, 2), ("dp", "ez", "core"))
    ins, outs = specs(("dp", "ez", "core"), ("ez", "core"))
    gathered = jax.shard_map(local_gather, mesh=split, in_specs=ins, out_specs=outs, check_vma=False)
    ins, outs = specs(("dp", "expert"), "expert")
    routed = jax.shard_map(local_a2a, mesh=mesh, in_specs=ins, out_specs=outs, check_vma=False)

    def run(*args):
        if args[0].shape[0] // ndp <= GATHER_ROWS:
            return gathered(*args)
        return routed(*args)

    return run
```
